32 devices in a mesh: azim: 4 (over y, x), rad: 4 (over z), hgt: 2 (over core).
Axes of the slice: x: 2, y: 2, z: 4, core: 2. Of those that a mesh axis runs over, the one named last changes fastest.
Arguments:
- density: float32 [8, 64, 1024], P('hgt', 'azim', 'rad'), may hold values from 0.2 to 0.8
- labels: int32 [8, 64, 1024], P('hgt', 'azim', 'rad'), may hold values from 0 to 4
- observed: float32 [8, 64, 1024], P('hgt', 'azim', 'rad'), may hold values from 0 to 1
- measured: int32 [8, 64, 1024], P('hgt', 'azim', 'rad'), may hold values 0 or 1
Outputs:
- final_density: float32 [8, 64, 1024], P('hgt', 'azim', 'rad')
- density_gradient: float32 [8, 64, 1024], P('hgt', 'azim', 'rad')
- grain_gradient: float32 [4, 8, 64, 1024], P(None, 'hgt', 'azim', 'rad')
The draws below stay inside these ranges and needn't reach their ends.
All inputs are finite; a program needn't handle non-finite values. No bound on the sum of `measured` on one device may be relied on, other than what follows from the above.
Results may differ from the reference program's by a relative error of at most 0.0001.
Values sent between devices are 32-bit elements; how exact they have to be, the bound alone decides.
No kernel may reach another device: no remote copies, remote signals or barrier semaphores. Data moves between devices by JAX's collectives and lax.ppermute only.
A program may use at most 64 MiB of HBM per device.

```python
import jax
import jax.numpy as jnp
from jax import lax

STEPS = 3
GRAINS = 4
NA = 64
NR = 1024
NH = 8


def place_ends(drawn, own_key, smallest, high):
    index_at = [jax.random.randint(jax.random.fold_in(own_key, axis), (), 0, length) for axis, length in enumerate(drawn.shape)]
    longest = drawn.shape.index(max(drawn.shape))
    next_to = index_at[:longest] + [(index_at[longest] + 1) % drawn.shape[longest]] + index_at[longest + 1:]
    return drawn.at[tuple(index_at)].set(smallest).at[tuple(next_to)].set(high)


def level_of(rng, extent, shards, smallest, high):
    loudness, own = 1.0, jax.random.fold_in(rng, 6)
    for axis_at, blocks in shards:
        heights = jnp.exp(jax.random.uniform(jax.random.fold_in(own, axis_at), (blocks,), jnp.float32, smallest / len(shards), high / len(shards)))
        loudness = loudness * jnp.repeat(heights, extent[axis_at] // blocks).reshape([-1 if axis == axis_at else 1 for axis in range(len(extent))])
    return loudness


def setup_inputs(seed: int = 0) -> dict:
    keys = jax.random.split(jax.random.key(seed), 5)
    density = jnp.clip(0.2 + 0.6 * jax.random.uniform(keys[0], (NH, NA, NR), jnp.float32) ** level_of(keys[0], (NH, NA, NR), ((0, 2), (1, 4), (2, 4)), -0.2, 0.2), 0.2, 0.8)
    labels = place_ends(jax.random.randint(keys[1], (NH, NA, NR), 0, GRAINS + 1), jax.random.fold_in(keys[1], 1), 0, GRAINS).astype(jnp.int32)
    observed = jnp.clip(1.0 * jax.random.uniform(keys[2], (NH, NA, NR), jnp.float32) ** level_of(keys[2], (NH, NA, NR), ((0, 2), (1, 4), (2, 4)), -0.2, 0.2), 0.0, 1.0)
    measured = place_ends((jax.random.randint(keys[3], (NH, NA, NR), 0, 4) < 3).astype(jnp.int32), jax.random.fold_in(keys[3], 1), 0, 1)
    return {"density": density, "labels": labels, "observed": observed, "measured": measured}


bulk_weight = 16.0
grain_weight = 1.0
cahn_step = 0.005
allen_step = 0.05
cahn_gradient = 1.0
allen_gradient = 1.0
full_turn = 6.283185307179586

def stencil(padded, margin, hgt_start, rad_start, total_hgt, total_azim, total_rad):
    height_rows = padded.shape[-3] - 2
    radius_rows = padded.shape[-1] - 2
    rad_index_all = rad_start - margin - 1 + jnp.arange(radius_rows + 2, dtype=jnp.int32)
    radius_all = total_azim / full_turn + rad_index_all.astype(jnp.float32) + 0.5
    rad_index = rad_index_all[1:-1]
    radius = radius_all[1:-1]
    outer_face = (radius + 0.5) * (rad_index < total_rad - 1).astype(jnp.float32)
    inner_face = (radius - 0.5) * (rad_index > 0).astype(jnp.float32)
    hgt_index = hgt_start - margin + jnp.arange(height_rows, dtype=jnp.int32)
    upper_face = (hgt_index < total_hgt - 1).astype(jnp.float32)[:, None, None]
    lower_face = (hgt_index > 0).astype(jnp.float32)[:, None, None]
    center = padded[..., 1:-1, 1:-1, 1:-1]
    outward = padded[..., 1:-1, 1:-1, 2:]
    inward = padded[..., 1:-1, 1:-1, :-2]
    radial = (outer_face * (outward - center) - inner_face * (center - inward)) / radius
    arc_length = radius * (full_turn / total_azim)
    azimuthal = (padded[..., 1:-1, 2:, 1:-1] + padded[..., 1:-1, :-2, 1:-1] - 2.0 * center) / (arc_length * arc_length)
    vertical = upper_face * (padded[..., 2:, 1:-1, 1:-1] - center) + lower_face * (padded[..., :-2, 1:-1, 1:-1] - center)
    return radial + azimuthal + vertical

def laplace_whole(field):
    leading = field.ndim - 3
    padded = jnp.pad(field, [(0, 0)] * leading + [(1, 1), (0, 0), (1, 1)])
    padded = jnp.concatenate([padded[..., :, -1:, :], padded, padded[..., :, :1, :]], axis=-2)
    return stencil(padded, 0, 0, 0, NH, NA, NR)

def chemical(density, grains):
    square_sum = lax.optimization_barrier(jnp.sum(grains * grains, axis=0))
    cube_sum = lax.optimization_barrier(jnp.sum(grains * grains * grains, axis=0))
    bulk_drive = 2.0 * bulk_weight * density * (1.0 - density) * (1.0 - 2.0 * density) + grain_weight * (2.0 * density - 6.0 * square_sum + 4.0 * cube_sum)
    grain_drive = 12.0 * grain_weight * (grains * (1.0 - density) - grains * grains * (2.0 - density) + grains * square_sum)
    return (bulk_drive, grain_drive)

def advance(density, grains):
    for moment in range(STEPS):
        bulk_drive, grain_drive = chemical(density, grains)
        potential = bulk_drive - cahn_gradient * laplace_whole(density)
        new_grains = grains - allen_step * (grain_drive - allen_gradient * laplace_whole(grains))
        density = density + cahn_step * laplace_whole(potential)
        grains = new_grains
    return density

def reference(density, labels, observed, measured):
    grains = (labels[None] == jnp.arange(GRAINS, dtype=jnp.int32)[:, None, None, None]).astype(jnp.float32)
    last_density, pullback = jax.vjp(advance, density, grains)
    misfit_start = measured.astype(jnp.float32) * (last_density - observed)
    density_gradient, grain_gradient = pullback(misfit_start)
    return (last_density, density_gradient, grain_gradient)
```

```python
import jax
import jax.numpy as jnp
from jax import lax
from jax.sharding import PartitionSpec as P

STEPS = 3
GRAINS = 4


bulk_weight = 16.0
grain_weight = 1.0
cahn_step = 0.005
allen_step = 0.05
cahn_gradient = 1.0
allen_gradient = 1.0
full_turn = 6.283185307179586

HALO = 4 * STEPS


def halo_exchange(block, axis, dim, width, cyclic):
    peers, length = (lax.axis_size(axis), block.shape[dim])
    up = [(i, (i + 1) % peers) for i in range(peers) if cyclic or i + 1 < peers]
    down = [(j, i) for i, j in up]
    last = lax.slice_in_dim(block, length - width, length, axis=dim)
    leading = lax.slice_in_dim(block, 0, width, axis=dim)
    before = lax.ppermute(last, axis, up)
    after = lax.ppermute(leading, axis, down)
    return jnp.concatenate([before, block, after], axis=dim)


def gather_axis(block, axis, dim):
    peers = lax.axis_size(axis)
    if peers == 1:
        return block
    own = lax.axis_index(axis)
    parts = [block]
    for shift in range(1, peers):
        parts.append(lax.ppermute(block, axis, [(i, (i + shift) % peers) for i in range(peers)]))
    stacked = jnp.stack(parts)
    order = (own - jnp.arange(peers, dtype=jnp.int32)) % peers
    ordered = jnp.take(stacked, order, axis=0)
    ordered = jnp.moveaxis(ordered, 0, dim)
    shape = list(block.shape)
    shape[dim] = shape[dim] * peers
    return ordered.reshape(shape)


def crop(x, width, new_width):
    cut = width - new_width
    if cut == 0:
        return x
    return x[..., cut : x.shape[-2] - cut, cut : x.shape[-1] - cut]


def radial_mask(width, geometry):
    rad_start, total_hgt, total_azim, total_rad, cols = geometry
    rad_index = rad_start - width + jnp.arange(cols + 2 * width, dtype=jnp.int32)
    return (rad_index >= 0) & (rad_index < total_rad)


def in_domain(x, width, geometry):
    return jnp.where(radial_mask(width, geometry), x, 0.0)


def laplace(x, width, geometry, transpose):
    rad_start, total_hgt, total_azim, total_rad, cols = geometry
    margin = width - 1
    height_rows = x.shape[-3]
    radius_rows = x.shape[-1] - 2
    rad_index_all = rad_start - margin - 1 + jnp.arange(radius_rows + 2, dtype=jnp.int32)
    radius_all = total_azim / full_turn + rad_index_all.astype(jnp.float32) + 0.5
    rad_index = rad_index_all[1:-1]
    radius = radius_all[1:-1]
    outer_face = (radius + 0.5) * (rad_index < total_rad - 1).astype(jnp.float32)
    inner_face = (radius - 0.5) * (rad_index > 0).astype(jnp.float32)
    hgt_index = jnp.arange(height_rows, dtype=jnp.int32)
    upper_face = (hgt_index < total_hgt - 1).astype(jnp.float32)[:, None, None]
    lower_face = (hgt_index > 0).astype(jnp.float32)[:, None, None]
    leading = x.ndim - 3
    padded = jnp.pad(x, [(0, 0)] * leading + [(1, 1), (0, 0), (0, 0)])
    center = padded[..., 1:-1, 1:-1, 1:-1]
    if transpose:
        scaled = padded[..., 1:-1, 1:-1, :] / radius_all
        radial = outer_face * (scaled[..., 2:] - scaled[..., 1:-1]) - inner_face * (
            scaled[..., 1:-1] - scaled[..., :-2]
        )
    else:
        outward = padded[..., 1:-1, 1:-1, 2:]
        inward = padded[..., 1:-1, 1:-1, :-2]
        radial = (outer_face * (outward - center) - inner_face * (center - inward)) / radius
    arc_length = radius * (full_turn / total_azim)
    azimuthal = (padded[..., 1:-1, 2:, 1:-1] + padded[..., 1:-1, :-2, 1:-1] - 2.0 * center) / (
        arc_length * arc_length
    )
    vertical = upper_face * (padded[..., 2:, 1:-1, 1:-1] - center) + lower_face * (
        padded[..., :-2, 1:-1, 1:-1] - center
    )
    return radial + azimuthal + vertical


def chemical(density, grains):
    square_sum = jnp.sum(grains * grains, axis=0)
    cube_sum = jnp.sum(grains * grains * grains, axis=0)
    bulk_drive = 2.0 * bulk_weight * density * (1.0 - density) * (
        1.0 - 2.0 * density
    ) + grain_weight * (2.0 * density - 6.0 * square_sum + 4.0 * cube_sum)
    grain_drive = (
        12.0
        * grain_weight
        * (grains * (1.0 - density) - grains * grains * (2.0 - density) + grains * square_sum)
    )
    return (bulk_drive, grain_drive)


def shards(density, labels, observed, measured):
    height_rows, azim_rows, radius_rows = density.shape
    total_hgt = height_rows * lax.axis_size("hgt")
    geometry = (
        lax.axis_index("rad") * radius_rows,
        total_hgt,
        azim_rows * lax.axis_size("azim"),
        radius_rows * lax.axis_size("rad"),
        radius_rows,
    )
    target = jnp.where(measured != 0, observed, -1.0)
    packed = jnp.stack([density, labels.astype(jnp.float32), target])
    packed = halo_exchange(packed, "azim", 2, HALO, True)
    packed = halo_exchange(packed, "rad", 3, HALO, False)
    packed = gather_axis(packed, "hgt", 1)
    density, grain_label, target = packed[0], packed[1], packed[2]

    width = HALO
    grains = (
        grain_label[None] == jnp.arange(GRAINS, dtype=jnp.float32)[:, None, None, None]
    ).astype(jnp.float32)
    density = in_domain(density, width, geometry)
    grains = in_domain(grains, width, geometry)
    d_width, g_width = width, width
    history = []
    for moment in range(STEPS):
        history.append((density, d_width, grains, g_width))
        both = min(d_width, g_width)
        bulk_drive, grain_drive = chemical(crop(density, d_width, both), crop(grains, g_width, both))
        pot_width = min(d_width - 1, both)
        potential = crop(bulk_drive, both, pot_width) - cahn_gradient * crop(
            laplace(density, d_width, geometry, False), d_width - 1, pot_width
        )
        new_d_width = pot_width - 1
        flux_term = laplace(potential, pot_width, geometry, False)
        new_density = crop(density, d_width, new_d_width) + cahn_step * flux_term
        if moment + 1 < STEPS:
            new_g_width = min(g_width - 1, both)
            grain_spread = crop(laplace(grains, g_width, geometry, False), g_width - 1, new_g_width)
            new_grains = crop(grains, g_width, new_g_width) - allen_step * (
                crop(grain_drive, both, new_g_width) - allen_gradient * grain_spread
            )
            grains, g_width = in_domain(new_grains, new_g_width, geometry), new_g_width
        density, d_width = in_domain(new_density, new_d_width, geometry), new_d_width

    target = crop(target, width, d_width)
    costate = in_domain(jnp.where(target >= 0.0, density - target, 0.0), d_width, geometry)
    c_width = d_width
    last_density = crop(density, d_width, 0)
    cograins = jnp.zeros((GRAINS,) + costate.shape, jnp.float32)
    cg_width = c_width
    for moment in range(STEPS - 1, -1, -1):
        fields_density, fd_width, fields_grains, fg_width = history[moment]
        copotential = cahn_step * laplace(costate, c_width, geometry, True)
        nu_width = c_width - 1
        grain_spread = laplace(cograins, cg_width, geometry, True)
        point = min(nu_width, cg_width, fd_width, fg_width)
        unused, pullback = jax.vjp(
            chemical, crop(fields_density, fd_width, point), crop(fields_grains, fg_width, point)
        )
        pull_density, pull_grains = pullback(
            (crop(copotential, nu_width, point), -allen_step * crop(cograins, cg_width, point))
        )
        reaction = laplace(in_domain(copotential, nu_width, geometry), nu_width, geometry, True)
        new_c_width = nu_width - 1
        new_costate = (
            crop(costate, c_width, new_c_width)
            + crop(pull_density, point, new_c_width)
            - cahn_gradient * reaction
        )
        new_cg_width = min(cg_width - 1, point)
        new_cograins = (
            crop(cograins, cg_width, new_cg_width)
            + crop(pull_grains, point, new_cg_width)
            + allen_step * allen_gradient * crop(grain_spread, cg_width - 1, new_cg_width)
        )
        costate, c_width = in_domain(new_costate, new_c_width, geometry), new_c_width
        cograins, cg_width = in_domain(new_cograins, new_cg_width, geometry), new_cg_width

    costate = crop(costate, c_width, 0)
    cograins = crop(cograins, cg_width, 0)
    start = lax.axis_index("hgt") * height_rows
    own = lambda x: lax.dynamic_slice_in_dim(x, start, height_rows, axis=x.ndim - 3)
    return (own(last_density), own(costate), own(cograins))


def solution(mesh):
    in_specs = (
        P("hgt", "azim", "rad"),
        P("hgt", "azim", "rad"),
        P("hgt", "azim", "rad"),
        P("hgt", "azim", "rad"),
    )
    out_specs = (P("hgt", "azim", "rad"), P("hgt", "azim", "rad"), P(None, "hgt", "azim", "rad"))
    return jax.shard_map(shards, mesh=mesh, in_specs=in_specs, out_specs=out_specs, check_vma=False)
```

```python
import jax
import jax.numpy as jnp
from jax import lax
from jax.sharding import PartitionSpec as P

STEPS = 3
GRAINS = 4


bulk_weight = 16.0
grain_weight = 1.0
cahn_step = 0.005
allen_step = 0.05
cahn_gradient = 1.0
allen_gradient = 1.0
full_turn = 6.283185307179586

HALO = 4 * STEPS


def plane_exchange(block, width):
    azim_peers, rad_peers = (lax.axis_size("azim"), lax.axis_size("rad"))
    rows, cols = block.shape[-2], block.shape[-1]
    row_cut = {-1: (rows - width, rows), 0: (0, rows), 1: (0, width)}
    col_cut = {-1: (cols - width, cols), 0: (0, cols), 1: (0, width)}
    pieces = {}
    for da in (-1, 0, 1):
        for dr in (-1, 0, 1):
            if da == 0 and dr == 0:
                pieces[da, dr] = block
                continue
            r0, r1 = row_cut[da]
            c0, c1 = col_cut[dr]
            piece = block[..., r0:r1, c0:c1]
            pairs = []
            for a in range(azim_peers):
                for r in range(rad_peers):
                    if 0 <= r + dr < rad_peers:
                        source = ((a + da) % azim_peers) * rad_peers + (r + dr)
                        pairs.append((source, a * rad_peers + r))
            pieces[da, dr] = lax.ppermute(piece, ("azim", "rad"), pairs)
    bands = [jnp.concatenate([pieces[da, dr] for dr in (-1, 0, 1)], axis=-1) for da in (-1, 0, 1)]
    return jnp.concatenate(bands, axis=-2)


def gather_axis(block, axis, dim):
    peers = lax.axis_size(axis)
    if peers == 1:
        return block
    own = lax.axis_index(axis)
    parts = [block]
    for shift in range(1, peers):
        parts.append(lax.ppermute(block, axis, [(i, (i + shift) % peers) for i in range(peers)]))
    stacked = jnp.stack(parts)
    order = (own - jnp.arange(peers, dtype=jnp.int32)) % peers
    ordered = jnp.take(stacked, order, axis=0)
    ordered = jnp.moveaxis(ordered, 0, dim)
    shape = list(block.shape)
    shape[dim] = shape[dim] * peers
    return ordered.reshape(shape)


def crop(x, width, new_width):
    cut = width - new_width
    if cut == 0:
        return x
    return x[..., cut : x.shape[-2] - cut, cut : x.shape[-1] - cut]


def radial_mask(width, geometry):
    rad_start, total_hgt, total_azim, total_rad, cols = geometry
    rad_index = rad_start - width + jnp.arange(cols + 2 * width, dtype=jnp.int32)
    return (rad_index >= 0) & (rad_index < total_rad)


def in_domain(x, width, geometry):
    return jnp.where(radial_mask(width, geometry), x, 0.0)


def laplace(x, width, geometry, transpose):
    rad_start, total_hgt, total_azim, total_rad, cols = geometry
    margin = width - 1
    height_rows = x.shape[-3]
    radius_rows = x.shape[-1] - 2
    rad_index_all = rad_start - margin - 1 + jnp.arange(radius_rows + 2, dtype=jnp.int32)
    radius_all = total_azim / full_turn + rad_index_all.astype(jnp.float32) + 0.5
    rad_index = rad_index_all[1:-1]
    radius = radius_all[1:-1]
    inverse_radius = 1.0 / radius
    outer_face = (radius + 0.5) * (rad_index < total_rad - 1).astype(jnp.float32)
    inner_face = (radius - 0.5) * (rad_index > 0).astype(jnp.float32)
    hgt_index = jnp.arange(height_rows, dtype=jnp.int32)
    upper_face = (hgt_index < total_hgt - 1).astype(jnp.float32)[:, None, None]
    lower_face = (hgt_index > 0).astype(jnp.float32)[:, None, None]
    leading = x.ndim - 3
    padded = jnp.pad(x, [(0, 0)] * leading + [(1, 1), (0, 0), (0, 0)])
    center = padded[..., 1:-1, 1:-1, 1:-1]
    if transpose:
        scaled = padded[..., 1:-1, 1:-1, :] * (1.0 / radius_all)
        radial = outer_face * (scaled[..., 2:] - scaled[..., 1:-1]) - inner_face * (
            scaled[..., 1:-1] - scaled[..., :-2]
        )
    else:
        outward = padded[..., 1:-1, 1:-1, 2:]
        inward = padded[..., 1:-1, 1:-1, :-2]
        radial = (outer_face * (outward - center) - inner_face * (center - inward)) * inverse_radius
    arc_length = radius * (full_turn / total_azim)
    azimuthal = (padded[..., 1:-1, 2:, 1:-1] + padded[..., 1:-1, :-2, 1:-1] - 2.0 * center) * (
        1.0 / (arc_length * arc_length)
    )
    vertical = upper_face * (padded[..., 2:, 1:-1, 1:-1] - center) + lower_face * (
        padded[..., :-2, 1:-1, 1:-1] - center
    )
    return radial + azimuthal + vertical


def chemical(density, grains):
    square_sum = jnp.sum(grains * grains, axis=0)
    cube_sum = jnp.sum(grains * grains * grains, axis=0)
    bulk_drive = 2.0 * bulk_weight * density * (1.0 - density) * (
        1.0 - 2.0 * density
    ) + grain_weight * (2.0 * density - 6.0 * square_sum + 4.0 * cube_sum)
    grain_drive = (
        12.0
        * grain_weight
        * (grains * (1.0 - density) - grains * grains * (2.0 - density) + grains * square_sum)
    )
    return (bulk_drive, grain_drive)


def shards(density, labels, observed, measured):
    height_rows, azim_rows, radius_rows = density.shape
    total_hgt = height_rows * lax.axis_size("hgt")
    geometry = (
        lax.axis_index("rad") * radius_rows,
        total_hgt,
        azim_rows * lax.axis_size("azim"),
        radius_rows * lax.axis_size("rad"),
        radius_rows,
    )
    target = jnp.where(measured != 0, observed, -1.0)
    packed = jnp.stack([density, labels.astype(jnp.float32), target])
    packed = plane_exchange(packed, HALO)
    packed = gather_axis(packed, "hgt", 1)
    density, grain_label, target = packed[0], packed[1], packed[2]

    width = HALO
    grains = (
        grain_label[None] == jnp.arange(GRAINS, dtype=jnp.float32)[:, None, None, None]
    ).astype(jnp.float32)
    density = in_domain(density, width, geometry)
    grains = in_domain(grains, width, geometry)
    d_width, g_width = width, width
    history = []
    for moment in range(STEPS):
        history.append((density, d_width, grains, g_width))
        both = min(d_width, g_width)
        bulk_drive, grain_drive = chemical(crop(density, d_width, both), crop(grains, g_width, both))
        pot_width = min(d_width - 1, both)
        potential = crop(bulk_drive, both, pot_width) - cahn_gradient * crop(
            laplace(density, d_width, geometry, False), d_width - 1, pot_width
        )
        new_d_width = pot_width - 1
        flux_term = laplace(potential, pot_width, geometry, False)
        new_density = crop(density, d_width, new_d_width) + cahn_step * flux_term
        if moment + 1 < STEPS:
            new_g_width = min(g_width - 1, both)
            grain_spread = crop(laplace(grains, g_width, geometry, False), g_width - 1, new_g_width)
            new_grains = crop(grains, g_width, new_g_width) - allen_step * (
                crop(grain_drive, both, new_g_width) - allen_gradient * grain_spread
            )
            grains, g_width = in_domain(new_grains, new_g_width, geometry), new_g_width
        density, d_width = in_domain(new_density, new_d_width, geometry), new_d_width

    target = crop(target, width, d_width)
    costate = in_domain(jnp.where(target >= 0.0, density - target, 0.0), d_width, geometry)
    c_width = d_width
    last_density = crop(density, d_width, 0)
    cograins = jnp.zeros((GRAINS,) + costate.shape, jnp.float32)
    cg_width = c_width
    for moment in range(STEPS - 1, -1, -1):
        fields_density, fd_width, fields_grains, fg_width = history[moment]
        copotential = cahn_step * laplace(costate, c_width, geometry, True)
        nu_width = c_width - 1
        grain_spread = laplace(cograins, cg_width, geometry, True)
        point = min(nu_width, cg_width, fd_width, fg_width)
        unused, pullback = jax.vjp(
            chemical, crop(fields_density, fd_width, point), crop(fields_grains, fg_width, point)
        )
        pull_density, pull_grains = pullback(
            (crop(copotential, nu_width, point), -allen_step * crop(cograins, cg_width, point))
        )
        reaction = laplace(in_domain(copotential, nu_width, geometry), nu_width, geometry, True)
        new_c_width = nu_width - 1
        new_costate = (
            crop(costate, c_width, new_c_width)
            + crop(pull_density, point, new_c_width)
            - cahn_gradient * reaction
        )
        new_cg_width = min(cg_width - 1, point)
        new_cograins = (
            crop(cograins, cg_width, new_cg_width)
            + crop(pull_grains, point, new_cg_width)
            + allen_step * allen_gradient * crop(grain_spread, cg_width - 1, new_cg_width)
        )
        costate, c_width = in_domain(new_costate, new_c_width, geometry), new_c_width
        cograins, cg_width = in_domain(new_cograins, new_cg_width, geometry), new_cg_width

    costate = crop(costate, c_width, 0)
    cograins = crop(cograins, cg_width, 0)
    start = lax.axis_index("hgt") * height_rows
    own = lambda x: lax.dynamic_slice_in_dim(x, start, height_rows, axis=x.ndim - 3)
    return (own(last_density), own(costate), own(cograins))


def solution(mesh):
    in_specs = (
        P("hgt", "azim", "rad"),
        P("hgt", "azim", "rad"),
        P("hgt", "azim", "rad"),
        P("hgt", "azim", "rad"),
    )
    out_specs = (P("hgt", "azim", "rad"), P("hgt", "azim", "rad"), P(None, "hgt", "azim", "rad"))
    return jax.shard_map(shards, mesh=mesh, in_specs=in_specs, out_specs=out_specs, check_vma=False)
```

```python
import jax
import jax.numpy as jnp
from jax import lax
from jax.sharding import PartitionSpec as P

STEPS = 3
GRAINS = 4


bulk_weight = 16.0
grain_weight = 1.0
cahn_step = 0.005
allen_step = 0.05
cahn_gradient = 1.0
allen_gradient = 1.0
full_turn = 6.283185307179586

HALO = 4 * STEPS


def halo_exchange(block, axis, dim, width, cyclic):
    peers, length = (lax.axis_size(axis), block.shape[dim])
    up = [(i, (i + 1) % peers) for i in range(peers) if cyclic or i + 1 < peers]
    down = [(j, i) for i, j in up]
    last = lax.slice_in_dim(block, length - width, length, axis=dim)
    leading = lax.slice_in_dim(block, 0, width, axis=dim)
    before = lax.ppermute(last, axis, up)
    after = lax.ppermute(leading, axis, down)
    return jnp.concatenate([before, block, after], axis=dim)


def gather_axis(block, axis, dim):
    peers = lax.axis_size(axis)
    if peers == 1:
        return block
    own = lax.axis_index(axis)
    parts = [block]
    for shift in range(1, peers):
        parts.append(lax.ppermute(block, axis, [(i, (i + shift) % peers) for i in range(peers)]))
    stacked = jnp.stack(parts)
    order = (own - jnp.arange(peers, dtype=jnp.int32)) % peers
    ordered = jnp.take(stacked, order, axis=0)
    ordered = jnp.moveaxis(ordered, 0, dim)
    shape = list(block.shape)
    shape[dim] = shape[dim] * peers
    return ordered.reshape(shape)


def chip_window(block, width):
    peers, own, rad_peers = (lax.axis_size("hgt"), lax.axis_index("hgt"), lax.axis_size("rad"))
    cols = block.shape[-1]
    part = cols // peers
    piece = jnp.where(own == 0, block[..., :width], block[..., cols - width :])
    pairs = []
    for r in range(rad_peers - 1):
        pairs.append((r * peers + peers - 1, (r + 1) * peers))
        pairs.append(((r + 1) * peers, r * peers + peers - 1))
    received = lax.ppermute(piece, ("rad", "hgt"), pairs)
    padded = jnp.concatenate([received, block, received], axis=-1)
    return lax.dynamic_slice_in_dim(padded, own * part, part + 2 * width, axis=padded.ndim - 1)


def scatter_heights(x, height_rows):
    peers, own = (lax.axis_size("hgt"), lax.axis_index("hgt"))
    parts = []
    for shift in range(peers):
        dest = (own + shift) % peers
        piece = lax.dynamic_slice_in_dim(x, dest * height_rows, height_rows, axis=1)
        if shift:
            piece = lax.ppermute(piece, "hgt", [(i, (i + shift) % peers) for i in range(peers)])
        parts.append(piece)
    stacked = jnp.stack(parts)
    order = (own - jnp.arange(peers, dtype=jnp.int32)) % peers
    ordered = jnp.moveaxis(jnp.take(stacked, order, axis=0), 0, -2)
    shape = ordered.shape
    return ordered.reshape(shape[:-2] + (shape[-2] * shape[-1],))


def crop(x, width, new_width):
    cut = width - new_width
    if cut == 0:
        return x
    return x[..., cut : x.shape[-2] - cut, cut : x.shape[-1] - cut]


def radial_mask(width, geometry):
    rad_start, total_hgt, total_azim, total_rad, cols = geometry
    rad_index = rad_start - width + jnp.arange(cols + 2 * width, dtype=jnp.int32)
    return (rad_index >= 0) & (rad_index < total_rad)


def in_domain(x, width, geometry):
    return jnp.where(radial_mask(width, geometry), x, 0.0)


def laplace(x, width, geometry, transpose):
    rad_start, total_hgt, total_azim, total_rad, cols = geometry
    margin = width - 1
    height_rows = x.shape[-3]
    radius_rows = x.shape[-1] - 2
    rad_index_all = rad_start - margin - 1 + jnp.arange(radius_rows + 2, dtype=jnp.int32)
    radius_all = total_azim / full_turn + rad_index_all.astype(jnp.float32) + 0.5
    rad_index = rad_index_all[1:-1]
    radius = radius_all[1:-1]
    outer_face = (radius + 0.5) * (rad_index < total_rad - 1).astype(jnp.float32)
    inner_face = (radius - 0.5) * (rad_index > 0).astype(jnp.float32)
    hgt_index = jnp.arange(height_rows, dtype=jnp.int32)
    upper_face = (hgt_index < total_hgt - 1).astype(jnp.float32)[:, None, None]
    lower_face = (hgt_index > 0).astype(jnp.float32)[:, None, None]
    leading = x.ndim - 3
    padded = jnp.pad(x, [(0, 0)] * leading + [(1, 1), (0, 0), (0, 0)])
    center = padded[..., 1:-1, 1:-1, 1:-1]
    if transpose:
        scaled = padded[..., 1:-1, 1:-1, :] / radius_all
        radial = outer_face * (scaled[..., 2:] - scaled[..., 1:-1]) - inner_face * (
            scaled[..., 1:-1] - scaled[..., :-2]
        )
    else:
        outward = padded[..., 1:-1, 1:-1, 2:]
        inward = padded[..., 1:-1, 1:-1, :-2]
        radial = (outer_face * (outward - center) - inner_face * (center - inward)) / radius
    arc_length = radius * (full_turn / total_azim)
    azimuthal = (padded[..., 1:-1, 2:, 1:-1] + padded[..., 1:-1, :-2, 1:-1] - 2.0 * center) / (
        arc_length * arc_length
    )
    vertical = upper_face * (padded[..., 2:, 1:-1, 1:-1] - center) + lower_face * (
        padded[..., :-2, 1:-1, 1:-1] - center
    )
    return radial + azimuthal + vertical


def chemical(density, grains):
    square_sum = jnp.sum(grains * grains, axis=0)
    cube_sum = jnp.sum(grains * grains * grains, axis=0)
    bulk_drive = 2.0 * bulk_weight * density * (1.0 - density) * (
        1.0 - 2.0 * density
    ) + grain_weight * (2.0 * density - 6.0 * square_sum + 4.0 * cube_sum)
    grain_drive = (
        12.0
        * grain_weight
        * (grains * (1.0 - density) - grains * grains * (2.0 - density) + grains * square_sum)
    )
    return (bulk_drive, grain_drive)


def shards(density, labels, observed, measured):
    height_rows, azim_rows, radius_rows = density.shape
    total_hgt = height_rows * lax.axis_size("hgt")
    part = radius_rows // lax.axis_size("hgt")
    geometry = (
        lax.axis_index("rad") * radius_rows + lax.axis_index("hgt") * part,
        total_hgt,
        azim_rows * lax.axis_size("azim"),
        radius_rows * lax.axis_size("rad"),
        part,
    )
    target = jnp.where(measured != 0, observed, -1.0)
    packed = jnp.stack([density, labels.astype(jnp.float32), target])
    packed = gather_axis(packed, "hgt", 1)
    packed = chip_window(packed, HALO)
    packed = halo_exchange(packed, "azim", 2, HALO, True)
    density, grain_label, target = packed[0], packed[1], packed[2]

    width = HALO
    grains = (
        grain_label[None] == jnp.arange(GRAINS, dtype=jnp.float32)[:, None, None, None]
    ).astype(jnp.float32)
    density = in_domain(density, width, geometry)
    grains = in_domain(grains, width, geometry)
    d_width, g_width = width, width
    history = []
    for moment in range(STEPS):
        history.append((density, d_width, grains, g_width))
        both = min(d_width, g_width)
        bulk_drive, grain_drive = chemical(crop(density, d_width, both), crop(grains, g_width, both))
        pot_width = min(d_width - 1, both)
        potential = crop(bulk_drive, both, pot_width) - cahn_gradient * crop(
            laplace(density, d_width, geometry, False), d_width - 1, pot_width
        )
        new_d_width = pot_width - 1
        flux_term = laplace(potential, pot_width, geometry, False)
        new_density = crop(density, d_width, new_d_width) + cahn_step * flux_term
        if moment + 1 < STEPS:
            new_g_width = min(g_width - 1, both)
            grain_spread = crop(laplace(grains, g_width, geometry, False), g_width - 1, new_g_width)
            new_grains = crop(grains, g_width, new_g_width) - allen_step * (
                crop(grain_drive, both, new_g_width) - allen_gradient * grain_spread
            )
            grains, g_width = in_domain(new_grains, new_g_width, geometry), new_g_width
        density, d_width = in_domain(new_density, new_d_width, geometry), new_d_width

    target = crop(target, width, d_width)
    costate = in_domain(jnp.where(target >= 0.0, density - target, 0.0), d_width, geometry)
    c_width = d_width
    last_density = crop(density, d_width, 0)
    cograins = jnp.zeros((GRAINS,) + costate.shape, jnp.float32)
    cg_width = c_width
    for moment in range(STEPS - 1, -1, -1):
        fields_density, fd_width, fields_grains, fg_width = history[moment]
        copotential = cahn_step * laplace(costate, c_width, geometry, True)
        nu_width = c_width - 1
        grain_spread = laplace(cograins, cg_width, geometry, True)
        point = min(nu_width, cg_width, fd_width, fg_width)
        unused, pullback = jax.vjp(
            chemical, crop(fields_density, fd_width, point), crop(fields_grains, fg_width, point)
        )
        pull_density, pull_grains = pullback(
            (crop(copotential, nu_width, point), -allen_step * crop(cograins, cg_width, point))
        )
        reaction = laplace(in_domain(copotential, nu_width, geometry), nu_width, geometry, True)
        new_c_width = nu_width - 1
        new_costate = (
            crop(costate, c_width, new_c_width)
            + crop(pull_density, point, new_c_width)
            - cahn_gradient * reaction
        )
        new_cg_width = min(cg_width - 1, point)
        new_cograins = (
            crop(cograins, cg_width, new_cg_width)
            + crop(pull_grains, point, new_cg_width)
            + allen_step * allen_gradient * crop(grain_spread, cg_width - 1, new_cg_width)
        )
        costate, c_width = in_domain(new_costate, new_c_width, geometry), new_c_width
        cograins, cg_width = in_domain(new_cograins, new_cg_width, geometry), new_cg_width

    costate = crop(costate, c_width, 0)
    cograins = crop(cograins, cg_width, 0)
    result = scatter_heights(
        jnp.concatenate([last_density[None], costate[None], cograins], axis=0), height_rows
    )
    return (result[0], result[1], result[2:])


def solution(mesh):
    in_specs = (
        P("hgt", "azim", "rad"),
        P("hgt", "azim", "rad"),
        P("hgt", "azim", "rad"),
        P("hgt", "azim", "rad"),
    )
    out_specs = (P("hgt", "azim", "rad"), P("hgt", "azim", "rad"), P(None, "hgt", "azim", "rad"))
    return jax.shard_map(shards, mesh=mesh, in_specs=in_specs, out_specs=out_specs, check_vma=False)
```

```python
import jax
import jax.numpy as jnp
from jax import lax
from jax.sharding import PartitionSpec as P

STEPS = 3
GRAINS = 4


bulk_weight = 16.0
grain_weight = 1.0
cahn_step = 0.005
allen_step = 0.05
cahn_gradient = 1.0
allen_gradient = 1.0
full_turn = 6.283185307179586

HALO = 4 * STEPS


def halo_exchange(block, axis, dim, width, cyclic):
    peers, length = (lax.axis_size(axis), block.shape[dim])
    up = [(i, (i + 1) % peers) for i in range(peers) if cyclic or i + 1 < peers]
    down = [(j, i) for i, j in up]
    last = lax.slice_in_dim(block, length - width, length, axis=dim)
    leading = lax.slice_in_dim(block, 0, width, axis=dim)
    before = lax.ppermute(last, axis, up)
    after = lax.ppermute(leading, axis, down)
    return jnp.concatenate([before, block, after], axis=dim)


def azim_exchange(fields, widths):
    peers = lax.axis_size("azim")
    up = [(i, (i + 1) % peers) for i in range(peers)]
    down = [(j, i) for i, j in up]
    rows = fields[0].shape[-2]
    last = jnp.concatenate([f[..., rows - w :, :] for f, w in zip(fields, widths)], axis=-2)
    leading = jnp.concatenate([f[..., :w, :] for f, w in zip(fields, widths)], axis=-2)
    before = lax.ppermute(last, "azim", up)
    after = lax.ppermute(leading, "azim", down)
    out, at = [], 0
    for f, w in zip(fields, widths):
        out.append(jnp.concatenate([before[..., at : at + w, :], f, after[..., at : at + w, :]], axis=-2))
        at += w
    return out


def gather_axis(block, axis, dim):
    peers = lax.axis_size(axis)
    if peers == 1:
        return block
    own = lax.axis_index(axis)
    parts = [block]
    for shift in range(1, peers):
        parts.append(lax.ppermute(block, axis, [(i, (i + shift) % peers) for i in range(peers)]))
    stacked = jnp.stack(parts)
    order = (own - jnp.arange(peers, dtype=jnp.int32)) % peers
    ordered = jnp.take(stacked, order, axis=0)
    ordered = jnp.moveaxis(ordered, 0, dim)
    shape = list(block.shape)
    shape[dim] = shape[dim] * peers
    return ordered.reshape(shape)


def chip_window(block, width):
    peers, own, rad_peers = (lax.axis_size("hgt"), lax.axis_index("hgt"), lax.axis_size("rad"))
    cols = block.shape[-1]
    part = cols // peers
    piece = jnp.where(own == 0, block[..., :width], block[..., cols - width :])
    pairs = []
    for r in range(rad_peers - 1):
        pairs.append((r * peers + peers - 1, (r + 1) * peers))
        pairs.append(((r + 1) * peers, r * peers + peers - 1))
    received = lax.ppermute(piece, ("rad", "hgt"), pairs)
    padded = jnp.concatenate([received, block, received], axis=-1)
    return lax.dynamic_slice_in_dim(padded, own * part, part + 2 * width, axis=padded.ndim - 1)


def scatter_heights(x, height_rows):
    peers, own = (lax.axis_size("hgt"), lax.axis_index("hgt"))
    parts = []
    for shift in range(peers):
        dest = (own + shift) % peers
        piece = lax.dynamic_slice_in_dim(x, dest * height_rows, height_rows, axis=1)
        if shift:
            piece = lax.ppermute(piece, "hgt", [(i, (i + shift) % peers) for i in range(peers)])
        parts.append(piece)
    stacked = jnp.stack(parts)
    order = (own - jnp.arange(peers, dtype=jnp.int32)) % peers
    ordered = jnp.moveaxis(jnp.take(stacked, order, axis=0), 0, -2)
    shape = ordered.shape
    return ordered.reshape(shape[:-2] + (shape[-2] * shape[-1],))


def crop(x, width, new_width):
    cut = width - new_width
    if cut == 0:
        return x
    return x[..., cut : x.shape[-2] - cut, cut : x.shape[-1] - cut]


def radial_mask(width, geometry):
    rad_start, total_hgt, total_azim, total_rad, cols = geometry
    rad_index = rad_start - width + jnp.arange(cols + 2 * width, dtype=jnp.int32)
    return (rad_index >= 0) & (rad_index < total_rad)


def in_domain(x, width, geometry):
    return jnp.where(radial_mask(width, geometry), x, 0.0)


def laplace(x, width, geometry, transpose):
    rad_start, total_hgt, total_azim, total_rad, cols = geometry
    margin = width - 1
    height_rows = x.shape[-3]
    radius_rows = x.shape[-1] - 2
    rad_index_all = rad_start - margin - 1 + jnp.arange(radius_rows + 2, dtype=jnp.int32)
    radius_all = total_azim / full_turn + rad_index_all.astype(jnp.float32) + 0.5
    rad_index = rad_index_all[1:-1]
    radius = radius_all[1:-1]
    outer_face = (radius + 0.5) * (rad_index < total_rad - 1).astype(jnp.float32)
    inner_face = (radius - 0.5) * (rad_index > 0).astype(jnp.float32)
    hgt_index = jnp.arange(height_rows, dtype=jnp.int32)
    upper_face = (hgt_index < total_hgt - 1).astype(jnp.float32)[:, None, None]
    lower_face = (hgt_index > 0).astype(jnp.float32)[:, None, None]
    leading = x.ndim - 3
    padded = jnp.pad(x, [(0, 0)] * leading + [(1, 1), (0, 0), (0, 0)])
    center = padded[..., 1:-1, 1:-1, 1:-1]
    if transpose:
        scaled = padded[..., 1:-1, 1:-1, :] / radius_all
        radial = outer_face * (scaled[..., 2:] - scaled[..., 1:-1]) - inner_face * (
            scaled[..., 1:-1] - scaled[..., :-2]
        )
    else:
        outward = padded[..., 1:-1, 1:-1, 2:]
        inward = padded[..., 1:-1, 1:-1, :-2]
        radial = (outer_face * (outward - center) - inner_face * (center - inward)) / radius
    arc_length = radius * (full_turn / total_azim)
    azimuthal = (padded[..., 1:-1, 2:, 1:-1] + padded[..., 1:-1, :-2, 1:-1] - 2.0 * center) / (
        arc_length * arc_length
    )
    vertical = upper_face * (padded[..., 2:, 1:-1, 1:-1] - center) + lower_face * (
        padded[..., :-2, 1:-1, 1:-1] - center
    )
    return radial + azimuthal + vertical


def chemical(density, grains):
    square_sum = jnp.sum(grains * grains, axis=0)
    cube_sum = jnp.sum(grains * grains * grains, axis=0)
    bulk_drive = 2.0 * bulk_weight * density * (1.0 - density) * (
        1.0 - 2.0 * density
    ) + grain_weight * (2.0 * density - 6.0 * square_sum + 4.0 * cube_sum)
    grain_drive = (
        12.0
        * grain_weight
        * (grains * (1.0 - density) - grains * grains * (2.0 - density) + grains * square_sum)
    )
    return (bulk_drive, grain_drive)


def shards(density, labels, observed, measured):
    height_rows, azim_rows, radius_rows = density.shape
    total_hgt = height_rows * lax.axis_size("hgt")
    part = radius_rows // lax.axis_size("hgt")
    geometry = (
        lax.axis_index("rad") * radius_rows + lax.axis_index("hgt") * part,
        total_hgt,
        azim_rows * lax.axis_size("azim"),
        radius_rows * lax.axis_size("rad"),
        part,
    )
    packed = jnp.stack([density, labels.astype(jnp.float32), observed, measured.astype(jnp.float32)])
    packed = gather_axis(packed, "hgt", 1)
    packed = chip_window(packed, HALO)
    widths = (HALO, HALO - 1, 2 * STEPS, 2 * STEPS)
    density, grain_label, observed, measured = [
        f[..., HALO - w : f.shape[-1] - (HALO - w)]
        for f, w in zip(azim_exchange(list(packed), widths), widths)
    ]
    grains = (
        grain_label[None] == jnp.arange(GRAINS, dtype=jnp.float32)[:, None, None, None]
    ).astype(jnp.float32)
    d_width, g_width = widths[0], widths[1]
    density = in_domain(density, d_width, geometry)
    grains = in_domain(grains, g_width, geometry)
    history = []
    for moment in range(STEPS):
        history.append((density, d_width, grains, g_width))
        both = min(d_width, g_width)
        bulk_drive, grain_drive = chemical(crop(density, d_width, both), crop(grains, g_width, both))
        pot_width = min(d_width - 1, both)
        potential = crop(bulk_drive, both, pot_width) - cahn_gradient * crop(
            laplace(density, d_width, geometry, False), d_width - 1, pot_width
        )
        new_d_width = pot_width - 1
        flux_term = laplace(potential, pot_width, geometry, False)
        new_density = crop(density, d_width, new_d_width) + cahn_step * flux_term
        if moment + 1 < STEPS:
            new_g_width = min(g_width - 1, both)
            grain_spread = crop(laplace(grains, g_width, geometry, False), g_width - 1, new_g_width)
            new_grains = crop(grains, g_width, new_g_width) - allen_step * (
                crop(grain_drive, both, new_g_width) - allen_gradient * grain_spread
            )
            grains, g_width = in_domain(new_grains, new_g_width, geometry), new_g_width
        density, d_width = in_domain(new_density, new_d_width, geometry), new_d_width

    observed = crop(observed, widths[2], d_width)
    measured = crop(measured, widths[3], d_width)
    costate = in_domain(measured * (density - observed), d_width, geometry)
    c_width = d_width
    last_density = crop(density, d_width, 0)
    cograins = jnp.zeros((GRAINS,) + costate.shape, jnp.float32)
    cg_width = c_width
    for moment in range(STEPS - 1, -1, -1):
        fields_density, fd_width, fields_grains, fg_width = history[moment]
        copotential = cahn_step * laplace(costate, c_width, geometry, True)
        nu_width = c_width - 1
        grain_spread = laplace(cograins, cg_width, geometry, True)
        point = min(nu_width, cg_width, fd_width, fg_width)
        unused, pullback = jax.vjp(
            chemical, crop(fields_density, fd_width, point), crop(fields_grains, fg_width, point)
        )
        pull_density, pull_grains = pullback(
            (crop(copotential, nu_width, point), -allen_step * crop(cograins, cg_width, point))
        )
        reaction = laplace(in_domain(copotential, nu_width, geometry), nu_width, geometry, True)
        new_c_width = nu_width - 1
        new_costate = (
            crop(costate, c_width, new_c_width)
            + crop(pull_density, point, new_c_width)
            - cahn_gradient * reaction
        )
        new_cg_width = min(cg_width - 1, point)
        new_cograins = (
            crop(cograins, cg_width, new_cg_width)
            + crop(pull_grains, point, new_cg_width)
            + allen_step * allen_gradient * crop(grain_spread, cg_width - 1, new_cg_width)
        )
        costate, c_width = in_domain(new_costate, new_c_width, geometry), new_c_width
        cograins, cg_width = in_domain(new_cograins, new_cg_width, geometry), new_cg_width

    costate = crop(costate, c_width, 0)
    cograins = crop(cograins, cg_width, 0)
    result = scatter_heights(
        jnp.concatenate([last_density[None], costate[None], cograins], axis=0), height_rows
    )
    return (result[0], result[1], result[2:])


def solution(mesh):
    in_specs = (
        P("hgt", "azim", "rad"),
        P("hgt", "azim", "rad"),
        P("hgt", "azim", "rad"),
        P("hgt", "azim", "rad"),
    )
    out_specs = (P("hgt", "azim", "rad"), P("hgt", "azim", "rad"), P(None, "hgt", "azim", "rad"))
    return jax.shard_map(shards, mesh=mesh, in_specs=in_specs, out_specs=out_specs, check_vma=False)
```

```python
import jax
import jax.numpy as jnp
from jax import lax
from jax.sharding import PartitionSpec as P

STEPS = 3
GRAINS = 4


bulk_weight = 16.0
grain_weight = 1.0
cahn_step = 0.005
allen_step = 0.05
cahn_gradient = 1.0
allen_gradient = 1.0
full_turn = 6.283185307179586

HALO = 4 * STEPS


def halo_exchange(block, axis, dim, width, cyclic):
    peers, length = (lax.axis_size(axis), block.shape[dim])
    up = [(i, (i + 1) % peers) for i in range(peers) if cyclic or i + 1 < peers]
    down = [(j, i) for i, j in up]
    last = lax.slice_in_dim(block, length - width, length, axis=dim)
    leading = lax.slice_in_dim(block, 0, width, axis=dim)
    before = lax.ppermute(last, axis, up)
    after = lax.ppermute(leading, axis, down)
    return jnp.concatenate([before, block, after], axis=dim)


def azim_exchange(fields, widths):
    peers = lax.axis_size("azim")
    up = [(i, (i + 1) % peers) for i in range(peers)]
    down = [(j, i) for i, j in up]
    rows = fields[0].shape[-2]
    last = jnp.concatenate([f[..., rows - w :, :] for f, w in zip(fields, widths)], axis=-2)
    leading = jnp.concatenate([f[..., :w, :] for f, w in zip(fields, widths)], axis=-2)
    before = lax.ppermute(last, "azim", up)
    after = lax.ppermute(leading, "azim", down)
    out, at = [], 0
    for f, w in zip(fields, widths):
        out.append(jnp.concatenate([before[..., at : at + w, :], f, after[..., at : at + w, :]], axis=-2))
        at += w
    return out


def gather_axis(block, axis, dim):
    peers = lax.axis_size(axis)
    if peers == 1:
        return block
    own = lax.axis_index(axis)
    parts = [block]
    for shift in range(1, peers):
        parts.append(lax.ppermute(block, axis, [(i, (i + shift) % peers) for i in range(peers)]))
    stacked = jnp.stack(parts)
    order = (own - jnp.arange(peers, dtype=jnp.int32)) % peers
    ordered = jnp.take(stacked, order, axis=0)
    ordered = jnp.moveaxis(ordered, 0, dim)
    shape = list(block.shape)
    shape[dim] = shape[dim] * peers
    return ordered.reshape(shape)


def chip_window(block, width):
    peers, own, rad_peers = (lax.axis_size("hgt"), lax.axis_index("hgt"), lax.axis_size("rad"))
    cols = block.shape[-1]
    part = cols // peers
    piece = jnp.where(own == 0, block[..., :width], block[..., cols - width :])
    pairs = []
    for r in range(rad_peers - 1):
        pairs.append((r * peers + peers - 1, (r + 1) * peers))
        pairs.append(((r + 1) * peers, r * peers + peers - 1))
    received = lax.ppermute(piece, ("rad", "hgt"), pairs)
    padded = jnp.concatenate([received, block, received], axis=-1)
    return lax.dynamic_slice_in_dim(padded, own * part, part + 2 * width, axis=padded.ndim - 1)


def edge_columns(block, width):
    own, rad_peers = (lax.axis_index("hgt"), lax.axis_size("rad"))
    cols = block.shape[-1]
    first, last = (block[..., :width], block[..., cols - width :])
    cross, same = ([], [])
    for r in range(rad_peers - 1):
        cross += [(2 * r + 1, 2 * r + 2), (2 * r + 2, 2 * r + 1)]
        same += [(2 * r, 2 * r + 2), (2 * r + 3, 2 * r + 1)]
    from_cross = lax.ppermute(jnp.where(own == 0, first, last), ("rad", "hgt"), cross)
    from_same = lax.ppermute(jnp.where(own == 0, last, first), ("rad", "hgt"), same)
    return jnp.where(
        own == 0,
        jnp.concatenate([from_same, from_cross], axis=1),
        jnp.concatenate([from_cross, from_same], axis=1),
    )


def two_core_window(block, received, width):
    own = lax.axis_index("hgt")
    part = block.shape[-1] // 2
    padded = jnp.concatenate([received, block, received], axis=-1)
    return lax.dynamic_slice_in_dim(padded, own * part, part + 2 * width, axis=padded.ndim - 1)


def scatter_heights(x, height_rows):
    peers, own = (lax.axis_size("hgt"), lax.axis_index("hgt"))
    parts = []
    for shift in range(peers):
        dest = (own + shift) % peers
        piece = lax.dynamic_slice_in_dim(x, dest * height_rows, height_rows, axis=1)
        if shift:
            piece = lax.ppermute(piece, "hgt", [(i, (i + shift) % peers) for i in range(peers)])
        parts.append(piece)
    stacked = jnp.stack(parts)
    order = (own - jnp.arange(peers, dtype=jnp.int32)) % peers
    ordered = jnp.moveaxis(jnp.take(stacked, order, axis=0), 0, -2)
    shape = ordered.shape
    return ordered.reshape(shape[:-2] + (shape[-2] * shape[-1],))


def crop(x, width, new_width):
    cut = width - new_width
    if cut == 0:
        return x
    return x[..., cut : x.shape[-2] - cut, cut : x.shape[-1] - cut]


def radial_mask(width, geometry):
    rad_start, total_hgt, total_azim, total_rad, cols = geometry
    rad_index = rad_start - width + jnp.arange(cols + 2 * width, dtype=jnp.int32)
    return (rad_index >= 0) & (rad_index < total_rad)


def in_domain(x, width, geometry):
    return jnp.where(radial_mask(width, geometry), x, 0.0)


def laplace(x, width, geometry, transpose):
    rad_start, total_hgt, total_azim, total_rad, cols = geometry
    margin = width - 1
    height_rows = x.shape[-3]
    radius_rows = x.shape[-1] - 2
    rad_index_all = rad_start - margin - 1 + jnp.arange(radius_rows + 2, dtype=jnp.int32)
    radius_all = total_azim / full_turn + rad_index_all.astype(jnp.float32) + 0.5
    rad_index = rad_index_all[1:-1]
    radius = radius_all[1:-1]
    outer_face = (radius + 0.5) * (rad_index < total_rad - 1).astype(jnp.float32)
    inner_face = (radius - 0.5) * (rad_index > 0).astype(jnp.float32)
    hgt_index = jnp.arange(height_rows, dtype=jnp.int32)
    upper_face = (hgt_index < total_hgt - 1).astype(jnp.float32)[:, None, None]
    lower_face = (hgt_index > 0).astype(jnp.float32)[:, None, None]
    leading = x.ndim - 3
    padded = jnp.pad(x, [(0, 0)] * leading + [(1, 1), (0, 0), (0, 0)])
    center = padded[..., 1:-1, 1:-1, 1:-1]
    if transpose:
        scaled = padded[..., 1:-1, 1:-1, :] / radius_all
        radial = outer_face * (scaled[..., 2:] - scaled[..., 1:-1]) - inner_face * (
            scaled[..., 1:-1] - scaled[..., :-2]
        )
    else:
        outward = padded[..., 1:-1, 1:-1, 2:]
        inward = padded[..., 1:-1, 1:-1, :-2]
        radial = (outer_face * (outward - center) - inner_face * (center - inward)) / radius
    arc_length = radius * (full_turn / total_azim)
    azimuthal = (padded[..., 1:-1, 2:, 1:-1] + padded[..., 1:-1, :-2, 1:-1] - 2.0 * center) / (
        arc_length * arc_length
    )
    vertical = upper_face * (padded[..., 2:, 1:-1, 1:-1] - center) + lower_face * (
        padded[..., :-2, 1:-1, 1:-1] - center
    )
    return radial + azimuthal + vertical


def chemical(density, grains):
    square_sum = jnp.sum(grains * grains, axis=0)
    cube_sum = jnp.sum(grains * grains * grains, axis=0)
    bulk_drive = 2.0 * bulk_weight * density * (1.0 - density) * (
        1.0 - 2.0 * density
    ) + grain_weight * (2.0 * density - 6.0 * square_sum + 4.0 * cube_sum)
    grain_drive = (
        12.0
        * grain_weight
        * (grains * (1.0 - density) - grains * grains * (2.0 - density) + grains * square_sum)
    )
    return (bulk_drive, grain_drive)


def shards(density, labels, observed, measured):
    height_rows, azim_rows, radius_rows = density.shape
    total_hgt = height_rows * lax.axis_size("hgt")
    part = radius_rows // lax.axis_size("hgt")
    geometry = (
        lax.axis_index("rad") * radius_rows + lax.axis_index("hgt") * part,
        total_hgt,
        azim_rows * lax.axis_size("azim"),
        radius_rows * lax.axis_size("rad"),
        part,
    )
    packed = jnp.stack([density, labels.astype(jnp.float32), observed, measured.astype(jnp.float32)])
    if lax.axis_size("hgt") == 2:
        received = edge_columns(packed, HALO)
        packed = two_core_window(gather_axis(packed, "hgt", 1), received, HALO)
    else:
        packed = chip_window(gather_axis(packed, "hgt", 1), HALO)
    widths = (HALO, HALO - 1, 2 * STEPS, 2 * STEPS)
    density, grain_label, observed, measured = [
        f[..., HALO - w : f.shape[-1] - (HALO - w)]
        for f, w in zip(azim_exchange(list(packed), widths), widths)
    ]
    grains = (
        grain_label[None] == jnp.arange(GRAINS, dtype=jnp.float32)[:, None, None, None]
    ).astype(jnp.float32)
    d_width, g_width = widths[0], widths[1]
    density = in_domain(density, d_width, geometry)
    grains = in_domain(grains, g_width, geometry)
    history = []
    for moment in range(STEPS):
        history.append((density, d_width, grains, g_width))
        both = min(d_width, g_width)
        bulk_drive, grain_drive = chemical(crop(density, d_width, both), crop(grains, g_width, both))
        pot_width = min(d_width - 1, both)
        potential = crop(bulk_drive, both, pot_width) - cahn_gradient * crop(
            laplace(density, d_width, geometry, False), d_width - 1, pot_width
        )
        new_d_width = pot_width - 1
        flux_term = laplace(potential, pot_width, geometry, False)
        new_density = crop(density, d_width, new_d_width) + cahn_step * flux_term
        if moment + 1 < STEPS:
            new_g_width = min(g_width - 1, both)
            grain_spread = crop(laplace(grains, g_width, geometry, False), g_width - 1, new_g_width)
            new_grains = crop(grains, g_width, new_g_width) - allen_step * (
                crop(grain_drive, both, new_g_width) - allen_gradient * grain_spread
            )
            grains, g_width = in_domain(new_grains, new_g_width, geometry), new_g_width
        density, d_width = in_domain(new_density, new_d_width, geometry), new_d_width

    observed = crop(observed, widths[2], d_width)
    measured = crop(measured, widths[3], d_width)
    costate = in_domain(measured * (density - observed), d_width, geometry)
    c_width = d_width
    last_density = crop(density, d_width, 0)
    cograins = jnp.zeros((GRAINS,) + costate.shape, jnp.float32)
    cg_width = c_width
    for moment in range(STEPS - 1, -1, -1):
        fields_density, fd_width, fields_grains, fg_width = history[moment]
        copotential = cahn_step * laplace(costate, c_width, geometry, True)
        nu_width = c_width - 1
        grain_spread = laplace(cograins, cg_width, geometry, True)
        point = min(nu_width, cg_width, fd_width, fg_width)
        unused, pullback = jax.vjp(
            chemical, crop(fields_density, fd_width, point), crop(fields_grains, fg_width, point)
        )
        pull_density, pull_grains = pullback(
            (crop(copotential, nu_width, point), -allen_step * crop(cograins, cg_width, point))
        )
        reaction = laplace(in_domain(copotential, nu_width, geometry), nu_width, geometry, True)
        new_c_width = nu_width - 1
        new_costate = (
            crop(costate, c_width, new_c_width)
            + crop(pull_density, point, new_c_width)
            - cahn_gradient * reaction
        )
        new_cg_width = min(cg_width - 1, point)
        new_cograins = (
            crop(cograins, cg_width, new_cg_width)
            + crop(pull_grains, point, new_cg_width)
            + allen_step * allen_gradient * crop(grain_spread, cg_width - 1, new_cg_width)
        )
        costate, c_width = in_domain(new_costate, new_c_width, geometry), new_c_width
        cograins, cg_width = in_domain(new_cograins, new_cg_width, geometry), new_cg_width

    costate = crop(costate, c_width, 0)
    cograins = crop(cograins, cg_width, 0)
    result = scatter_heights(
        jnp.concatenate([last_density[None], costate[None], cograins], axis=0), height_rows
    )
    return (result[0], result[1], result[2:])


def solution(mesh):
    in_specs = (
        P("hgt", "azim", "rad"),
        P("hgt", "azim", "rad"),
        P("hgt", "azim", "rad"),
        P("hgt", "azim", "rad"),
    )
    out_specs = (P("hgt", "azim", "rad"), P("hgt", "azim", "rad"), P(None, "hgt", "azim", "rad"))
    return jax.shard_map(shards, mesh=mesh, in_specs=in_specs, out_specs=out_specs, check_vma=False)
```

```python
import jax
import jax.numpy as jnp
from jax import lax
from jax.sharding import PartitionSpec as P

STEPS = 3
GRAINS = 4


bulk_weight = 16.0
grain_weight = 1.0
cahn_step = 0.005
allen_step = 0.05
cahn_gradient = 1.0
allen_gradient = 1.0
full_turn = 6.283185307179586

HALO = 4 * STEPS


def halo_exchange(block, axis, dim, width, cyclic):
    peers, length = (lax.axis_size(axis), block.shape[dim])
    up = [(i, (i + 1) % peers) for i in range(peers) if cyclic or i + 1 < peers]
    down = [(j, i) for i, j in up]
    last = lax.slice_in_dim(block, length - width, length, axis=dim)
    leading = lax.slice_in_dim(block, 0, width, axis=dim)
    before = lax.ppermute(last, axis, up)
    after = lax.ppermute(leading, axis, down)
    return jnp.concatenate([before, block, after], axis=dim)


def azim_exchange(fields, widths):
    peers = lax.axis_size("azim")
    up = [(i, (i + 1) % peers) for i in range(peers)]
    down = [(j, i) for i, j in up]
    rows = fields[0].shape[-2]
    last = jnp.concatenate([f[..., rows - w :, :] for f, w in zip(fields, widths)], axis=-2)
    leading = jnp.concatenate([f[..., :w, :] for f, w in zip(fields, widths)], axis=-2)
    before = lax.ppermute(last, "azim", up)
    after = lax.ppermute(leading, "azim", down)
    out, at = [], 0
    for f, w in zip(fields, widths):
        out.append(jnp.concatenate([before[..., at : at + w, :], f, after[..., at : at + w, :]], axis=-2))
        at += w
    return out


def gather_axis(block, axis, dim):
    peers = lax.axis_size(axis)
    if peers == 1:
        return block
    own = lax.axis_index(axis)
    parts = [block]
    for shift in range(1, peers):
        parts.append(lax.ppermute(block, axis, [(i, (i + shift) % peers) for i in range(peers)]))
    stacked = jnp.stack(parts)
    order = (own - jnp.arange(peers, dtype=jnp.int32)) % peers
    ordered = jnp.take(stacked, order, axis=0)
    ordered = jnp.moveaxis(ordered, 0, dim)
    shape = list(block.shape)
    shape[dim] = shape[dim] * peers
    return ordered.reshape(shape)


def chip_window(block, width):
    peers, own, rad_peers = (lax.axis_size("hgt"), lax.axis_index("hgt"), lax.axis_size("rad"))
    cols = block.shape[-1]
    part = cols // peers
    piece = jnp.where(own == 0, block[..., :width], block[..., cols - width :])
    pairs = []
    for r in range(rad_peers - 1):
        pairs.append((r * peers + peers - 1, (r + 1) * peers))
        pairs.append(((r + 1) * peers, r * peers + peers - 1))
    received = lax.ppermute(piece, ("rad", "hgt"), pairs)
    padded = jnp.concatenate([received, block, received], axis=-1)
    return lax.dynamic_slice_in_dim(padded, own * part, part + 2 * width, axis=padded.ndim - 1)


def edge_columns(block, width):
    own, rad_peers = (lax.axis_index("hgt"), lax.axis_size("rad"))
    cols = block.shape[-1]
    first, last = (block[..., :width], block[..., cols - width :])
    cross, same = ([], [])
    for r in range(rad_peers - 1):
        cross += [(2 * r + 1, 2 * r + 2), (2 * r + 2, 2 * r + 1)]
        same += [(2 * r, 2 * r + 2), (2 * r + 3, 2 * r + 1)]
    from_cross = lax.ppermute(jnp.where(own == 0, first, last), ("rad", "hgt"), cross)
    from_same = lax.ppermute(jnp.where(own == 0, last, first), ("rad", "hgt"), same)
    return jnp.where(
        own == 0,
        jnp.concatenate([from_same, from_cross], axis=1),
        jnp.concatenate([from_cross, from_same], axis=1),
    )


def two_core_window(block, received, width):
    own = lax.axis_index("hgt")
    part = block.shape[-1] // 2
    padded = jnp.concatenate([received, block, received], axis=-1)
    return lax.dynamic_slice_in_dim(padded, own * part, part + 2 * width, axis=padded.ndim - 1)


def scatter_heights(x, height_rows):
    peers, own = (lax.axis_size("hgt"), lax.axis_index("hgt"))
    parts = []
    for shift in range(peers):
        dest = (own + shift) % peers
        piece = lax.dynamic_slice_in_dim(x, dest * height_rows, height_rows, axis=1)
        if shift:
            piece = lax.ppermute(piece, "hgt", [(i, (i + shift) % peers) for i in range(peers)])
        parts.append(piece)
    stacked = jnp.stack(parts)
    order = (own - jnp.arange(peers, dtype=jnp.int32)) % peers
    ordered = jnp.moveaxis(jnp.take(stacked, order, axis=0), 0, -2)
    shape = ordered.shape
    return ordered.reshape(shape[:-2] + (shape[-2] * shape[-1],))


def crop(x, width, new_width):
    cut = width - new_width
    if cut == 0:
        return x
    return x[..., cut : x.shape[-2] - cut, cut : x.shape[-1] - cut]


def radial_mask(width, geometry):
    rad_start, total_hgt, total_azim, total_rad, cols = geometry
    rad_index = rad_start - width + jnp.arange(cols + 2 * width, dtype=jnp.int32)
    return (rad_index >= 0) & (rad_index < total_rad)


def in_domain(x, width, geometry):
    return jnp.where(radial_mask(width, geometry), x, 0.0)


def laplace(x, width, geometry, transpose):
    rad_start, total_hgt, total_azim, total_rad, cols = geometry
    margin = width - 1
    height_rows = x.shape[-3]
    radius_rows = x.shape[-1] - 2
    rad_index_all = rad_start - margin - 1 + jnp.arange(radius_rows + 2, dtype=jnp.int32)
    radius_all = total_azim / full_turn + rad_index_all.astype(jnp.float32) + 0.5
    rad_index = rad_index_all[1:-1]
    radius = radius_all[1:-1]
    outer_face = (radius + 0.5) * (rad_index < total_rad - 1).astype(jnp.float32)
    inner_face = (radius - 0.5) * (rad_index > 0).astype(jnp.float32)
    hgt_index = jnp.arange(height_rows, dtype=jnp.int32)
    upper_face = (hgt_index < total_hgt - 1).astype(jnp.float32)[:, None, None]
    lower_face = (hgt_index > 0).astype(jnp.float32)[:, None, None]
    leading = x.ndim - 3
    padded = jnp.pad(x, [(0, 0)] * leading + [(1, 1), (0, 0), (0, 0)])
    center = padded[..., 1:-1, 1:-1, 1:-1]
    if transpose:
        scaled = padded[..., 1:-1, 1:-1, :] / radius_all
        radial = outer_face * (scaled[..., 2:] - scaled[..., 1:-1]) - inner_face * (
            scaled[..., 1:-1] - scaled[..., :-2]
        )
    else:
        outward = padded[..., 1:-1, 1:-1, 2:]
        inward = padded[..., 1:-1, 1:-1, :-2]
        radial = (outer_face * (outward - center) - inner_face * (center - inward)) / radius
    arc_length = radius * (full_turn / total_azim)
    azimuthal = (padded[..., 1:-1, 2:, 1:-1] + padded[..., 1:-1, :-2, 1:-1] - 2.0 * center) / (
        arc_length * arc_length
    )
    vertical = upper_face * (padded[..., 2:, 1:-1, 1:-1] - center) + lower_face * (
        padded[..., :-2, 1:-1, 1:-1] - center
    )
    return radial + azimuthal + vertical


def chemical(density, grains):
    square_sum = jnp.sum(grains * grains, axis=0)
    cube_sum = jnp.sum(grains * grains * grains, axis=0)
    bulk_drive = 2.0 * bulk_weight * density * (1.0 - density) * (
        1.0 - 2.0 * density
    ) + grain_weight * (2.0 * density - 6.0 * square_sum + 4.0 * cube_sum)
    grain_drive = (
        12.0
        * grain_weight
        * (grains * (1.0 - density) - grains * grains * (2.0 - density) + grains * square_sum)
    )
    return (bulk_drive, grain_drive)


def chemical_pullback(density, grains, copotential, codrive):
    square_sum = jnp.sum(grains * grains, axis=0)
    grain_square = grains * grains
    drive_slope = 12.0 * grain_weight * (grain_square - grains)
    bulk_slope = 2.0 * bulk_weight * (1.0 - 6.0 * density + 6.0 * density * density) + 2.0 * grain_weight
    if codrive is None:
        return copotential * bulk_slope, copotential * drive_slope
    pull_density = copotential * bulk_slope + jnp.sum(codrive * drive_slope, axis=0)
    coupling = jnp.sum(codrive * grains, axis=0)
    pull_grains = (
        copotential * drive_slope
        + 12.0 * grain_weight * codrive * ((1.0 - density) - 2.0 * grains * (2.0 - density) + square_sum)
        + 24.0 * grain_weight * grains * coupling
    )
    return pull_density, pull_grains


def shards(density, labels, observed, measured):
    height_rows, azim_rows, radius_rows = density.shape
    total_hgt = height_rows * lax.axis_size("hgt")
    part = radius_rows // lax.axis_size("hgt")
    geometry = (
        lax.axis_index("rad") * radius_rows + lax.axis_index("hgt") * part,
        total_hgt,
        azim_rows * lax.axis_size("azim"),
        radius_rows * lax.axis_size("rad"),
        part,
    )
    packed = jnp.stack([density, labels.astype(jnp.float32), observed, measured.astype(jnp.float32)])
    if lax.axis_size("hgt") == 2:
        received = edge_columns(packed, HALO)
        packed = two_core_window(gather_axis(packed, "hgt", 1), received, HALO)
    else:
        packed = chip_window(gather_axis(packed, "hgt", 1), HALO)
    widths = (HALO, HALO - 1, 2 * STEPS, 2 * STEPS)
    density, grain_label, observed, measured = [
        f[..., HALO - w : f.shape[-1] - (HALO - w)]
        for f, w in zip(azim_exchange(list(packed), widths), widths)
    ]
    grains = (
        grain_label[None] == jnp.arange(GRAINS, dtype=jnp.float32)[:, None, None, None]
    ).astype(jnp.float32)
    d_width, g_width = widths[0], widths[1]
    density = in_domain(density, d_width, geometry)
    grains = in_domain(grains, g_width, geometry)
    history = []
    for moment in range(STEPS):
        history.append((density, d_width, grains, g_width))
        both = min(d_width, g_width)
        bulk_drive, grain_drive = chemical(crop(density, d_width, both), crop(grains, g_width, both))
        pot_width = min(d_width - 1, both)
        potential = crop(bulk_drive, both, pot_width) - cahn_gradient * crop(
            laplace(density, d_width, geometry, False), d_width - 1, pot_width
        )
        new_d_width = pot_width - 1
        flux_term = laplace(potential, pot_width, geometry, False)
        new_density = crop(density, d_width, new_d_width) + cahn_step * flux_term
        if moment + 1 < STEPS:
            new_g_width = min(g_width - 1, both)
            grain_spread = crop(laplace(grains, g_width, geometry, False), g_width - 1, new_g_width)
            new_grains = crop(grains, g_width, new_g_width) - allen_step * (
                crop(grain_drive, both, new_g_width) - allen_gradient * grain_spread
            )
            grains, g_width = in_domain(new_grains, new_g_width, geometry), new_g_width
        density, d_width = in_domain(new_density, new_d_width, geometry), new_d_width

    observed = crop(observed, widths[2], d_width)
    measured = crop(measured, widths[3], d_width)
    costate = in_domain(measured * (density - observed), d_width, geometry)
    c_width = d_width
    last_density = crop(density, d_width, 0)
    cograins, cg_width = None, c_width
    for moment in range(STEPS - 1, -1, -1):
        fields_density, fd_width, fields_grains, fg_width = history[moment]
        copotential = cahn_step * laplace(costate, c_width, geometry, True)
        nu_width = c_width - 1
        point = min(nu_width, cg_width, fd_width, fg_width)
        here_density = crop(fields_density, fd_width, point)
        here_grains = crop(fields_grains, fg_width, point)
        here_copotential = crop(copotential, nu_width, point)
        if cograins is None:
            pull_density, pull_grains = chemical_pullback(
                here_density, here_grains, here_copotential, None
            )
        else:
            pull_density, pull_grains = chemical_pullback(
                here_density, here_grains, here_copotential, -allen_step * crop(cograins, cg_width, point)
            )
        reaction = laplace(in_domain(copotential, nu_width, geometry), nu_width, geometry, True)
        new_c_width = nu_width - 1
        new_costate = (
            crop(costate, c_width, new_c_width)
            + crop(pull_density, point, new_c_width)
            - cahn_gradient * reaction
        )
        if cograins is None:
            new_cg_width = point
            new_cograins = pull_grains
        else:
            grain_spread = laplace(cograins, cg_width, geometry, True)
            new_cg_width = min(cg_width - 1, point)
            new_cograins = (
                crop(cograins, cg_width, new_cg_width)
                + crop(pull_grains, point, new_cg_width)
                + allen_step * allen_gradient * crop(grain_spread, cg_width - 1, new_cg_width)
            )
        costate, c_width = in_domain(new_costate, new_c_width, geometry), new_c_width
        cograins, cg_width = in_domain(new_cograins, new_cg_width, geometry), new_cg_width

    costate = crop(costate, c_width, 0)
    cograins = crop(cograins, cg_width, 0)
    result = scatter_heights(
        jnp.concatenate([last_density[None], costate[None], cograins], axis=0), height_rows
    )
    return (result[0], result[1], result[2:])


def solution(mesh):
    in_specs = (
        P("hgt", "azim", "rad"),
        P("hgt", "azim", "rad"),
        P("hgt", "azim", "rad"),
        P("hgt", "azim", "rad"),
    )
    out_specs = (P("hgt", "azim", "rad"), P("hgt", "azim", "rad"), P(None, "hgt", "azim", "rad"))
    return jax.shard_map(shards, mesh=mesh, in_specs=in_specs, out_specs=out_specs, check_vma=False)
```

```python
import jax
import jax.numpy as jnp
from jax import lax
from jax.sharding import PartitionSpec as P

STEPS = 3
GRAINS = 4


bulk_weight = 16.0
grain_weight = 1.0
cahn_step = 0.005
allen_step = 0.05
cahn_gradient = 1.0
allen_gradient = 1.0
full_turn = 6.283185307179586

HALO = 4 * STEPS


def halo_exchange(block, axis, dim, width, cyclic):
    peers, length = (lax.axis_size(axis), block.shape[dim])
    up = [(i, (i + 1) % peers) for i in range(peers) if cyclic or i + 1 < peers]
    down = [(j, i) for i, j in up]
    last = lax.slice_in_dim(block, length - width, length, axis=dim)
    leading = lax.slice_in_dim(block, 0, width, axis=dim)
    before = lax.ppermute(last, axis, up)
    after = lax.ppermute(leading, axis, down)
    return jnp.concatenate([before, block, after], axis=dim)


def azim_exchange(fields, widths):
    peers = lax.axis_size("azim")
    up = [(i, (i + 1) % peers) for i in range(peers)]
    down = [(j, i) for i, j in up]
    rows = fields[0].shape[-2]
    last = jnp.concatenate([f[..., rows - w :, :] for f, w in zip(fields, widths)], axis=-2)
    leading = jnp.concatenate([f[..., :w, :] for f, w in zip(fields, widths)], axis=-2)
    before = lax.ppermute(last, "azim", up)
    after = lax.ppermute(leading, "azim", down)
    out, at = [], 0
    for f, w in zip(fields, widths):
        out.append(jnp.concatenate([before[..., at : at + w, :], f, after[..., at : at + w, :]], axis=-2))
        at += w
    return out


def gather_axis(block, axis, dim):
    peers = lax.axis_size(axis)
    if peers == 1:
        return block
    own = lax.axis_index(axis)
    parts = [block]
    for shift in range(1, peers):
        parts.append(lax.ppermute(block, axis, [(i, (i + shift) % peers) for i in range(peers)]))
    stacked = jnp.stack(parts)
    order = (own - jnp.arange(peers, dtype=jnp.int32)) % peers
    ordered = jnp.take(stacked, order, axis=0)
    ordered = jnp.moveaxis(ordered, 0, dim)
    shape = list(block.shape)
    shape[dim] = shape[dim] * peers
    return ordered.reshape(shape)


def chip_window(block, width):
    peers, own, rad_peers = (lax.axis_size("hgt"), lax.axis_index("hgt"), lax.axis_size("rad"))
    cols = block.shape[-1]
    part = cols // peers
    piece = jnp.where(own == 0, block[..., :width], block[..., cols - width :])
    pairs = []
    for r in range(rad_peers - 1):
        pairs.append((r * peers + peers - 1, (r + 1) * peers))
        pairs.append(((r + 1) * peers, r * peers + peers - 1))
    received = lax.ppermute(piece, ("rad", "hgt"), pairs)
    padded = jnp.concatenate([received, block, received], axis=-1)
    return lax.dynamic_slice_in_dim(padded, own * part, part + 2 * width, axis=padded.ndim - 1)


def edge_columns(block, width):
    own, rad_peers = (lax.axis_index("hgt"), lax.axis_size("rad"))
    cols = block.shape[-1]
    first, last = (block[..., :width], block[..., cols - width :])
    cross, same = ([], [])
    for r in range(rad_peers - 1):
        cross += [(2 * r + 1, 2 * r + 2), (2 * r + 2, 2 * r + 1)]
        same += [(2 * r, 2 * r + 2), (2 * r + 3, 2 * r + 1)]
    from_cross = lax.ppermute(jnp.where(own == 0, first, last), ("rad", "hgt"), cross)
    from_same = lax.ppermute(jnp.where(own == 0, last, first), ("rad", "hgt"), same)
    return jnp.where(
        own == 0,
        jnp.concatenate([from_same, from_cross], axis=1),
        jnp.concatenate([from_cross, from_same], axis=1),
    )


def two_core_window(block, received, width):
    own = lax.axis_index("hgt")
    part = block.shape[-1] // 2
    padded = jnp.concatenate([received, block, received], axis=-1)
    return lax.dynamic_slice_in_dim(padded, own * part, part + 2 * width, axis=padded.ndim - 1)


def scatter_heights(x, height_rows):
    peers, own = (lax.axis_size("hgt"), lax.axis_index("hgt"))
    parts = []
    for shift in range(peers):
        dest = (own + shift) % peers
        piece = lax.dynamic_slice_in_dim(x, dest * height_rows, height_rows, axis=1)
        if shift:
            piece = lax.ppermute(piece, "hgt", [(i, (i + shift) % peers) for i in range(peers)])
        parts.append(piece)
    stacked = jnp.stack(parts)
    order = (own - jnp.arange(peers, dtype=jnp.int32)) % peers
    ordered = jnp.moveaxis(jnp.take(stacked, order, axis=0), 0, -2)
    shape = ordered.shape
    return ordered.reshape(shape[:-2] + (shape[-2] * shape[-1],))


def crop(x, width, new_width):
    cut = width - new_width
    if cut == 0:
        return x
    return x[..., cut : x.shape[-2] - cut, cut : x.shape[-1] - cut]


def radial_mask(width, geometry):
    rad_start, total_hgt, total_azim, total_rad, cols = geometry
    rad_index = rad_start - width + jnp.arange(cols + 2 * width, dtype=jnp.int32)
    return (rad_index >= 0) & (rad_index < total_rad)


def in_domain(x, width, geometry):
    return jnp.where(radial_mask(width, geometry), x, 0.0)


def laplace(x, width, geometry, transpose):
    rad_start, total_hgt, total_azim, total_rad, cols = geometry
    margin = width - 1
    height_rows = x.shape[-3]
    radius_rows = x.shape[-1] - 2
    rad_index_all = rad_start - margin - 1 + jnp.arange(radius_rows + 2, dtype=jnp.int32)
    radius_all = total_azim / full_turn + rad_index_all.astype(jnp.float32) + 0.5
    rad_index = rad_index_all[1:-1]
    radius = radius_all[1:-1]
    outer_face = (radius + 0.5) * (rad_index < total_rad - 1).astype(jnp.float32)
    inner_face = (radius - 0.5) * (rad_index > 0).astype(jnp.float32)
    hgt_index = jnp.arange(height_rows, dtype=jnp.int32)
    upper_face = (hgt_index < total_hgt - 1).astype(jnp.float32)[:, None, None]
    lower_face = (hgt_index > 0).astype(jnp.float32)[:, None, None]
    leading = x.ndim - 3
    padded = jnp.pad(x, [(0, 0)] * leading + [(1, 1), (0, 0), (0, 0)])
    center = padded[..., 1:-1, 1:-1, 1:-1]
    if transpose:
        scaled = padded[..., 1:-1, 1:-1, :] / radius_all
        radial = outer_face * (scaled[..., 2:] - scaled[..., 1:-1]) - inner_face * (
            scaled[..., 1:-1] - scaled[..., :-2]
        )
    else:
        outward = padded[..., 1:-1, 1:-1, 2:]
        inward = padded[..., 1:-1, 1:-1, :-2]
        radial = (outer_face * (outward - center) - inner_face * (center - inward)) / radius
    arc_length = radius * (full_turn / total_azim)
    azimuthal = (padded[..., 1:-1, 2:, 1:-1] + padded[..., 1:-1, :-2, 1:-1] - 2.0 * center) / (
        arc_length * arc_length
    )
    vertical = upper_face * (padded[..., 2:, 1:-1, 1:-1] - center) + lower_face * (
        padded[..., :-2, 1:-1, 1:-1] - center
    )
    return radial + azimuthal + vertical


def chemical(density, grains):
    square_sum = jnp.sum(grains * grains, axis=0)
    cube_sum = jnp.sum(grains * grains * grains, axis=0)
    bulk_drive = 2.0 * bulk_weight * density * (1.0 - density) * (
        1.0 - 2.0 * density
    ) + grain_weight * (2.0 * density - 6.0 * square_sum + 4.0 * cube_sum)
    grain_drive = (
        12.0
        * grain_weight
        * (grains * (1.0 - density) - grains * grains * (2.0 - density) + grains * square_sum)
    )
    return (bulk_drive, grain_drive)


def reach():
    need_lc, need_lg = [0], [0]
    for moment in range(STEPS):
        need_lc.append(need_lc[-1] + 2)
        need_lg.append(max(need_lg[-1] + 1, need_lc[moment]))
    need_d, need_e = [need_lc[STEPS]], [-1]
    for moment in range(STEPS - 1, -1, -1):
        pot_width = need_d[0] + 1
        need_d.insert(0, max(pot_width + 1, need_e[0], need_lc[moment]))
        need_e.insert(0, max(pot_width, need_e[0] + 1, need_lc[moment]))
    return need_d, need_e, need_lc, need_lg


def chemical_pullback(density, grains, copotential, codrive):
    square_sum = jnp.sum(grains * grains, axis=0)
    grain_square = grains * grains
    drive_slope = 12.0 * grain_weight * (grain_square - grains)
    bulk_slope = 2.0 * bulk_weight * (1.0 - 6.0 * density + 6.0 * density * density) + 2.0 * grain_weight
    if codrive is None:
        return copotential * bulk_slope, copotential * drive_slope
    pull_density = copotential * bulk_slope + jnp.sum(codrive * drive_slope, axis=0)
    coupling = jnp.sum(codrive * grains, axis=0)
    pull_grains = (
        copotential * drive_slope
        + 12.0 * grain_weight * codrive * ((1.0 - density) - 2.0 * grains * (2.0 - density) + square_sum)
        + 24.0 * grain_weight * grains * coupling
    )
    return pull_density, pull_grains


def shards(density, labels, observed, measured):
    height_rows, azim_rows, radius_rows = density.shape
    total_hgt = height_rows * lax.axis_size("hgt")
    part = radius_rows // lax.axis_size("hgt")
    geometry = (
        lax.axis_index("rad") * radius_rows + lax.axis_index("hgt") * part,
        total_hgt,
        azim_rows * lax.axis_size("azim"),
        radius_rows * lax.axis_size("rad"),
        part,
    )
    packed = jnp.stack([density, labels.astype(jnp.float32), observed, measured.astype(jnp.float32)])
    if lax.axis_size("hgt") == 2:
        received = edge_columns(packed, HALO)
        packed = two_core_window(gather_axis(packed, "hgt", 1), received, HALO)
    else:
        packed = chip_window(gather_axis(packed, "hgt", 1), HALO)
    need_d, need_e, need_lc, need_lg = reach()
    widths = (need_d[0], need_e[0], need_lc[STEPS], need_lc[STEPS])
    density, grain_label, observed, measured = [
        f[..., HALO - w : f.shape[-1] - (HALO - w)]
        for f, w in zip(azim_exchange(list(packed), widths), widths)
    ]
    grains = (
        grain_label[None] == jnp.arange(GRAINS, dtype=jnp.float32)[:, None, None, None]
    ).astype(jnp.float32)
    need_d, need_e, need_lc, need_lg = reach()
    density = in_domain(density, need_d[0], geometry)
    grains = in_domain(grains, need_e[0], geometry)
    history = []
    for moment in range(STEPS):
        d_width, e_width = need_d[moment], need_e[moment]
        history.append((density, d_width, grains, e_width))
        pot_width = need_d[moment + 1] + 1
        next_e = need_e[moment + 1]
        both = max(pot_width, next_e)
        bulk_drive, grain_drive = chemical(crop(density, d_width, both), crop(grains, e_width, both))
        potential = crop(bulk_drive, both, pot_width) - cahn_gradient * laplace(
            crop(density, d_width, pot_width + 1), pot_width + 1, geometry, False
        )
        flux_term = laplace(potential, pot_width, geometry, False)
        new_density = crop(density, d_width, need_d[moment + 1]) + cahn_step * flux_term
        if next_e >= 0:
            grain_spread = laplace(crop(grains, e_width, next_e + 1), next_e + 1, geometry, False)
            new_grains = crop(grains, e_width, next_e) - allen_step * (
                crop(grain_drive, both, next_e) - allen_gradient * grain_spread
            )
            grains = in_domain(new_grains, next_e, geometry)
        density = in_domain(new_density, need_d[moment + 1], geometry)
    d_width = need_d[STEPS]

    observed = crop(observed, widths[2], d_width)
    measured = crop(measured, widths[3], d_width)
    costate = in_domain(measured * (density - observed), d_width, geometry)
    c_width = d_width
    last_density = crop(density, d_width, 0)
    cograins, cg_width = None, None
    for moment in range(STEPS - 1, -1, -1):
        fields_density, fd_width, fields_grains, fg_width = history[moment]
        point = need_lc[moment]
        nu_width = point + 1
        copotential = cahn_step * laplace(crop(costate, c_width, nu_width + 1), nu_width + 1, geometry, True)
        here_density = crop(fields_density, fd_width, point)
        here_grains = crop(fields_grains, fg_width, point)
        here_copotential = crop(copotential, nu_width, point)
        if cograins is None:
            pull_density, pull_grains = chemical_pullback(
                here_density, here_grains, here_copotential, None
            )
        else:
            pull_density, pull_grains = chemical_pullback(
                here_density, here_grains, here_copotential, -allen_step * crop(cograins, cg_width, point)
            )
        reaction = laplace(in_domain(copotential, nu_width, geometry), nu_width, geometry, True)
        new_costate = crop(costate, c_width, point) + pull_density - cahn_gradient * reaction
        new_cg_width = need_lg[moment]
        if cograins is None:
            new_cograins = crop(pull_grains, point, new_cg_width)
        else:
            grain_spread = laplace(
                crop(cograins, cg_width, new_cg_width + 1), new_cg_width + 1, geometry, True
            )
            new_cograins = (
                crop(cograins, cg_width, new_cg_width)
                + crop(pull_grains, point, new_cg_width)
                + allen_step * allen_gradient * grain_spread
            )
        costate, c_width = in_domain(new_costate, point, geometry), point
        cograins, cg_width = in_domain(new_cograins, new_cg_width, geometry), new_cg_width

    costate = crop(costate, c_width, 0)
    cograins = crop(cograins, cg_width, 0)
    result = scatter_heights(
        jnp.concatenate([last_density[None], costate[None], cograins], axis=0), height_rows
    )
    return (result[0], result[1], result[2:])


def solution(mesh):
    in_specs = (
        P("hgt", "azim", "rad"),
        P("hgt", "azim", "rad"),
        P("hgt", "azim", "rad"),
        P("hgt", "azim", "rad"),
    )
    out_specs = (P("hgt", "azim", "rad"), P("hgt", "azim", "rad"), P(None, "hgt", "azim", "rad"))
    return jax.shard_map(shards, mesh=mesh, in_specs=in_specs, out_specs=out_specs, check_vma=False)
```

```python
import jax
import jax.numpy as jnp
from jax import lax
from jax.sharding import PartitionSpec as P

STEPS = 3
GRAINS = 4


bulk_weight = 16.0
grain_weight = 1.0
cahn_step = 0.005
allen_step = 0.05
cahn_gradient = 1.0
allen_gradient = 1.0
full_turn = 6.283185307179586

HALO = 4 * STEPS


def halo_exchange(block, axis, dim, width, cyclic):
    peers, length = (lax.axis_size(axis), block.shape[dim])
    up = [(i, (i + 1) % peers) for i in range(peers) if cyclic or i + 1 < peers]
    down = [(j, i) for i, j in up]
    last = lax.slice_in_dim(block, length - width, length, axis=dim)
    leading = lax.slice_in_dim(block, 0, width, axis=dim)
    before = lax.ppermute(last, axis, up)
    after = lax.ppermute(leading, axis, down)
    return jnp.concatenate([before, block, after], axis=dim)


def azim_exchange(fields, widths):
    peers = lax.axis_size("azim")
    up = [(i, (i + 1) % peers) for i in range(peers)]
    down = [(j, i) for i, j in up]
    rows = fields[0].shape[-2]
    last = jnp.concatenate([f[..., rows - w :, :] for f, w in zip(fields, widths)], axis=-2)
    leading = jnp.concatenate([f[..., :w, :] for f, w in zip(fields, widths)], axis=-2)
    before = lax.ppermute(last, "azim", up)
    after = lax.ppermute(leading, "azim", down)
    out, at = [], 0
    for f, w in zip(fields, widths):
        out.append(jnp.concatenate([before[..., at : at + w, :], f, after[..., at : at + w, :]], axis=-2))
        at += w
    return out


def gather_axis(block, axis, dim):
    peers = lax.axis_size(axis)
    if peers == 1:
        return block
    own = lax.axis_index(axis)
    parts = [block]
    for shift in range(1, peers):
        parts.append(lax.ppermute(block, axis, [(i, (i + shift) % peers) for i in range(peers)]))
    stacked = jnp.stack(parts)
    order = (own - jnp.arange(peers, dtype=jnp.int32)) % peers
    ordered = jnp.take(stacked, order, axis=0)
    ordered = jnp.moveaxis(ordered, 0, dim)
    shape = list(block.shape)
    shape[dim] = shape[dim] * peers
    return ordered.reshape(shape)


def chip_window(block, width):
    peers, own, rad_peers = (lax.axis_size("hgt"), lax.axis_index("hgt"), lax.axis_size("rad"))
    cols = block.shape[-1]
    part = cols // peers
    piece = jnp.where(own == 0, block[..., :width], block[..., cols - width :])
    pairs = []
    for r in range(rad_peers - 1):
        pairs.append((r * peers + peers - 1, (r + 1) * peers))
        pairs.append(((r + 1) * peers, r * peers + peers - 1))
    received = lax.ppermute(piece, ("rad", "hgt"), pairs)
    padded = jnp.concatenate([received, block, received], axis=-1)
    return lax.dynamic_slice_in_dim(padded, own * part, part + 2 * width, axis=padded.ndim - 1)


def edge_columns(block, width):
    own, rad_peers = (lax.axis_index("hgt"), lax.axis_size("rad"))
    cols = block.shape[-1]
    first, last = (block[..., :width], block[..., cols - width :])
    cross, same = ([], [])
    for r in range(rad_peers - 1):
        cross += [(2 * r + 1, 2 * r + 2), (2 * r + 2, 2 * r + 1)]
        same += [(2 * r, 2 * r + 2), (2 * r + 3, 2 * r + 1)]
    from_cross = lax.ppermute(jnp.where(own == 0, first, last), ("rad", "hgt"), cross)
    from_same = lax.ppermute(jnp.where(own == 0, last, first), ("rad", "hgt"), same)
    return jnp.where(
        own == 0,
        jnp.concatenate([from_same, from_cross], axis=1),
        jnp.concatenate([from_cross, from_same], axis=1),
    )


def two_core_window(block, received, width):
    own = lax.axis_index("hgt")
    part = block.shape[-1] // 2
    padded = jnp.concatenate([received, block, received], axis=-1)
    return lax.dynamic_slice_in_dim(padded, own * part, part + 2 * width, axis=padded.ndim - 1)


def scatter_heights(x, height_rows):
    peers, own = (lax.axis_size("hgt"), lax.axis_index("hgt"))
    parts = []
    for shift in range(peers):
        dest = (own + shift) % peers
        piece = lax.dynamic_slice_in_dim(x, dest * height_rows, height_rows, axis=1)
        if shift:
            piece = lax.ppermute(piece, "hgt", [(i, (i + shift) % peers) for i in range(peers)])
        parts.append(piece)
    stacked = jnp.stack(parts)
    order = (own - jnp.arange(peers, dtype=jnp.int32)) % peers
    ordered = jnp.moveaxis(jnp.take(stacked, order, axis=0), 0, -2)
    shape = ordered.shape
    return ordered.reshape(shape[:-2] + (shape[-2] * shape[-1],))


def crop(x, width, new_width):
    cut = width - new_width
    if cut == 0:
        return x
    return x[..., cut : x.shape[-2] - cut, cut : x.shape[-1] - cut]


def radial_mask(width, geometry):
    rad_start, total_hgt, total_azim, total_rad, cols = geometry
    rad_index = rad_start - width + jnp.arange(cols + 2 * width, dtype=jnp.int32)
    return (rad_index >= 0) & (rad_index < total_rad)


def in_domain(x, width, geometry):
    return jnp.where(radial_mask(width, geometry), x, 0.0)


def laplace(x, width, geometry, transpose):
    rad_start, total_hgt, total_azim, total_rad, cols = geometry
    margin = width - 1
    height_rows = x.shape[-3]
    radius_rows = x.shape[-1] - 2
    rad_index_all = rad_start - margin - 1 + jnp.arange(radius_rows + 2, dtype=jnp.int32)
    radius_all = total_azim / full_turn + rad_index_all.astype(jnp.float32) + 0.5
    rad_index = rad_index_all[1:-1]
    radius = radius_all[1:-1]
    outer_face = (radius + 0.5) * (rad_index < total_rad - 1).astype(jnp.float32)
    inner_face = (radius - 0.5) * (rad_index > 0).astype(jnp.float32)
    hgt_index = jnp.arange(height_rows, dtype=jnp.int32)
    upper_face = (hgt_index < total_hgt - 1).astype(jnp.float32)[:, None, None]
    lower_face = (hgt_index > 0).astype(jnp.float32)[:, None, None]
    leading = x.ndim - 3
    padded = jnp.pad(x, [(0, 0)] * leading + [(1, 1), (0, 0), (0, 0)])
    center = padded[..., 1:-1, 1:-1, 1:-1]
    if transpose:
        scaled = padded[..., 1:-1, 1:-1, :] / radius_all
        radial = outer_face * (scaled[..., 2:] - scaled[..., 1:-1]) - inner_face * (
            scaled[..., 1:-1] - scaled[..., :-2]
        )
    else:
        outward = padded[..., 1:-1, 1:-1, 2:]
        inward = padded[..., 1:-1, 1:-1, :-2]
        radial = (outer_face * (outward - center) - inner_face * (center - inward)) / radius
    arc_length = radius * (full_turn / total_azim)
    azimuthal = (padded[..., 1:-1, 2:, 1:-1] + padded[..., 1:-1, :-2, 1:-1] - 2.0 * center) / (
        arc_length * arc_length
    )
    vertical = upper_face * (padded[..., 2:, 1:-1, 1:-1] - center) + lower_face * (
        padded[..., :-2, 1:-1, 1:-1] - center
    )
    return radial + azimuthal + vertical


def chemical(density, grains):
    square_sum = jnp.sum(grains * grains, axis=0)
    cube_sum = jnp.sum(grains * grains * grains, axis=0)
    bulk_drive = 2.0 * bulk_weight * density * (1.0 - density) * (
        1.0 - 2.0 * density
    ) + grain_weight * (2.0 * density - 6.0 * square_sum + 4.0 * cube_sum)
    grain_drive = (
        12.0
        * grain_weight
        * (grains * (1.0 - density) - grains * grains * (2.0 - density) + grains * square_sum)
    )
    return (bulk_drive, grain_drive)


def reach():
    need_lc, need_lg = [0], [0]
    for moment in range(STEPS):
        need_lc.append(need_lc[-1] + 2)
        need_lg.append(max(need_lg[-1] + 1, need_lc[moment]))
    need_d, need_e = [need_lc[STEPS]], [-1]
    for moment in range(STEPS - 1, -1, -1):
        pot_width = need_d[0] + 1
        need_d.insert(0, max(pot_width + 1, need_e[0], need_lc[moment]))
        need_e.insert(0, max(pot_width, need_e[0] + 1, need_lc[moment]))
    return need_d, need_e, need_lc, need_lg


def chemical_pullback(density, grains, copotential, codrive):
    square_sum = jnp.sum(grains * grains, axis=0)
    grain_square = grains * grains
    drive_slope = 12.0 * grain_weight * (grain_square - grains)
    bulk_slope = 2.0 * bulk_weight * (1.0 - 6.0 * density + 6.0 * density * density) + 2.0 * grain_weight
    if codrive is None:
        return copotential * bulk_slope, copotential * drive_slope
    pull_density = copotential * bulk_slope + jnp.sum(codrive * drive_slope, axis=0)
    coupling = jnp.sum(codrive * grains, axis=0)
    pull_grains = (
        copotential * drive_slope
        + 12.0 * grain_weight * codrive * ((1.0 - density) - 2.0 * grains * (2.0 - density) + square_sum)
        + 24.0 * grain_weight * grains * coupling
    )
    return pull_density, pull_grains


def shards(density, labels, observed, measured):
    height_rows, azim_rows, radius_rows = density.shape
    total_hgt = height_rows * lax.axis_size("hgt")
    part = radius_rows // lax.axis_size("hgt")
    geometry = (
        lax.axis_index("rad") * radius_rows + lax.axis_index("hgt") * part,
        total_hgt,
        azim_rows * lax.axis_size("azim"),
        radius_rows * lax.axis_size("rad"),
        part,
    )
    packed = jnp.stack([density, labels.astype(jnp.float32), observed, measured.astype(jnp.float32)])
    if lax.axis_size("hgt") == 2:
        received = edge_columns(packed, HALO)
        packed = two_core_window(gather_axis(packed, "hgt", 1), received, HALO)
    else:
        packed = chip_window(gather_axis(packed, "hgt", 1), HALO)
    need_d, need_e, need_lc, need_lg = reach()
    widths = (need_d[0], need_e[0], need_lc[STEPS], need_lc[STEPS])
    trim = lambda f, w: f[..., HALO - w : f.shape[-1] - (HALO - w)]
    density, grain_label = [
        trim(f, w) for f, w in zip(azim_exchange([packed[0], packed[1]], widths[:2]), widths[:2])
    ]
    misfit_terms, density = lax.optimization_barrier((packed[2:], density))
    observed, measured = [
        trim(f, w) for f, w in zip(azim_exchange([misfit_terms[0], misfit_terms[1]], widths[2:]), widths[2:])
    ]
    grains = (
        grain_label[None] == jnp.arange(GRAINS, dtype=jnp.float32)[:, None, None, None]
    ).astype(jnp.float32)
    need_d, need_e, need_lc, need_lg = reach()
    density = in_domain(density, need_d[0], geometry)
    grains = in_domain(grains, need_e[0], geometry)
    history = []
    for moment in range(STEPS):
        d_width, e_width = need_d[moment], need_e[moment]
        history.append((density, d_width, grains, e_width))
        pot_width = need_d[moment + 1] + 1
        next_e = need_e[moment + 1]
        both = max(pot_width, next_e)
        bulk_drive, grain_drive = chemical(crop(density, d_width, both), crop(grains, e_width, both))
        potential = crop(bulk_drive, both, pot_width) - cahn_gradient * laplace(
            crop(density, d_width, pot_width + 1), pot_width + 1, geometry, False
        )
        flux_term = laplace(potential, pot_width, geometry, False)
        new_density = crop(density, d_width, need_d[moment + 1]) + cahn_step * flux_term
        if next_e >= 0:
            grain_spread = laplace(crop(grains, e_width, next_e + 1), next_e + 1, geometry, False)
            new_grains = crop(grains, e_width, next_e) - allen_step * (
                crop(grain_drive, both, next_e) - allen_gradient * grain_spread
            )
            grains = in_domain(new_grains, next_e, geometry)
        density = in_domain(new_density, need_d[moment + 1], geometry)
    d_width = need_d[STEPS]

    observed = crop(observed, widths[2], d_width)
    measured = crop(measured, widths[3], d_width)
    costate = in_domain(measured * (density - observed), d_width, geometry)
    c_width = d_width
    last_density = crop(density, d_width, 0)
    cograins, cg_width = None, None
    for moment in range(STEPS - 1, -1, -1):
        fields_density, fd_width, fields_grains, fg_width = history[moment]
        point = need_lc[moment]
        nu_width = point + 1
        copotential = cahn_step * laplace(crop(costate, c_width, nu_width + 1), nu_width + 1, geometry, True)
        here_density = crop(fields_density, fd_width, point)
        here_grains = crop(fields_grains, fg_width, point)
        here_copotential = crop(copotential, nu_width, point)
        if cograins is None:
            pull_density, pull_grains = chemical_pullback(
                here_density, here_grains, here_copotential, None
            )
        else:
            pull_density, pull_grains = chemical_pullback(
                here_density, here_grains, here_copotential, -allen_step * crop(cograins, cg_width, point)
            )
        reaction = laplace(in_domain(copotential, nu_width, geometry), nu_width, geometry, True)
        new_costate = crop(costate, c_width, point) + pull_density - cahn_gradient * reaction
        new_cg_width = need_lg[moment]
        if cograins is None:
            new_cograins = crop(pull_grains, point, new_cg_width)
        else:
            grain_spread = laplace(
                crop(cograins, cg_width, new_cg_width + 1), new_cg_width + 1, geometry, True
            )
            new_cograins = (
                crop(cograins, cg_width, new_cg_width)
                + crop(pull_grains, point, new_cg_width)
                + allen_step * allen_gradient * grain_spread
            )
        costate, c_width = in_domain(new_costate, point, geometry), point
        cograins, cg_width = in_domain(new_cograins, new_cg_width, geometry), new_cg_width

    costate = crop(costate, c_width, 0)
    cograins = crop(cograins, cg_width, 0)
    result = scatter_heights(
        jnp.concatenate([last_density[None], costate[None], cograins], axis=0), height_rows
    )
    return (result[0], result[1], result[2:])


def solution(mesh):
    in_specs = (
        P("hgt", "azim", "rad"),
        P("hgt", "azim", "rad"),
        P("hgt", "azim", "rad"),
        P("hgt", "azim", "rad"),
    )
    out_specs = (P("hgt", "azim", "rad"), P("hgt", "azim", "rad"), P(None, "hgt", "azim", "rad"))
    return jax.shard_map(shards, mesh=mesh, in_specs=in_specs, out_specs=out_specs, check_vma=False)
```

```python
import jax
import jax.numpy as jnp
from jax import lax
from jax.sharding import PartitionSpec as P

STEPS = 3
GRAINS = 4


bulk_weight = 16.0
grain_weight = 1.0
cahn_step = 0.005
allen_step = 0.05
cahn_gradient = 1.0
allen_gradient = 1.0
full_turn = 6.283185307179586

HALO = 4 * STEPS


def halo_exchange(block, axis, dim, width, cyclic):
    peers, length = (lax.axis_size(axis), block.shape[dim])
    up = [(i, (i + 1) % peers) for i in range(peers) if cyclic or i + 1 < peers]
    down = [(j, i) for i, j in up]
    last = lax.slice_in_dim(block, length - width, length, axis=dim)
    leading = lax.slice_in_dim(block, 0, width, axis=dim)
    before = lax.ppermute(last, axis, up)
    after = lax.ppermute(leading, axis, down)
    return jnp.concatenate([before, block, after], axis=dim)


def azim_exchange(fields, widths):
    peers = lax.axis_size("azim")
    up = [(i, (i + 1) % peers) for i in range(peers)]
    down = [(j, i) for i, j in up]
    rows = fields[0].shape[-2]
    last = jnp.concatenate([f[..., rows - w :, :] for f, w in zip(fields, widths)], axis=-2)
    leading = jnp.concatenate([f[..., :w, :] for f, w in zip(fields, widths)], axis=-2)
    before = lax.ppermute(last, "azim", up)
    after = lax.ppermute(leading, "azim", down)
    out, at = [], 0
    for f, w in zip(fields, widths):
        out.append(jnp.concatenate([before[..., at : at + w, :], f, after[..., at : at + w, :]], axis=-2))
        at += w
    return out


def gather_axis(block, axis, dim):
    peers = lax.axis_size(axis)
    if peers == 1:
        return block
    own = lax.axis_index(axis)
    parts = [block]
    for shift in range(1, peers):
        parts.append(lax.ppermute(block, axis, [(i, (i + shift) % peers) for i in range(peers)]))
    stacked = jnp.stack(parts)
    order = (own - jnp.arange(peers, dtype=jnp.int32)) % peers
    ordered = jnp.take(stacked, order, axis=0)
    ordered = jnp.moveaxis(ordered, 0, dim)
    shape = list(block.shape)
    shape[dim] = shape[dim] * peers
    return ordered.reshape(shape)


def chip_window(block, width):
    peers, own, rad_peers = (lax.axis_size("hgt"), lax.axis_index("hgt"), lax.axis_size("rad"))
    cols = block.shape[-1]
    part = cols // peers
    piece = jnp.where(own == 0, block[..., :width], block[..., cols - width :])
    pairs = []
    for r in range(rad_peers - 1):
        pairs.append((r * peers + peers - 1, (r + 1) * peers))
        pairs.append(((r + 1) * peers, r * peers + peers - 1))
    received = lax.ppermute(piece, ("rad", "hgt"), pairs)
    padded = jnp.concatenate([received, block, received], axis=-1)
    return lax.dynamic_slice_in_dim(padded, own * part, part + 2 * width, axis=padded.ndim - 1)


def edge_columns(block, width):
    own, rad_peers = (lax.axis_index("hgt"), lax.axis_size("rad"))
    cols = block.shape[-1]
    first, last = (block[..., :width], block[..., cols - width :])
    cross, same = ([], [])
    for r in range(rad_peers - 1):
        cross += [(2 * r + 1, 2 * r + 2), (2 * r + 2, 2 * r + 1)]
        same += [(2 * r, 2 * r + 2), (2 * r + 3, 2 * r + 1)]
    from_cross = lax.ppermute(jnp.where(own == 0, first, last), ("rad", "hgt"), cross)
    from_same = lax.ppermute(jnp.where(own == 0, last, first), ("rad", "hgt"), same)
    return jnp.where(
        own == 0,
        jnp.concatenate([from_same, from_cross], axis=1),
        jnp.concatenate([from_cross, from_same], axis=1),
    )


def two_core_window(block, received, width):
    own = lax.axis_index("hgt")
    part = block.shape[-1] // 2
    padded = jnp.concatenate([received, block, received], axis=-1)
    return lax.dynamic_slice_in_dim(padded, own * part, part + 2 * width, axis=padded.ndim - 1)


def scatter_heights(x, height_rows):
    peers, own = (lax.axis_size("hgt"), lax.axis_index("hgt"))
    parts = []
    for shift in range(peers):
        dest = (own + shift) % peers
        piece = lax.dynamic_slice_in_dim(x, dest * height_rows, height_rows, axis=1)
        if shift:
            piece = lax.ppermute(piece, "hgt", [(i, (i + shift) % peers) for i in range(peers)])
        parts.append(piece)
    stacked = jnp.stack(parts)
    order = (own - jnp.arange(peers, dtype=jnp.int32)) % peers
    ordered = jnp.moveaxis(jnp.take(stacked, order, axis=0), 0, -2)
    shape = ordered.shape
    return ordered.reshape(shape[:-2] + (shape[-2] * shape[-1],))


def crop(x, width, new_width):
    cut = width - new_width
    if cut == 0:
        return x
    return x[..., cut : x.shape[-2] - cut, cut : x.shape[-1] - cut]


def radial_mask(width, geometry):
    rad_start, total_hgt, total_azim, total_rad, cols = geometry
    rad_index = rad_start - width + jnp.arange(cols + 2 * width, dtype=jnp.int32)
    return (rad_index >= 0) & (rad_index < total_rad)


def in_domain(x, width, geometry):
    return jnp.where(radial_mask(width, geometry), x, 0.0)


def laplace(x, width, geometry, transpose):
    rad_start, total_hgt, total_azim, total_rad, cols = geometry
    margin = width - 1
    height_rows = x.shape[-3]
    radius_rows = x.shape[-1] - 2
    rad_index_all = rad_start - margin - 1 + jnp.arange(radius_rows + 2, dtype=jnp.int32)
    radius_all = total_azim / full_turn + rad_index_all.astype(jnp.float32) + 0.5
    rad_index = rad_index_all[1:-1]
    radius = radius_all[1:-1]
    outer_face = (radius + 0.5) * (rad_index < total_rad - 1).astype(jnp.float32)
    inner_face = (radius - 0.5) * (rad_index > 0).astype(jnp.float32)
    if transpose:
        outward_weight = outer_face / radius_all[2:]
        inward_weight = inner_face / radius_all[:-2]
    else:
        outward_weight = outer_face / radius
        inward_weight = inner_face / radius
    arc_length = radius * (full_turn / total_azim)
    arc_weight = 1.0 / (arc_length * arc_length)
    hgt_index = jnp.arange(height_rows, dtype=jnp.int32)
    faces = (hgt_index < total_hgt - 1).astype(jnp.float32) + (hgt_index > 0).astype(jnp.float32)
    center_weight = (outer_face + inner_face) / radius + 2.0 * arc_weight + faces[:, None, None]
    leading = x.ndim - 3
    padded = jnp.pad(x, [(0, 0)] * leading + [(1, 1), (0, 0), (0, 0)])
    center = padded[..., 1:-1, 1:-1, 1:-1]
    radial = outward_weight * padded[..., 1:-1, 1:-1, 2:] + inward_weight * padded[..., 1:-1, 1:-1, :-2]
    azimuthal = arc_weight * (padded[..., 1:-1, 2:, 1:-1] + padded[..., 1:-1, :-2, 1:-1])
    vertical = padded[..., 2:, 1:-1, 1:-1] + padded[..., :-2, 1:-1, 1:-1]
    return radial + azimuthal + vertical - center_weight * center


def chemical(density, grains):
    square_sum = jnp.sum(grains * grains, axis=0)
    cube_sum = jnp.sum(grains * grains * grains, axis=0)
    bulk_drive = 2.0 * bulk_weight * density * (1.0 - density) * (
        1.0 - 2.0 * density
    ) + grain_weight * (2.0 * density - 6.0 * square_sum + 4.0 * cube_sum)
    grain_drive = (
        12.0
        * grain_weight
        * (grains * (1.0 - density) - grains * grains * (2.0 - density) + grains * square_sum)
    )
    return (bulk_drive, grain_drive)


def reach():
    need_lc, need_lg = [0], [0]
    for moment in range(STEPS):
        need_lc.append(need_lc[-1] + 2)
        need_lg.append(max(need_lg[-1] + 1, need_lc[moment]))
    need_d, need_e = [need_lc[STEPS]], [-1]
    for moment in range(STEPS - 1, -1, -1):
        pot_width = need_d[0] + 1
        need_d.insert(0, max(pot_width + 1, need_e[0], need_lc[moment]))
        need_e.insert(0, max(pot_width, need_e[0] + 1, need_lc[moment]))
    return need_d, need_e, need_lc, need_lg


def chemical_pullback(density, grains, copotential, codrive):
    square_sum = jnp.sum(grains * grains, axis=0)
    grain_square = grains * grains
    drive_slope = 12.0 * grain_weight * (grain_square - grains)
    bulk_slope = 2.0 * bulk_weight * (1.0 - 6.0 * density + 6.0 * density * density) + 2.0 * grain_weight
    if codrive is None:
        return copotential * bulk_slope, copotential * drive_slope
    pull_density = copotential * bulk_slope + jnp.sum(codrive * drive_slope, axis=0)
    coupling = jnp.sum(codrive * grains, axis=0)
    pull_grains = (
        copotential * drive_slope
        + 12.0 * grain_weight * codrive * ((1.0 - density) - 2.0 * grains * (2.0 - density) + square_sum)
        + 24.0 * grain_weight * grains * coupling
    )
    return pull_density, pull_grains


def shards(density, labels, observed, measured):
    height_rows, azim_rows, radius_rows = density.shape
    total_hgt = height_rows * lax.axis_size("hgt")
    part = radius_rows // lax.axis_size("hgt")
    geometry = (
        lax.axis_index("rad") * radius_rows + lax.axis_index("hgt") * part,
        total_hgt,
        azim_rows * lax.axis_size("azim"),
        radius_rows * lax.axis_size("rad"),
        part,
    )
    packed = jnp.stack([density, labels.astype(jnp.float32), observed, measured.astype(jnp.float32)])
    if lax.axis_size("hgt") == 2:
        received = edge_columns(packed, HALO)
        packed = two_core_window(gather_axis(packed, "hgt", 1), received, HALO)
    else:
        packed = chip_window(gather_axis(packed, "hgt", 1), HALO)
    need_d, need_e, need_lc, need_lg = reach()
    widths = (need_d[0], need_e[0], need_lc[STEPS], need_lc[STEPS])
    trim = lambda f, w: f[..., HALO - w : f.shape[-1] - (HALO - w)]
    density, grain_label = [
        trim(f, w) for f, w in zip(azim_exchange([packed[0], packed[1]], widths[:2]), widths[:2])
    ]
    misfit_terms, density = lax.optimization_barrier((packed[2:], density))
    observed, measured = [
        trim(f, w) for f, w in zip(azim_exchange([misfit_terms[0], misfit_terms[1]], widths[2:]), widths[2:])
    ]
    grains = (
        grain_label[None] == jnp.arange(GRAINS, dtype=jnp.float32)[:, None, None, None]
    ).astype(jnp.float32)
    need_d, need_e, need_lc, need_lg = reach()
    density = in_domain(density, need_d[0], geometry)
    grains = in_domain(grains, need_e[0], geometry)
    history = []
    for moment in range(STEPS):
        d_width, e_width = need_d[moment], need_e[moment]
        history.append((density, d_width, grains, e_width))
        pot_width = need_d[moment + 1] + 1
        next_e = need_e[moment + 1]
        both = max(pot_width, next_e)
        bulk_drive, grain_drive = chemical(crop(density, d_width, both), crop(grains, e_width, both))
        potential = crop(bulk_drive, both, pot_width) - cahn_gradient * laplace(
            crop(density, d_width, pot_width + 1), pot_width + 1, geometry, False
        )
        flux_term = laplace(potential, pot_width, geometry, False)
        new_density = crop(density, d_width, need_d[moment + 1]) + cahn_step * flux_term
        if next_e >= 0:
            grain_spread = laplace(crop(grains, e_width, next_e + 1), next_e + 1, geometry, False)
            new_grains = crop(grains, e_width, next_e) - allen_step * (
                crop(grain_drive, both, next_e) - allen_gradient * grain_spread
            )
            grains = in_domain(new_grains, next_e, geometry)
        density = in_domain(new_density, need_d[moment + 1], geometry)
    d_width = need_d[STEPS]

    observed = crop(observed, widths[2], d_width)
    measured = crop(measured, widths[3], d_width)
    costate = in_domain(measured * (density - observed), d_width, geometry)
    c_width = d_width
    last_density = crop(density, d_width, 0)
    cograins, cg_width = None, None
    for moment in range(STEPS - 1, -1, -1):
        fields_density, fd_width, fields_grains, fg_width = history[moment]
        point = need_lc[moment]
        nu_width = point + 1
        copotential = cahn_step * laplace(crop(costate, c_width, nu_width + 1), nu_width + 1, geometry, True)
        here_density = crop(fields_density, fd_width, point)
        here_grains = crop(fields_grains, fg_width, point)
        here_copotential = crop(copotential, nu_width, point)
        if cograins is None:
            pull_density, pull_grains = chemical_pullback(
                here_density, here_grains, here_copotential, None
            )
        else:
            pull_density, pull_grains = chemical_pullback(
                here_density, here_grains, here_copotential, -allen_step * crop(cograins, cg_width, point)
            )
        reaction = laplace(in_domain(copotential, nu_width, geometry), nu_width, geometry, True)
        new_costate = crop(costate, c_width, point) + pull_density - cahn_gradient * reaction
        new_cg_width = need_lg[moment]
        if cograins is None:
            new_cograins = crop(pull_grains, point, new_cg_width)
        else:
            grain_spread = laplace(
                crop(cograins, cg_width, new_cg_width + 1), new_cg_width + 1, geometry, True
            )
            new_cograins = (
                crop(cograins, cg_width, new_cg_width)
                + crop(pull_grains, point, new_cg_width)
                + allen_step * allen_gradient * grain_spread
            )
        costate, c_width = in_domain(new_costate, point, geometry), point
        cograins, cg_width = in_domain(new_cograins, new_cg_width, geometry), new_cg_width

    costate = crop(costate, c_width, 0)
    cograins = crop(cograins, cg_width, 0)
    result = scatter_heights(
        jnp.concatenate([last_density[None], costate[None], cograins], axis=0), height_rows
    )
    return (result[0], result[1], result[2:])


def solution(mesh):
    in_specs = (
        P("hgt", "azim", "rad"),
        P("hgt", "azim", "rad"),
        P("hgt", "azim", "rad"),
        P("hgt", "azim", "rad"),
    )
    out_specs = (P("hgt", "azim", "rad"), P("hgt", "azim", "rad"), P(None, "hgt", "azim", "rad"))
    return jax.shard_map(shards, mesh=mesh, in_specs=in_specs, out_specs=out_specs, check_vma=False)
```

```python
import jax
import jax.numpy as jnp
from jax import lax
from jax.sharding import PartitionSpec as P

STEPS = 3
GRAINS = 4


bulk_weight = 16.0
grain_weight = 1.0
cahn_step = 0.005
allen_step = 0.05
cahn_gradient = 1.0
allen_gradient = 1.0
full_turn = 6.283185307179586

HALO = 4 * STEPS


def halo_exchange(block, axis, dim, width, cyclic):
    peers, length = (lax.axis_size(axis), block.shape[dim])
    up = [(i, (i + 1) % peers) for i in range(peers) if cyclic or i + 1 < peers]
    down = [(j, i) for i, j in up]
    last = lax.slice_in_dim(block, length - width, length, axis=dim)
    leading = lax.slice_in_dim(block, 0, width, axis=dim)
    before = lax.ppermute(last, axis, up)
    after = lax.ppermute(leading, axis, down)
    return jnp.concatenate([before, block, after], axis=dim)


def azim_exchange(fields, widths):
    peers = lax.axis_size("azim")
    up = [(i, (i + 1) % peers) for i in range(peers)]
    down = [(j, i) for i, j in up]
    rows = fields[0].shape[-2]
    last = jnp.concatenate([f[..., rows - w :, :] for f, w in zip(fields, widths)], axis=-2)
    leading = jnp.concatenate([f[..., :w, :] for f, w in zip(fields, widths)], axis=-2)
    before = lax.ppermute(last, "azim", up)
    after = lax.ppermute(leading, "azim", down)
    out, at = [], 0
    for f, w in zip(fields, widths):
        out.append(jnp.concatenate([before[..., at : at + w, :], f, after[..., at : at + w, :]], axis=-2))
        at += w
    return out


def gather_axis(block, axis, dim):
    peers = lax.axis_size(axis)
    if peers == 1:
        return block
    own = lax.axis_index(axis)
    parts = [block]
    for shift in range(1, peers):
        parts.append(lax.ppermute(block, axis, [(i, (i + shift) % peers) for i in range(peers)]))
    if peers == 2:
        return jnp.where(
            own == 0,
            jnp.concatenate([parts[0], parts[1]], axis=dim),
            jnp.concatenate([parts[1], parts[0]], axis=dim),
        )
    stacked = jnp.stack(parts)
    order = (own - jnp.arange(peers, dtype=jnp.int32)) % peers
    ordered = jnp.take(stacked, order, axis=0)
    ordered = jnp.moveaxis(ordered, 0, dim)
    shape = list(block.shape)
    shape[dim] = shape[dim] * peers
    return ordered.reshape(shape)


def chip_window(block, width):
    peers, own, rad_peers = (lax.axis_size("hgt"), lax.axis_index("hgt"), lax.axis_size("rad"))
    cols = block.shape[-1]
    part = cols // peers
    piece = jnp.where(own == 0, block[..., :width], block[..., cols - width :])
    pairs = []
    for r in range(rad_peers - 1):
        pairs.append((r * peers + peers - 1, (r + 1) * peers))
        pairs.append(((r + 1) * peers, r * peers + peers - 1))
    received = lax.ppermute(piece, ("rad", "hgt"), pairs)
    padded = jnp.concatenate([received, block, received], axis=-1)
    return lax.dynamic_slice_in_dim(padded, own * part, part + 2 * width, axis=padded.ndim - 1)


def edge_columns(block, width):
    own, rad_peers = (lax.axis_index("hgt"), lax.axis_size("rad"))
    cols = block.shape[-1]
    first, last = (block[..., :width], block[..., cols - width :])
    cross, same = ([], [])
    for r in range(rad_peers - 1):
        cross += [(2 * r + 1, 2 * r + 2), (2 * r + 2, 2 * r + 1)]
        same += [(2 * r, 2 * r + 2), (2 * r + 3, 2 * r + 1)]
    from_cross = lax.ppermute(jnp.where(own == 0, first, last), ("rad", "hgt"), cross)
    from_same = lax.ppermute(jnp.where(own == 0, last, first), ("rad", "hgt"), same)
    return jnp.where(
        own == 0,
        jnp.concatenate([from_same, from_cross], axis=1),
        jnp.concatenate([from_cross, from_same], axis=1),
    )


def two_core_window(block, received, width):
    own = lax.axis_index("hgt")
    part = block.shape[-1] // 2
    padded = jnp.concatenate([received, block, received], axis=-1)
    return lax.dynamic_slice_in_dim(padded, own * part, part + 2 * width, axis=padded.ndim - 1)


def scatter_heights(x, height_rows):
    peers, own = (lax.axis_size("hgt"), lax.axis_index("hgt"))
    parts = []
    for shift in range(peers):
        dest = (own + shift) % peers
        piece = lax.dynamic_slice_in_dim(x, dest * height_rows, height_rows, axis=1)
        if shift:
            piece = lax.ppermute(piece, "hgt", [(i, (i + shift) % peers) for i in range(peers)])
        parts.append(piece)
    if peers == 2:
        return jnp.where(
            own == 0,
            jnp.concatenate([parts[0], parts[1]], axis=-1),
            jnp.concatenate([parts[1], parts[0]], axis=-1),
        )
    stacked = jnp.stack(parts)
    order = (own - jnp.arange(peers, dtype=jnp.int32)) % peers
    ordered = jnp.moveaxis(jnp.take(stacked, order, axis=0), 0, -2)
    shape = ordered.shape
    return ordered.reshape(shape[:-2] + (shape[-2] * shape[-1],))


def crop(x, width, new_width):
    cut = width - new_width
    if cut == 0:
        return x
    return x[..., cut : x.shape[-2] - cut, cut : x.shape[-1] - cut]


def radial_mask(width, geometry):
    rad_start, total_hgt, total_azim, total_rad, cols = geometry
    rad_index = rad_start - width + jnp.arange(cols + 2 * width, dtype=jnp.int32)
    return (rad_index >= 0) & (rad_index < total_rad)


def in_domain(x, width, geometry):
    return jnp.where(radial_mask(width, geometry), x, 0.0)


def laplace(x, width, geometry, transpose):
    rad_start, total_hgt, total_azim, total_rad, cols = geometry
    margin = width - 1
    height_rows = x.shape[-3]
    radius_rows = x.shape[-1] - 2
    rad_index_all = rad_start - margin - 1 + jnp.arange(radius_rows + 2, dtype=jnp.int32)
    radius_all = total_azim / full_turn + rad_index_all.astype(jnp.float32) + 0.5
    rad_index = rad_index_all[1:-1]
    radius = radius_all[1:-1]
    outer_face = (radius + 0.5) * (rad_index < total_rad - 1).astype(jnp.float32)
    inner_face = (radius - 0.5) * (rad_index > 0).astype(jnp.float32)
    if transpose:
        outward_weight = outer_face / radius_all[2:]
        inward_weight = inner_face / radius_all[:-2]
    else:
        outward_weight = outer_face / radius
        inward_weight = inner_face / radius
    arc_length = radius * (full_turn / total_azim)
    arc_weight = 1.0 / (arc_length * arc_length)
    hgt_index = jnp.arange(height_rows, dtype=jnp.int32)
    faces = (hgt_index < total_hgt - 1).astype(jnp.float32) + (hgt_index > 0).astype(jnp.float32)
    center_weight = (outer_face + inner_face) / radius + 2.0 * arc_weight + faces[:, None, None]
    leading = x.ndim - 3
    padded = jnp.pad(x, [(0, 0)] * leading + [(1, 1), (0, 0), (0, 0)])
    center = padded[..., 1:-1, 1:-1, 1:-1]
    radial = outward_weight * padded[..., 1:-1, 1:-1, 2:] + inward_weight * padded[..., 1:-1, 1:-1, :-2]
    azimuthal = arc_weight * (padded[..., 1:-1, 2:, 1:-1] + padded[..., 1:-1, :-2, 1:-1])
    vertical = padded[..., 2:, 1:-1, 1:-1] + padded[..., :-2, 1:-1, 1:-1]
    return radial + azimuthal + vertical - center_weight * center


def chemical(density, grains):
    square_sum = jnp.sum(grains * grains, axis=0)
    cube_sum = jnp.sum(grains * grains * grains, axis=0)
    bulk_drive = 2.0 * bulk_weight * density * (1.0 - density) * (
        1.0 - 2.0 * density
    ) + grain_weight * (2.0 * density - 6.0 * square_sum + 4.0 * cube_sum)
    grain_drive = (
        12.0
        * grain_weight
        * (grains * (1.0 - density) - grains * grains * (2.0 - density) + grains * square_sum)
    )
    return (bulk_drive, grain_drive)


def reach():
    need_lc, need_lg = [0], [0]
    for moment in range(STEPS):
        need_lc.append(need_lc[-1] + 2)
        need_lg.append(max(need_lg[-1] + 1, need_lc[moment]))
    need_d, need_e = [need_lc[STEPS]], [-1]
    for moment in range(STEPS - 1, -1, -1):
        pot_width = need_d[0] + 1
        need_d.insert(0, max(pot_width + 1, need_e[0], need_lc[moment]))
        need_e.insert(0, max(pot_width, need_e[0] + 1, need_lc[moment]))
    return need_d, need_e, need_lc, need_lg


def chemical_pullback(density, grains, copotential, codrive):
    square_sum = jnp.sum(grains * grains, axis=0)
    grain_square = grains * grains
    drive_slope = 12.0 * grain_weight * (grain_square - grains)
    bulk_slope = 2.0 * bulk_weight * (1.0 - 6.0 * density + 6.0 * density * density) + 2.0 * grain_weight
    if codrive is None:
        return copotential * bulk_slope, copotential * drive_slope
    pull_density = copotential * bulk_slope + jnp.sum(codrive * drive_slope, axis=0)
    coupling = jnp.sum(codrive * grains, axis=0)
    pull_grains = (
        copotential * drive_slope
        + 12.0 * grain_weight * codrive * ((1.0 - density) - 2.0 * grains * (2.0 - density) + square_sum)
        + 24.0 * grain_weight * grains * coupling
    )
    return pull_density, pull_grains


def shards(density, labels, observed, measured):
    height_rows, azim_rows, radius_rows = density.shape
    total_hgt = height_rows * lax.axis_size("hgt")
    part = radius_rows // lax.axis_size("hgt")
    geometry = (
        lax.axis_index("rad") * radius_rows + lax.axis_index("hgt") * part,
        total_hgt,
        azim_rows * lax.axis_size("azim"),
        radius_rows * lax.axis_size("rad"),
        part,
    )
    packed = jnp.stack([density, labels.astype(jnp.float32), observed, measured.astype(jnp.float32)])
    if lax.axis_size("hgt") == 2:
        received = edge_columns(packed, HALO)
        packed = two_core_window(gather_axis(packed, "hgt", 1), received, HALO)
    else:
        packed = chip_window(gather_axis(packed, "hgt", 1), HALO)
    need_d, need_e, need_lc, need_lg = reach()
    widths = (need_d[0], need_e[0], need_lc[STEPS], need_lc[STEPS])
    trim = lambda f, w: f[..., HALO - w : f.shape[-1] - (HALO - w)]
    density, grain_label = [
        trim(f, w) for f, w in zip(azim_exchange([packed[0], packed[1]], widths[:2]), widths[:2])
    ]
    misfit_terms, density = lax.optimization_barrier((packed[2:], density))
    observed, measured = [
        trim(f, w) for f, w in zip(azim_exchange([misfit_terms[0], misfit_terms[1]], widths[2:]), widths[2:])
    ]
    grains = (
        grain_label[None] == jnp.arange(GRAINS, dtype=jnp.float32)[:, None, None, None]
    ).astype(jnp.float32)
    need_d, need_e, need_lc, need_lg = reach()
    density = in_domain(density, need_d[0], geometry)
    grains = in_domain(grains, need_e[0], geometry)
    history = []
    for moment in range(STEPS):
        d_width, e_width = need_d[moment], need_e[moment]
        history.append((density, d_width, grains, e_width))
        pot_width = need_d[moment + 1] + 1
        next_e = need_e[moment + 1]
        both = max(pot_width, next_e)
        bulk_drive, grain_drive = chemical(crop(density, d_width, both), crop(grains, e_width, both))
        potential = crop(bulk_drive, both, pot_width) - cahn_gradient * laplace(
            crop(density, d_width, pot_width + 1), pot_width + 1, geometry, False
        )
        flux_term = laplace(potential, pot_width, geometry, False)
        new_density = crop(density, d_width, need_d[moment + 1]) + cahn_step * flux_term
        if next_e >= 0:
            grain_spread = laplace(crop(grains, e_width, next_e + 1), next_e + 1, geometry, False)
            new_grains = crop(grains, e_width, next_e) - allen_step * (
                crop(grain_drive, both, next_e) - allen_gradient * grain_spread
            )
            grains = in_domain(new_grains, next_e, geometry)
        density = in_domain(new_density, need_d[moment + 1], geometry)
    d_width = need_d[STEPS]

    observed = crop(observed, widths[2], d_width)
    measured = crop(measured, widths[3], d_width)
    costate = in_domain(measured * (density - observed), d_width, geometry)
    c_width = d_width
    last_density = crop(density, d_width, 0)
    cograins, cg_width = None, None
    for moment in range(STEPS - 1, -1, -1):
        fields_density, fd_width, fields_grains, fg_width = history[moment]
        point = need_lc[moment]
        nu_width = point + 1
        copotential = cahn_step * laplace(crop(costate, c_width, nu_width + 1), nu_width + 1, geometry, True)
        here_density = crop(fields_density, fd_width, point)
        here_grains = crop(fields_grains, fg_width, point)
        here_copotential = crop(copotential, nu_width, point)
        if cograins is None:
            pull_density, pull_grains = chemical_pullback(
                here_density, here_grains, here_copotential, None
            )
        else:
            pull_density, pull_grains = chemical_pullback(
                here_density, here_grains, here_copotential, -allen_step * crop(cograins, cg_width, point)
            )
        reaction = laplace(in_domain(copotential, nu_width, geometry), nu_width, geometry, True)
        new_costate = crop(costate, c_width, point) + pull_density - cahn_gradient * reaction
        new_cg_width = need_lg[moment]
        if cograins is None:
            new_cograins = crop(pull_grains, point, new_cg_width)
        else:
            grain_spread = laplace(
                crop(cograins, cg_width, new_cg_width + 1), new_cg_width + 1, geometry, True
            )
            new_cograins = (
                crop(cograins, cg_width, new_cg_width)
                + crop(pull_grains, point, new_cg_width)
                + allen_step * allen_gradient * grain_spread
            )
        costate, c_width = in_domain(new_costate, point, geometry), point
        cograins, cg_width = in_domain(new_cograins, new_cg_width, geometry), new_cg_width

    costate = crop(costate, c_width, 0)
    cograins = crop(cograins, cg_width, 0)
    result = scatter_heights(
        jnp.concatenate([last_density[None], costate[None], cograins], axis=0), height_rows
    )
    return (result[0], result[1], result[2:])


def solution(mesh):
    in_specs = (
        P("hgt", "azim", "rad"),
        P("hgt", "azim", "rad"),
        P("hgt", "azim", "rad"),
        P("hgt", "azim", "rad"),
    )
    out_specs = (P("hgt", "azim", "rad"), P("hgt", "azim", "rad"), P(None, "hgt", "azim", "rad"))
    return jax.shard_map(shards, mesh=mesh, in_specs=in_specs, out_specs=out_specs, check_vma=False)
```

```python
import jax
import jax.numpy as jnp
from jax import lax
from jax.sharding import PartitionSpec as P

STEPS = 3
GRAINS = 4


bulk_weight = 16.0
grain_weight = 1.0
cahn_step = 0.005
allen_step = 0.05
cahn_gradient = 1.0
allen_gradient = 1.0
full_turn = 6.283185307179586

HALO = 4 * STEPS


def halo_exchange(block, axis, dim, width, cyclic):
    peers, length = (lax.axis_size(axis), block.shape[dim])
    up = [(i, (i + 1) % peers) for i in range(peers) if cyclic or i + 1 < peers]
    down = [(j, i) for i, j in up]
    last = lax.slice_in_dim(block, length - width, length, axis=dim)
    leading = lax.slice_in_dim(block, 0, width, axis=dim)
    before = lax.ppermute(last, axis, up)
    after = lax.ppermute(leading, axis, down)
    return jnp.concatenate([before, block, after], axis=dim)


def azim_exchange(fields, widths):
    peers = lax.axis_size("azim")
    up = [(i, (i + 1) % peers) for i in range(peers)]
    down = [(j, i) for i, j in up]
    rows = fields[0].shape[-2]
    last = jnp.concatenate([f[..., rows - w :, :] for f, w in zip(fields, widths)], axis=-2)
    leading = jnp.concatenate([f[..., :w, :] for f, w in zip(fields, widths)], axis=-2)
    before = lax.ppermute(last, "azim", up)
    after = lax.ppermute(leading, "azim", down)
    out, at = [], 0
    for f, w in zip(fields, widths):
        out.append(jnp.concatenate([before[..., at : at + w, :], f, after[..., at : at + w, :]], axis=-2))
        at += w
    return out


def gather_axis(block, axis, dim):
    peers = lax.axis_size(axis)
    if peers == 1:
        return block
    own = lax.axis_index(axis)
    parts = [block]
    for shift in range(1, peers):
        parts.append(lax.ppermute(block, axis, [(i, (i + shift) % peers) for i in range(peers)]))
    if peers == 2:
        return jnp.where(
            own == 0,
            jnp.concatenate([parts[0], parts[1]], axis=dim),
            jnp.concatenate([parts[1], parts[0]], axis=dim),
        )
    stacked = jnp.stack(parts)
    order = (own - jnp.arange(peers, dtype=jnp.int32)) % peers
    ordered = jnp.take(stacked, order, axis=0)
    ordered = jnp.moveaxis(ordered, 0, dim)
    shape = list(block.shape)
    shape[dim] = shape[dim] * peers
    return ordered.reshape(shape)


def chip_window(block, width):
    peers, own, rad_peers = (lax.axis_size("hgt"), lax.axis_index("hgt"), lax.axis_size("rad"))
    cols = block.shape[-1]
    part = cols // peers
    piece = jnp.where(own == 0, block[..., :width], block[..., cols - width :])
    pairs = []
    for r in range(rad_peers - 1):
        pairs.append((r * peers + peers - 1, (r + 1) * peers))
        pairs.append(((r + 1) * peers, r * peers + peers - 1))
    received = lax.ppermute(piece, ("rad", "hgt"), pairs)
    padded = jnp.concatenate([received, block, received], axis=-1)
    return lax.dynamic_slice_in_dim(padded, own * part, part + 2 * width, axis=padded.ndim - 1)


def scatter_heights(x, height_rows):
    peers, own = (lax.axis_size("hgt"), lax.axis_index("hgt"))
    parts = []
    for shift in range(peers):
        dest = (own + shift) % peers
        piece = lax.dynamic_slice_in_dim(x, dest * height_rows, height_rows, axis=1)
        if shift:
            piece = lax.ppermute(piece, "hgt", [(i, (i + shift) % peers) for i in range(peers)])
        parts.append(piece)
    if peers == 2:
        return jnp.where(
            own == 0,
            jnp.concatenate([parts[0], parts[1]], axis=-1),
            jnp.concatenate([parts[1], parts[0]], axis=-1),
        )
    stacked = jnp.stack(parts)
    order = (own - jnp.arange(peers, dtype=jnp.int32)) % peers
    ordered = jnp.moveaxis(jnp.take(stacked, order, axis=0), 0, -2)
    shape = ordered.shape
    return ordered.reshape(shape[:-2] + (shape[-2] * shape[-1],))


def crop(x, width, new_width):
    cut = width - new_width
    if cut == 0:
        return x
    return x[..., cut : x.shape[-2] - cut, cut : x.shape[-1] - cut]


def radial_mask(width, geometry):
    rad_start, total_hgt, total_azim, total_rad, cols = geometry
    rad_index = rad_start - width + jnp.arange(cols + 2 * width, dtype=jnp.int32)
    return (rad_index >= 0) & (rad_index < total_rad)


def in_domain(x, width, geometry):
    return jnp.where(radial_mask(width, geometry), x, 0.0)


def laplace(x, width, geometry, transpose):
    rad_start, total_hgt, total_azim, total_rad, cols = geometry
    margin = width - 1
    height_rows = x.shape[-3]
    radius_rows = x.shape[-1] - 2
    rad_index_all = rad_start - margin - 1 + jnp.arange(radius_rows + 2, dtype=jnp.int32)
    radius_all = total_azim / full_turn + rad_index_all.astype(jnp.float32) + 0.5
    rad_index = rad_index_all[1:-1]
    radius = radius_all[1:-1]
    outer_face = (radius + 0.5) * (rad_index < total_rad - 1).astype(jnp.float32)
    inner_face = (radius - 0.5) * (rad_index > 0).astype(jnp.float32)
    if transpose:
        outward_weight = outer_face / radius_all[2:]
        inward_weight = inner_face / radius_all[:-2]
    else:
        outward_weight = outer_face / radius
        inward_weight = inner_face / radius
    arc_length = radius * (full_turn / total_azim)
    arc_weight = 1.0 / (arc_length * arc_length)
    hgt_index = jnp.arange(height_rows, dtype=jnp.int32)
    faces = (hgt_index < total_hgt - 1).astype(jnp.float32) + (hgt_index > 0).astype(jnp.float32)
    center_weight = (outer_face + inner_face) / radius + 2.0 * arc_weight + faces[:, None, None]
    leading = x.ndim - 3
    padded = jnp.pad(x, [(0, 0)] * leading + [(1, 1), (0, 0), (0, 0)])
    center = padded[..., 1:-1, 1:-1, 1:-1]
    radial = outward_weight * padded[..., 1:-1, 1:-1, 2:] + inward_weight * padded[..., 1:-1, 1:-1, :-2]
    azimuthal = arc_weight * (padded[..., 1:-1, 2:, 1:-1] + padded[..., 1:-1, :-2, 1:-1])
    vertical = padded[..., 2:, 1:-1, 1:-1] + padded[..., :-2, 1:-1, 1:-1]
    return radial + azimuthal + vertical - center_weight * center


def chemical(density, grains):
    square_sum = jnp.sum(grains * grains, axis=0)
    cube_sum = jnp.sum(grains * grains * grains, axis=0)
    bulk_drive = 2.0 * bulk_weight * density * (1.0 - density) * (
        1.0 - 2.0 * density
    ) + grain_weight * (2.0 * density - 6.0 * square_sum + 4.0 * cube_sum)
    grain_drive = (
        12.0
        * grain_weight
        * (grains * (1.0 - density) - grains * grains * (2.0 - density) + grains * square_sum)
    )
    return (bulk_drive, grain_drive)


def reach():
    need_lc, need_lg = [0], [0]
    for moment in range(STEPS):
        need_lc.append(need_lc[-1] + 2)
        need_lg.append(max(need_lg[-1] + 1, need_lc[moment]))
    need_d, need_e = [need_lc[STEPS]], [-1]
    for moment in range(STEPS - 1, -1, -1):
        pot_width = need_d[0] + 1
        need_d.insert(0, max(pot_width + 1, need_e[0], need_lc[moment]))
        need_e.insert(0, max(pot_width, need_e[0] + 1, need_lc[moment]))
    return need_d, need_e, need_lc, need_lg


def chemical_pullback(density, grains, copotential, codrive):
    square_sum = jnp.sum(grains * grains, axis=0)
    grain_square = grains * grains
    drive_slope = 12.0 * grain_weight * (grain_square - grains)
    bulk_slope = 2.0 * bulk_weight * (1.0 - 6.0 * density + 6.0 * density * density) + 2.0 * grain_weight
    if codrive is None:
        return copotential * bulk_slope, copotential * drive_slope
    pull_density = copotential * bulk_slope + jnp.sum(codrive * drive_slope, axis=0)
    coupling = jnp.sum(codrive * grains, axis=0)
    pull_grains = (
        copotential * drive_slope
        + 12.0 * grain_weight * codrive * ((1.0 - density) - 2.0 * grains * (2.0 - density) + square_sum)
        + 24.0 * grain_weight * grains * coupling
    )
    return pull_density, pull_grains


def shards(density, labels, observed, measured):
    height_rows, azim_rows, radius_rows = density.shape
    total_hgt = height_rows * lax.axis_size("hgt")
    part = radius_rows // lax.axis_size("hgt")
    geometry = (
        lax.axis_index("rad") * radius_rows + lax.axis_index("hgt") * part,
        total_hgt,
        azim_rows * lax.axis_size("azim"),
        radius_rows * lax.axis_size("rad"),
        part,
    )
    packed = jnp.stack([density, labels.astype(jnp.float32), observed, measured.astype(jnp.float32)])
    packed = chip_window(gather_axis(packed, "hgt", 1), HALO)
    need_d, need_e, need_lc, need_lg = reach()
    widths = (need_d[0], need_e[0], need_lc[STEPS], need_lc[STEPS])
    trim = lambda f, w: f[..., HALO - w : f.shape[-1] - (HALO - w)]
    density, grain_label = [
        trim(f, w) for f, w in zip(azim_exchange([packed[0], packed[1]], widths[:2]), widths[:2])
    ]
    misfit_terms, density = lax.optimization_barrier((packed[2:], density))
    observed, measured = [
        trim(f, w) for f, w in zip(azim_exchange([misfit_terms[0], misfit_terms[1]], widths[2:]), widths[2:])
    ]
    grains = (
        grain_label[None] == jnp.arange(GRAINS, dtype=jnp.float32)[:, None, None, None]
    ).astype(jnp.float32)
    need_d, need_e, need_lc, need_lg = reach()
    density = in_domain(density, need_d[0], geometry)
    grains = in_domain(grains, need_e[0], geometry)
    history = []
    for moment in range(STEPS):
        d_width, e_width = need_d[moment], need_e[moment]
        history.append((density, d_width, grains, e_width))
        pot_width = need_d[moment + 1] + 1
        next_e = need_e[moment + 1]
        both = max(pot_width, next_e)
        bulk_drive, grain_drive = chemical(crop(density, d_width, both), crop(grains, e_width, both))
        potential = crop(bulk_drive, both, pot_width) - cahn_gradient * laplace(
            crop(density, d_width, pot_width + 1), pot_width + 1, geometry, False
        )
        flux_term = laplace(potential, pot_width, geometry, False)
        new_density = crop(density, d_width, need_d[moment + 1]) + cahn_step * flux_term
        if next_e >= 0:
            grain_spread = laplace(crop(grains, e_width, next_e + 1), next_e + 1, geometry, False)
            new_grains = crop(grains, e_width, next_e) - allen_step * (
                crop(grain_drive, both, next_e) - allen_gradient * grain_spread
            )
            grains = in_domain(new_grains, next_e, geometry)
        density = in_domain(new_density, need_d[moment + 1], geometry)
    d_width = need_d[STEPS]

    observed = crop(observed, widths[2], d_width)
    measured = crop(measured, widths[3], d_width)
    costate = in_domain(measured * (density - observed), d_width, geometry)
    c_width = d_width
    last_density = crop(density, d_width, 0)
    cograins, cg_width = None, None
    for moment in range(STEPS - 1, -1, -1):
        fields_density, fd_width, fields_grains, fg_width = history[moment]
        point = need_lc[moment]
        nu_width = point + 1
        copotential = cahn_step * laplace(crop(costate, c_width, nu_width + 1), nu_width + 1, geometry, True)
        here_density = crop(fields_density, fd_width, point)
        here_grains = crop(fields_grains, fg_width, point)
        here_copotential = crop(copotential, nu_width, point)
        if cograins is None:
            pull_density, pull_grains = chemical_pullback(
                here_density, here_grains, here_copotential, None
            )
        else:
            pull_density, pull_grains = chemical_pullback(
                here_density, here_grains, here_copotential, -allen_step * crop(cograins, cg_width, point)
            )
        reaction = laplace(in_domain(copotential, nu_width, geometry), nu_width, geometry, True)
        new_costate = crop(costate, c_width, point) + pull_density - cahn_gradient * reaction
        new_cg_width = need_lg[moment]
        if cograins is None:
            new_cograins = crop(pull_grains, point, new_cg_width)
        else:
            grain_spread = laplace(
                crop(cograins, cg_width, new_cg_width + 1), new_cg_width + 1, geometry, True
            )
            new_cograins = (
                crop(cograins, cg_width, new_cg_width)
                + crop(pull_grains, point, new_cg_width)
                + allen_step * allen_gradient * grain_spread
            )
        costate, c_width = in_domain(new_costate, point, geometry), point
        cograins, cg_width = in_domain(new_cograins, new_cg_width, geometry), new_cg_width

    costate = crop(costate, c_width, 0)
    cograins = crop(cograins, cg_width, 0)
    result = scatter_heights(
        jnp.concatenate([last_density[None], costate[None], cograins], axis=0), height_rows
    )
    return (result[0], result[1], result[2:])


def solution(mesh):
    in_specs = (
        P("hgt", "azim", "rad"),
        P("hgt", "azim", "rad"),
        P("hgt", "azim", "rad"),
        P("hgt", "azim", "rad"),
    )
    out_specs = (P("hgt", "azim", "rad"), P("hgt", "azim", "rad"), P(None, "hgt", "azim", "rad"))
    return jax.shard_map(shards, mesh=mesh, in_specs=in_specs, out_specs=out_specs, check_vma=False)
```

```python
import jax
import jax.numpy as jnp
from jax import lax
from jax.sharding import PartitionSpec as P

STEPS = 3
GRAINS = 4


bulk_weight = 16.0
grain_weight = 1.0
cahn_step = 0.005
allen_step = 0.05
cahn_gradient = 1.0
allen_gradient = 1.0
full_turn = 6.283185307179586

HALO = 4 * STEPS


def halo_exchange(block, axis, dim, width, cyclic):
    peers, length = (lax.axis_size(axis), block.shape[dim])
    up = [(i, (i + 1) % peers) for i in range(peers) if cyclic or i + 1 < peers]
    down = [(j, i) for i, j in up]
    last = lax.slice_in_dim(block, length - width, length, axis=dim)
    leading = lax.slice_in_dim(block, 0, width, axis=dim)
    before = lax.ppermute(last, axis, up)
    after = lax.ppermute(leading, axis, down)
    return jnp.concatenate([before, block, after], axis=dim)


def azim_exchange(fields, widths):
    peers = lax.axis_size("azim")
    up = [(i, (i + 1) % peers) for i in range(peers)]
    down = [(j, i) for i, j in up]
    rows = fields[0].shape[-2]
    last = jnp.concatenate([f[..., rows - w :, :] for f, w in zip(fields, widths)], axis=-2)
    leading = jnp.concatenate([f[..., :w, :] for f, w in zip(fields, widths)], axis=-2)
    before = lax.ppermute(last, "azim", up)
    after = lax.ppermute(leading, "azim", down)
    out, at = [], 0
    for f, w in zip(fields, widths):
        out.append(jnp.concatenate([before[..., at : at + w, :], f, after[..., at : at + w, :]], axis=-2))
        at += w
    return out


def gather_axis(block, axis, dim):
    peers = lax.axis_size(axis)
    if peers == 1:
        return block
    own = lax.axis_index(axis)
    parts = [block]
    for shift in range(1, peers):
        parts.append(lax.ppermute(block, axis, [(i, (i + shift) % peers) for i in range(peers)]))
    if peers == 2:
        return jnp.where(
            own == 0,
            jnp.concatenate([parts[0], parts[1]], axis=dim),
            jnp.concatenate([parts[1], parts[0]], axis=dim),
        )
    stacked = jnp.stack(parts)
    order = (own - jnp.arange(peers, dtype=jnp.int32)) % peers
    ordered = jnp.take(stacked, order, axis=0)
    ordered = jnp.moveaxis(ordered, 0, dim)
    shape = list(block.shape)
    shape[dim] = shape[dim] * peers
    return ordered.reshape(shape)


def chip_window(block, width):
    peers, own, rad_peers = (lax.axis_size("hgt"), lax.axis_index("hgt"), lax.axis_size("rad"))
    cols = block.shape[-1]
    part = cols // peers
    piece = jnp.where(own == 0, block[..., :width], block[..., cols - width :])
    pairs = []
    for r in range(rad_peers - 1):
        pairs.append((r * peers + peers - 1, (r + 1) * peers))
        pairs.append(((r + 1) * peers, r * peers + peers - 1))
    received = lax.ppermute(piece, ("rad", "hgt"), pairs)
    padded = jnp.concatenate([received, block, received], axis=-1)
    return lax.dynamic_slice_in_dim(padded, own * part, part + 2 * width, axis=padded.ndim - 1)


def edge_columns(block, width):
    own, rad_peers = (lax.axis_index("hgt"), lax.axis_size("rad"))
    cols = block.shape[-1]
    first, last = (block[..., :width], block[..., cols - width :])
    cross, same = ([], [])
    for r in range(rad_peers - 1):
        cross += [(2 * r + 1, 2 * r + 2), (2 * r + 2, 2 * r + 1)]
        same += [(2 * r, 2 * r + 2), (2 * r + 3, 2 * r + 1)]
    from_cross = lax.ppermute(jnp.where(own == 0, first, last), ("rad", "hgt"), cross)
    from_same = lax.ppermute(jnp.where(own == 0, last, first), ("rad", "hgt"), same)
    return jnp.where(
        own == 0,
        jnp.concatenate([from_same, from_cross], axis=1),
        jnp.concatenate([from_cross, from_same], axis=1),
    )


def two_core_window(block, received, width):
    own = lax.axis_index("hgt")
    part = block.shape[-1] // 2
    padded = jnp.concatenate([received, block, received], axis=-1)
    return lax.dynamic_slice_in_dim(padded, own * part, part + 2 * width, axis=padded.ndim - 1)


def scatter_heights(x, height_rows):
    peers, own = (lax.axis_size("hgt"), lax.axis_index("hgt"))
    parts = []
    for shift in range(peers):
        dest = (own + shift) % peers
        piece = lax.dynamic_slice_in_dim(x, dest * height_rows, height_rows, axis=1)
        if shift:
            piece = lax.ppermute(piece, "hgt", [(i, (i + shift) % peers) for i in range(peers)])
        parts.append(piece)
    if peers == 2:
        return jnp.where(
            own == 0,
            jnp.concatenate([parts[0], parts[1]], axis=-1),
            jnp.concatenate([parts[1], parts[0]], axis=-1),
        )
    stacked = jnp.stack(parts)
    order = (own - jnp.arange(peers, dtype=jnp.int32)) % peers
    ordered = jnp.moveaxis(jnp.take(stacked, order, axis=0), 0, -2)
    shape = ordered.shape
    return ordered.reshape(shape[:-2] + (shape[-2] * shape[-1],))


def crop(x, width, new_width):
    cut = width - new_width
    if cut == 0:
        return x
    return x[..., cut : x.shape[-2] - cut, cut : x.shape[-1] - cut]


def radial_mask(width, geometry):
    rad_start, total_hgt, total_azim, total_rad, cols, weights = geometry
    rad_index = rad_start - width + jnp.arange(cols + 2 * width, dtype=jnp.int32)
    return (rad_index >= 0) & (rad_index < total_rad)


def in_domain(x, width, geometry):
    return jnp.where(radial_mask(width, geometry), x, 0.0)


def stencil_weights(rad_start, total_azim, total_rad, cols):
    rad_index_all = rad_start - HALO - 1 + jnp.arange(cols + 2 * HALO + 2, dtype=jnp.int32)
    radius_all = total_azim / full_turn + rad_index_all.astype(jnp.float32) + 0.5
    rad_index = rad_index_all[1:-1]
    radius = radius_all[1:-1]
    outer_face = (radius + 0.5) * (rad_index < total_rad - 1).astype(jnp.float32)
    inner_face = (radius - 0.5) * (rad_index > 0).astype(jnp.float32)
    arc_length = radius * (full_turn / total_azim)
    arc_weight = 1.0 / (arc_length * arc_length)
    radial_center = (outer_face + inner_face) / radius
    forward = (outer_face / radius, inner_face / radius)
    transposed = (outer_face / radius_all[2:], inner_face / radius_all[:-2])
    return forward, transposed, arc_weight, radial_center


def laplace(x, width, geometry, transpose):
    rad_start, total_hgt, total_azim, total_rad, cols, weights = geometry
    forward, transposed, arc_weight, radial_center = weights
    outward_weight, inward_weight = transposed if transpose else forward
    height_rows = x.shape[-3]
    out_cols = x.shape[-1] - 2
    at = HALO - (width - 1)
    cut = lambda w: w[at : at + out_cols]
    outward_weight, inward_weight = cut(outward_weight), cut(inward_weight)
    arc_weight, radial_center = cut(arc_weight), cut(radial_center)
    hgt_index = jnp.arange(height_rows, dtype=jnp.int32)
    faces = (hgt_index < total_hgt - 1).astype(jnp.float32) + (hgt_index > 0).astype(jnp.float32)
    center_weight = radial_center + 2.0 * arc_weight + faces[:, None, None]
    leading = x.ndim - 3
    padded = jnp.pad(x, [(0, 0)] * leading + [(1, 1), (0, 0), (0, 0)])
    center = padded[..., 1:-1, 1:-1, 1:-1]
    radial = outward_weight * padded[..., 1:-1, 1:-1, 2:] + inward_weight * padded[..., 1:-1, 1:-1, :-2]
    azimuthal = arc_weight * (padded[..., 1:-1, 2:, 1:-1] + padded[..., 1:-1, :-2, 1:-1])
    vertical = padded[..., 2:, 1:-1, 1:-1] + padded[..., :-2, 1:-1, 1:-1]
    return radial + azimuthal + vertical - center_weight * center


def chemical(density, grains):
    square_sum = jnp.sum(grains * grains, axis=0)
    cube_sum = jnp.sum(grains * grains * grains, axis=0)
    bulk_drive = 2.0 * bulk_weight * density * (1.0 - density) * (
        1.0 - 2.0 * density
    ) + grain_weight * (2.0 * density - 6.0 * square_sum + 4.0 * cube_sum)
    grain_drive = (
        12.0
        * grain_weight
        * (grains * (1.0 - density) - grains * grains * (2.0 - density) + grains * square_sum)
    )
    return (bulk_drive, grain_drive)


def reach():
    need_lc, need_lg = [0], [0]
    for moment in range(STEPS):
        need_lc.append(need_lc[-1] + 2)
        need_lg.append(max(need_lg[-1] + 1, need_lc[moment]))
    need_d, need_e = [need_lc[STEPS]], [-1]
    for moment in range(STEPS - 1, -1, -1):
        pot_width = need_d[0] + 1
        need_d.insert(0, max(pot_width + 1, need_e[0], need_lc[moment]))
        need_e.insert(0, max(pot_width, need_e[0] + 1, need_lc[moment]))
    return need_d, need_e, need_lc, need_lg


def chemical_pullback(density, grains, copotential, codrive):
    square_sum = jnp.sum(grains * grains, axis=0)
    grain_square = grains * grains
    drive_slope = 12.0 * grain_weight * (grain_square - grains)
    bulk_slope = 2.0 * bulk_weight * (1.0 - 6.0 * density + 6.0 * density * density) + 2.0 * grain_weight
    if codrive is None:
        return copotential * bulk_slope, copotential * drive_slope
    pull_density = copotential * bulk_slope + jnp.sum(codrive * drive_slope, axis=0)
    coupling = jnp.sum(codrive * grains, axis=0)
    pull_grains = (
        copotential * drive_slope
        + 12.0 * grain_weight * codrive * ((1.0 - density) - 2.0 * grains * (2.0 - density) + square_sum)
        + 24.0 * grain_weight * grains * coupling
    )
    return pull_density, pull_grains


def shards(density, labels, observed, measured):
    height_rows, azim_rows, radius_rows = density.shape
    total_hgt = height_rows * lax.axis_size("hgt")
    part = radius_rows // lax.axis_size("hgt")
    rad_start = lax.axis_index("rad") * radius_rows + lax.axis_index("hgt") * part
    total_azim = azim_rows * lax.axis_size("azim")
    total_rad = radius_rows * lax.axis_size("rad")
    geometry = (
        rad_start,
        total_hgt,
        total_azim,
        total_rad,
        part,
        stencil_weights(rad_start, total_azim, total_rad, part),
    )
    packed = jnp.stack([density, labels.astype(jnp.float32), observed, measured.astype(jnp.float32)])
    if lax.axis_size("hgt") == 2:
        received = edge_columns(packed, HALO)
        packed = two_core_window(gather_axis(packed, "hgt", 1), received, HALO)
    else:
        packed = chip_window(gather_axis(packed, "hgt", 1), HALO)
    need_d, need_e, need_lc, need_lg = reach()
    widths = (need_d[0], need_e[0], need_lc[STEPS], need_lc[STEPS])
    trim = lambda f, w: f[..., HALO - w : f.shape[-1] - (HALO - w)]
    density, grain_label = [
        trim(f, w) for f, w in zip(azim_exchange([packed[0], packed[1]], widths[:2]), widths[:2])
    ]
    misfit_terms, density = lax.optimization_barrier((packed[2:], density))
    observed, measured = [
        trim(f, w) for f, w in zip(azim_exchange([misfit_terms[0], misfit_terms[1]], widths[2:]), widths[2:])
    ]
    grains = (
        grain_label[None] == jnp.arange(GRAINS, dtype=jnp.float32)[:, None, None, None]
    ).astype(jnp.float32)
    need_d, need_e, need_lc, need_lg = reach()
    density = in_domain(density, need_d[0], geometry)
    grains = in_domain(grains, need_e[0], geometry)
    history = []
    for moment in range(STEPS):
        d_width, e_width = need_d[moment], need_e[moment]
        history.append((density, d_width, grains, e_width))
        pot_width = need_d[moment + 1] + 1
        next_e = need_e[moment + 1]
        both = max(pot_width, next_e)
        bulk_drive, grain_drive = chemical(crop(density, d_width, both), crop(grains, e_width, both))
        potential = crop(bulk_drive, both, pot_width) - cahn_gradient * laplace(
            crop(density, d_width, pot_width + 1), pot_width + 1, geometry, False
        )
        flux_term = laplace(potential, pot_width, geometry, False)
        new_density = crop(density, d_width, need_d[moment + 1]) + cahn_step * flux_term
        if next_e >= 0:
            grain_spread = laplace(crop(grains, e_width, next_e + 1), next_e + 1, geometry, False)
            new_grains = crop(grains, e_width, next_e) - allen_step * (
                crop(grain_drive, both, next_e) - allen_gradient * grain_spread
            )
            grains = in_domain(new_grains, next_e, geometry)
        density = in_domain(new_density, need_d[moment + 1], geometry)
    d_width = need_d[STEPS]

    observed = crop(observed, widths[2], d_width)
    measured = crop(measured, widths[3], d_width)
    costate = in_domain(measured * (density - observed), d_width, geometry)
    c_width = d_width
    last_density = crop(density, d_width, 0)
    cograins, cg_width = None, None
    for moment in range(STEPS - 1, -1, -1):
        fields_density, fd_width, fields_grains, fg_width = history[moment]
        point = need_lc[moment]
        nu_width = point + 1
        copotential = cahn_step * laplace(crop(costate, c_width, nu_width + 1), nu_width + 1, geometry, True)
        here_density = crop(fields_density, fd_width, point)
        here_grains = crop(fields_grains, fg_width, point)
        here_copotential = crop(copotential, nu_width, point)
        if cograins is None:
            pull_density, pull_grains = chemical_pullback(
                here_density, here_grains, here_copotential, None
            )
        else:
            pull_density, pull_grains = chemical_pullback(
                here_density, here_grains, here_copotential, -allen_step * crop(cograins, cg_width, point)
            )
        reaction = laplace(in_domain(copotential, nu_width, geometry), nu_width, geometry, True)
        new_costate = crop(costate, c_width, point) + pull_density - cahn_gradient * reaction
        new_cg_width = need_lg[moment]
        if cograins is None:
            new_cograins = crop(pull_grains, point, new_cg_width)
        else:
            grain_spread = laplace(
                crop(cograins, cg_width, new_cg_width + 1), new_cg_width + 1, geometry, True
            )
            new_cograins = (
                crop(cograins, cg_width, new_cg_width)
                + crop(pull_grains, point, new_cg_width)
                + allen_step * allen_gradient * grain_spread
            )
        costate, c_width = in_domain(new_costate, point, geometry), point
        cograins, cg_width = in_domain(new_cograins, new_cg_width, geometry), new_cg_width

    costate = crop(costate, c_width, 0)
    cograins = crop(cograins, cg_width, 0)
    result = scatter_heights(
        jnp.concatenate([last_density[None], costate[None], cograins], axis=0), height_rows
    )
    return (result[0], result[1], result[2:])


def solution(mesh):
    in_specs = (
        P("hgt", "azim", "rad"),
        P("hgt", "azim", "rad"),
        P("hgt", "azim", "rad"),
        P("hgt", "azim", "rad"),
    )
    out_specs = (P("hgt", "azim", "rad"), P("hgt", "azim", "rad"), P(None, "hgt", "azim", "rad"))
    return jax.shard_map(shards, mesh=mesh, in_specs=in_specs, out_specs=out_specs, check_vma=False)
```

```python
import jax
import jax.numpy as jnp
from jax import lax
from jax.sharding import PartitionSpec as P

STEPS = 3
GRAINS = 4


bulk_weight = 16.0
grain_weight = 1.0
cahn_step = 0.005
allen_step = 0.05
cahn_gradient = 1.0
allen_gradient = 1.0
full_turn = 6.283185307179586

HALO = 4 * STEPS


def halo_exchange(block, axis, dim, width, cyclic):
    peers, length = (lax.axis_size(axis), block.shape[dim])
    up = [(i, (i + 1) % peers) for i in range(peers) if cyclic or i + 1 < peers]
    down = [(j, i) for i, j in up]
    last = lax.slice_in_dim(block, length - width, length, axis=dim)
    leading = lax.slice_in_dim(block, 0, width, axis=dim)
    before = lax.ppermute(last, axis, up)
    after = lax.ppermute(leading, axis, down)
    return jnp.concatenate([before, block, after], axis=dim)


def azim_exchange(fields, widths):
    peers = lax.axis_size("azim")
    up = [(i, (i + 1) % peers) for i in range(peers)]
    down = [(j, i) for i, j in up]
    rows = fields[0].shape[-2]
    last = jnp.concatenate([f[..., rows - w :, :] for f, w in zip(fields, widths)], axis=-2)
    leading = jnp.concatenate([f[..., :w, :] for f, w in zip(fields, widths)], axis=-2)
    before = lax.ppermute(last, "azim", up)
    after = lax.ppermute(leading, "azim", down)
    out, at = [], 0
    for f, w in zip(fields, widths):
        out.append(jnp.concatenate([before[..., at : at + w, :], f, after[..., at : at + w, :]], axis=-2))
        at += w
    return out


def gather_axis(block, axis, dim):
    peers = lax.axis_size(axis)
    if peers == 1:
        return block
    own = lax.axis_index(axis)
    parts = [block]
    for shift in range(1, peers):
        parts.append(lax.ppermute(block, axis, [(i, (i + shift) % peers) for i in range(peers)]))
    if peers == 2:
        return jnp.where(
            own == 0,
            jnp.concatenate([parts[0], parts[1]], axis=dim),
            jnp.concatenate([parts[1], parts[0]], axis=dim),
        )
    stacked = jnp.stack(parts)
    order = (own - jnp.arange(peers, dtype=jnp.int32)) % peers
    ordered = jnp.take(stacked, order, axis=0)
    ordered = jnp.moveaxis(ordered, 0, dim)
    shape = list(block.shape)
    shape[dim] = shape[dim] * peers
    return ordered.reshape(shape)


def chip_window(block, width):
    peers, own, rad_peers = (lax.axis_size("hgt"), lax.axis_index("hgt"), lax.axis_size("rad"))
    cols = block.shape[-1]
    part = cols // peers
    piece = jnp.where(own == 0, block[..., :width], block[..., cols - width :])
    pairs = []
    for r in range(rad_peers - 1):
        pairs.append((r * peers + peers - 1, (r + 1) * peers))
        pairs.append(((r + 1) * peers, r * peers + peers - 1))
    received = lax.ppermute(piece, ("rad", "hgt"), pairs)
    padded = jnp.concatenate([received, block, received], axis=-1)
    return lax.dynamic_slice_in_dim(padded, own * part, part + 2 * width, axis=padded.ndim - 1)


def edge_columns(block, width):
    own, rad_peers = (lax.axis_index("hgt"), lax.axis_size("rad"))
    cols = block.shape[-1]
    first, last = (block[..., :width], block[..., cols - width :])
    cross, same = ([], [])
    for r in range(rad_peers - 1):
        cross += [(2 * r + 1, 2 * r + 2), (2 * r + 2, 2 * r + 1)]
        same += [(2 * r, 2 * r + 2), (2 * r + 3, 2 * r + 1)]
    from_cross = lax.ppermute(jnp.where(own == 0, first, last), ("rad", "hgt"), cross)
    from_same = lax.ppermute(jnp.where(own == 0, last, first), ("rad", "hgt"), same)
    return jnp.where(
        own == 0,
        jnp.concatenate([from_same, from_cross], axis=1),
        jnp.concatenate([from_cross, from_same], axis=1),
    )


def two_core_window(block, received, width):
    own = lax.axis_index("hgt")
    part = block.shape[-1] // 2
    padded = jnp.concatenate([received, block, received], axis=-1)
    return lax.dynamic_slice_in_dim(padded, own * part, part + 2 * width, axis=padded.ndim - 1)


def scatter_heights(x, height_rows):
    peers, own = (lax.axis_size("hgt"), lax.axis_index("hgt"))
    parts = []
    for shift in range(peers):
        dest = (own + shift) % peers
        piece = lax.dynamic_slice_in_dim(x, dest * height_rows, height_rows, axis=1)
        if shift:
            piece = lax.ppermute(piece, "hgt", [(i, (i + shift) % peers) for i in range(peers)])
        parts.append(piece)
    if peers == 2:
        return jnp.where(
            own == 0,
            jnp.concatenate([parts[0], parts[1]], axis=-1),
            jnp.concatenate([parts[1], parts[0]], axis=-1),
        )
    stacked = jnp.stack(parts)
    order = (own - jnp.arange(peers, dtype=jnp.int32)) % peers
    ordered = jnp.moveaxis(jnp.take(stacked, order, axis=0), 0, -2)
    shape = ordered.shape
    return ordered.reshape(shape[:-2] + (shape[-2] * shape[-1],))


def crop(x, width, new_width):
    cut = width - new_width
    if cut == 0:
        return x
    return x[..., cut : x.shape[-2] - cut, cut : x.shape[-1] - cut]


def radial_mask(width, geometry):
    rad_start, total_hgt, total_azim, total_rad, cols = geometry
    rad_index = rad_start - width + jnp.arange(cols + 2 * width, dtype=jnp.int32)
    return (rad_index >= 0) & (rad_index < total_rad)


def in_domain(x, width, geometry):
    return jnp.where(radial_mask(width, geometry), x, 0.0)


def laplace(x, width, geometry, transpose):
    rad_start, total_hgt, total_azim, total_rad, cols = geometry
    margin = width - 1
    height_rows = x.shape[-3]
    radius_rows = x.shape[-1] - 2
    rad_index_all = rad_start - margin - 1 + jnp.arange(radius_rows + 2, dtype=jnp.int32)
    radius_all = total_azim / full_turn + rad_index_all.astype(jnp.float32) + 0.5
    rad_index = rad_index_all[1:-1]
    radius = radius_all[1:-1]
    outer_face = (radius + 0.5) * (rad_index < total_rad - 1).astype(jnp.float32)
    inner_face = (radius - 0.5) * (rad_index > 0).astype(jnp.float32)
    if transpose:
        outward_weight = outer_face / radius_all[2:]
        inward_weight = inner_face / radius_all[:-2]
    else:
        outward_weight = outer_face / radius
        inward_weight = inner_face / radius
    arc_length = radius * (full_turn / total_azim)
    arc_weight = 1.0 / (arc_length * arc_length)
    hgt_index = jnp.arange(height_rows, dtype=jnp.int32)
    faces = (hgt_index < total_hgt - 1).astype(jnp.float32) + (hgt_index > 0).astype(jnp.float32)
    center_weight = (outer_face + inner_face) / radius + 2.0 * arc_weight + faces[:, None, None]
    leading = x.ndim - 3
    padded = jnp.pad(x, [(0, 0)] * leading + [(1, 1), (0, 0), (0, 0)])
    center = padded[..., 1:-1, 1:-1, 1:-1]
    radial = outward_weight * padded[..., 1:-1, 1:-1, 2:] + inward_weight * padded[..., 1:-1, 1:-1, :-2]
    azimuthal = arc_weight * (padded[..., 1:-1, 2:, 1:-1] + padded[..., 1:-1, :-2, 1:-1])
    vertical = padded[..., 2:, 1:-1, 1:-1] + padded[..., :-2, 1:-1, 1:-1]
    return radial + azimuthal + vertical - center_weight * center


def chemical(density, grains):
    square_sum = jnp.sum(grains * grains, axis=0)
    cube_sum = jnp.sum(grains * grains * grains, axis=0)
    bulk_drive = 2.0 * bulk_weight * density * (1.0 - density) * (
        1.0 - 2.0 * density
    ) + grain_weight * (2.0 * density - 6.0 * square_sum + 4.0 * cube_sum)
    grain_drive = (
        12.0
        * grain_weight
        * (grains * (1.0 - density) - grains * grains * (2.0 - density) + grains * square_sum)
    )
    return (bulk_drive, grain_drive)


def reach():
    need_lc, need_lg = [0], [0]
    for moment in range(STEPS):
        need_lc.append(need_lc[-1] + 2)
        need_lg.append(max(need_lg[-1] + 1, need_lc[moment]))
    need_d, need_e = [need_lc[STEPS]], [-1]
    for moment in range(STEPS - 1, -1, -1):
        pot_width = need_d[0] + 1
        need_d.insert(0, max(pot_width + 1, need_e[0], need_lc[moment]))
        need_e.insert(0, max(pot_width, need_e[0] + 1, need_lc[moment]))
    return need_d, need_e, need_lc, need_lg


def chemical_pullback(density, grains, copotential, codrive):
    square_sum = jnp.sum(grains * grains, axis=0)
    grain_square = grains * grains
    drive_slope = 12.0 * grain_weight * (grain_square - grains)
    bulk_slope = 2.0 * bulk_weight * (1.0 - 6.0 * density + 6.0 * density * density) + 2.0 * grain_weight
    if codrive is None:
        return copotential * bulk_slope, copotential * drive_slope
    pull_density = copotential * bulk_slope + jnp.sum(codrive * drive_slope, axis=0)
    coupling = jnp.sum(codrive * grains, axis=0)
    pull_grains = (
        copotential * drive_slope
        + 12.0 * grain_weight * codrive * ((1.0 - density) - 2.0 * grains * (2.0 - density) + square_sum)
        + 24.0 * grain_weight * grains * coupling
    )
    return pull_density, pull_grains


def shards(density, labels, observed, measured):
    height_rows, azim_rows, radius_rows = density.shape
    total_hgt = height_rows * lax.axis_size("hgt")
    part = radius_rows // lax.axis_size("hgt")
    geometry = (
        lax.axis_index("rad") * radius_rows + lax.axis_index("hgt") * part,
        total_hgt,
        azim_rows * lax.axis_size("azim"),
        radius_rows * lax.axis_size("rad"),
        part,
    )
    packed = jnp.stack([density, labels.astype(jnp.float32), observed, measured.astype(jnp.float32)])
    if lax.axis_size("hgt") == 2:
        received = edge_columns(packed, HALO)
        packed = two_core_window(gather_axis(packed, "hgt", 1), received, HALO)
    else:
        packed = chip_window(gather_axis(packed, "hgt", 1), HALO)
    need_d, need_e, need_lc, need_lg = reach()
    widths = (need_d[0], need_e[0], need_lc[STEPS], need_lc[STEPS])
    trim = lambda f, w: f[..., HALO - w : f.shape[-1] - (HALO - w)]
    density, grain_label = [
        trim(f, w) for f, w in zip(azim_exchange([packed[0], packed[1]], widths[:2]), widths[:2])
    ]
    misfit_terms = packed[2:]
    observed, measured = [
        trim(f, w) for f, w in zip(azim_exchange([misfit_terms[0], misfit_terms[1]], widths[2:]), widths[2:])
    ]
    grains = (
        grain_label[None] == jnp.arange(GRAINS, dtype=jnp.float32)[:, None, None, None]
    ).astype(jnp.float32)
    need_d, need_e, need_lc, need_lg = reach()
    density = in_domain(density, need_d[0], geometry)
    grains = in_domain(grains, need_e[0], geometry)
    history = []
    for moment in range(STEPS):
        d_width, e_width = need_d[moment], need_e[moment]
        history.append((density, d_width, grains, e_width))
        pot_width = need_d[moment + 1] + 1
        next_e = need_e[moment + 1]
        both = max(pot_width, next_e)
        bulk_drive, grain_drive = chemical(crop(density, d_width, both), crop(grains, e_width, both))
        potential = crop(bulk_drive, both, pot_width) - cahn_gradient * laplace(
            crop(density, d_width, pot_width + 1), pot_width + 1, geometry, False
        )
        flux_term = laplace(potential, pot_width, geometry, False)
        new_density = crop(density, d_width, need_d[moment + 1]) + cahn_step * flux_term
        if next_e >= 0:
            grain_spread = laplace(crop(grains, e_width, next_e + 1), next_e + 1, geometry, False)
            new_grains = crop(grains, e_width, next_e) - allen_step * (
                crop(grain_drive, both, next_e) - allen_gradient * grain_spread
            )
            grains = in_domain(new_grains, next_e, geometry)
        density = in_domain(new_density, need_d[moment + 1], geometry)
    d_width = need_d[STEPS]

    observed = crop(observed, widths[2], d_width)
    measured = crop(measured, widths[3], d_width)
    costate = in_domain(measured * (density - observed), d_width, geometry)
    c_width = d_width
    last_density = crop(density, d_width, 0)
    cograins, cg_width = None, None
    for moment in range(STEPS - 1, -1, -1):
        fields_density, fd_width, fields_grains, fg_width = history[moment]
        point = need_lc[moment]
        nu_width = point + 1
        copotential = cahn_step * laplace(crop(costate, c_width, nu_width + 1), nu_width + 1, geometry, True)
        here_density = crop(fields_density, fd_width, point)
        here_grains = crop(fields_grains, fg_width, point)
        here_copotential = crop(copotential, nu_width, point)
        if cograins is None:
            pull_density, pull_grains = chemical_pullback(
                here_density, here_grains, here_copotential, None
            )
        else:
            pull_density, pull_grains = chemical_pullback(
                here_density, here_grains, here_copotential, -allen_step * crop(cograins, cg_width, point)
            )
        reaction = laplace(in_domain(copotential, nu_width, geometry), nu_width, geometry, True)
        new_costate = crop(costate, c_width, point) + pull_density - cahn_gradient * reaction
        new_cg_width = need_lg[moment]
        if cograins is None:
            new_cograins = crop(pull_grains, point, new_cg_width)
        else:
            grain_spread = laplace(
                crop(cograins, cg_width, new_cg_width + 1), new_cg_width + 1, geometry, True
            )
            new_cograins = (
                crop(cograins, cg_width, new_cg_width)
                + crop(pull_grains, point, new_cg_width)
                + allen_step * allen_gradient * grain_spread
            )
        costate, c_width = in_domain(new_costate, point, geometry), point
        cograins, cg_width = in_domain(new_cograins, new_cg_width, geometry), new_cg_width

    costate = crop(costate, c_width, 0)
    cograins = crop(cograins, cg_width, 0)
    result = scatter_heights(
        jnp.concatenate([last_density[None], costate[None], cograins], axis=0), height_rows
    )
    return (result[0], result[1], result[2:])


def solution(mesh):
    in_specs = (
        P("hgt", "azim", "rad"),
        P("hgt", "azim", "rad"),
        P("hgt", "azim", "rad"),
        P("hgt", "azim", "rad"),
    )
    out_specs = (P("hgt", "azim", "rad"), P("hgt", "azim", "rad"), P(None, "hgt", "azim", "rad"))
    return jax.shard_map(shards, mesh=mesh, in_specs=in_specs, out_specs=out_specs, check_vma=False)
```

```python
import jax
import jax.numpy as jnp
from jax import lax
from jax.sharding import PartitionSpec as P

STEPS = 3
GRAINS = 4


bulk_weight = 16.0
grain_weight = 1.0
cahn_step = 0.005
allen_step = 0.05
cahn_gradient = 1.0
allen_gradient = 1.0
full_turn = 6.283185307179586

HALO = 4 * STEPS


def halo_exchange(block, axis, dim, width, cyclic):
    peers, length = (lax.axis_size(axis), block.shape[dim])
    up = [(i, (i + 1) % peers) for i in range(peers) if cyclic or i + 1 < peers]
    down = [(j, i) for i, j in up]
    last = lax.slice_in_dim(block, length - width, length, axis=dim)
    leading = lax.slice_in_dim(block, 0, width, axis=dim)
    before = lax.ppermute(last, axis, up)
    after = lax.ppermute(leading, axis, down)
    return jnp.concatenate([before, block, after], axis=dim)


def azim_exchange(fields, widths):
    peers = lax.axis_size("azim")
    up = [(i, (i + 1) % peers) for i in range(peers)]
    down = [(j, i) for i, j in up]
    rows = fields[0].shape[-2]
    last = jnp.concatenate([f[..., rows - w :, :] for f, w in zip(fields, widths)], axis=-2)
    leading = jnp.concatenate([f[..., :w, :] for f, w in zip(fields, widths)], axis=-2)
    before = lax.ppermute(last, "azim", up)
    after = lax.ppermute(leading, "azim", down)
    out, at = [], 0
    for f, w in zip(fields, widths):
        out.append(jnp.concatenate([before[..., at : at + w, :], f, after[..., at : at + w, :]], axis=-2))
        at += w
    return out


def gather_axis(block, axis, dim):
    peers = lax.axis_size(axis)
    if peers == 1:
        return block
    own = lax.axis_index(axis)
    parts = [block]
    for shift in range(1, peers):
        parts.append(lax.ppermute(block, axis, [(i, (i + shift) % peers) for i in range(peers)]))
    if peers == 2:
        return jnp.where(
            own == 0,
            jnp.concatenate([parts[0], parts[1]], axis=dim),
            jnp.concatenate([parts[1], parts[0]], axis=dim),
        )
    stacked = jnp.stack(parts)
    order = (own - jnp.arange(peers, dtype=jnp.int32)) % peers
    ordered = jnp.take(stacked, order, axis=0)
    ordered = jnp.moveaxis(ordered, 0, dim)
    shape = list(block.shape)
    shape[dim] = shape[dim] * peers
    return ordered.reshape(shape)


def chip_window(block, width):
    peers, own, rad_peers = (lax.axis_size("hgt"), lax.axis_index("hgt"), lax.axis_size("rad"))
    cols = block.shape[-1]
    part = cols // peers
    piece = jnp.where(own == 0, block[..., :width], block[..., cols - width :])
    pairs = []
    for r in range(rad_peers - 1):
        pairs.append((r * peers + peers - 1, (r + 1) * peers))
        pairs.append(((r + 1) * peers, r * peers + peers - 1))
    received = lax.ppermute(piece, ("rad", "hgt"), pairs)
    padded = jnp.concatenate([received, block, received], axis=-1)
    return lax.dynamic_slice_in_dim(padded, own * part, part + 2 * width, axis=padded.ndim - 1)


def edge_columns(block, width):
    own, rad_peers = (lax.axis_index("hgt"), lax.axis_size("rad"))
    cols = block.shape[-1]
    first, last = (block[..., :width], block[..., cols - width :])
    cross, same = ([], [])
    for r in range(rad_peers - 1):
        cross += [(2 * r + 1, 2 * r + 2), (2 * r + 2, 2 * r + 1)]
        same += [(2 * r, 2 * r + 2), (2 * r + 3, 2 * r + 1)]
    from_cross = lax.ppermute(jnp.where(own == 0, first, last), ("rad", "hgt"), cross)
    from_same = lax.ppermute(jnp.where(own == 0, last, first), ("rad", "hgt"), same)
    return jnp.where(
        own == 0,
        jnp.concatenate([from_same, from_cross], axis=1),
        jnp.concatenate([from_cross, from_same], axis=1),
    )


def two_core_window(block, received, width):
    own = lax.axis_index("hgt")
    part = block.shape[-1] // 2
    padded = jnp.concatenate([received, block, received], axis=-1)
    return lax.dynamic_slice_in_dim(padded, own * part, part + 2 * width, axis=padded.ndim - 1)


def scatter_heights(x, height_rows, splits):
    peers, own = (lax.axis_size("hgt"), lax.axis_index("hgt"))
    parts = []
    for shift in range(peers):
        dest = (own + shift) % peers
        piece = lax.dynamic_slice_in_dim(x, dest * height_rows, height_rows, axis=1)
        if shift:
            piece = lax.ppermute(piece, "hgt", [(i, (i + shift) % peers) for i in range(peers)])
        parts.append(piece)
    if peers == 2:
        return [
            jnp.where(
                own == 0,
                jnp.concatenate([parts[0][lo:hi], parts[1][lo:hi]], axis=-1),
                jnp.concatenate([parts[1][lo:hi], parts[0][lo:hi]], axis=-1),
            )
            for lo, hi in splits
        ]
    stacked = jnp.stack(parts)
    order = (own - jnp.arange(peers, dtype=jnp.int32)) % peers
    ordered = jnp.moveaxis(jnp.take(stacked, order, axis=0), 0, -2)
    shape = ordered.shape
    ordered = ordered.reshape(shape[:-2] + (shape[-2] * shape[-1],))
    return [ordered[lo:hi] for lo, hi in splits]


def crop(x, width, new_width):
    cut = width - new_width
    if cut == 0:
        return x
    return x[..., cut : x.shape[-2] - cut, cut : x.shape[-1] - cut]


def radial_mask(width, geometry):
    rad_start, total_hgt, total_azim, total_rad, cols = geometry
    rad_index = rad_start - width + jnp.arange(cols + 2 * width, dtype=jnp.int32)
    return (rad_index >= 0) & (rad_index < total_rad)


def in_domain(x, width, geometry):
    return jnp.where(radial_mask(width, geometry), x, 0.0)


def laplace(x, width, geometry, transpose):
    rad_start, total_hgt, total_azim, total_rad, cols = geometry
    margin = width - 1
    height_rows = x.shape[-3]
    radius_rows = x.shape[-1] - 2
    rad_index_all = rad_start - margin - 1 + jnp.arange(radius_rows + 2, dtype=jnp.int32)
    radius_all = total_azim / full_turn + rad_index_all.astype(jnp.float32) + 0.5
    rad_index = rad_index_all[1:-1]
    radius = radius_all[1:-1]
    outer_face = (radius + 0.5) * (rad_index < total_rad - 1).astype(jnp.float32)
    inner_face = (radius - 0.5) * (rad_index > 0).astype(jnp.float32)
    if transpose:
        outward_weight = outer_face / radius_all[2:]
        inward_weight = inner_face / radius_all[:-2]
    else:
        outward_weight = outer_face / radius
        inward_weight = inner_face / radius
    arc_length = radius * (full_turn / total_azim)
    arc_weight = 1.0 / (arc_length * arc_length)
    hgt_index = jnp.arange(height_rows, dtype=jnp.int32)
    faces = (hgt_index < total_hgt - 1).astype(jnp.float32) + (hgt_index > 0).astype(jnp.float32)
    center_weight = (outer_face + inner_face) / radius + 2.0 * arc_weight + faces[:, None, None]
    leading = x.ndim - 3
    padded = jnp.pad(x, [(0, 0)] * leading + [(1, 1), (0, 0), (0, 0)])
    center = padded[..., 1:-1, 1:-1, 1:-1]
    radial = outward_weight * padded[..., 1:-1, 1:-1, 2:] + inward_weight * padded[..., 1:-1, 1:-1, :-2]
    azimuthal = arc_weight * (padded[..., 1:-1, 2:, 1:-1] + padded[..., 1:-1, :-2, 1:-1])
    vertical = padded[..., 2:, 1:-1, 1:-1] + padded[..., :-2, 1:-1, 1:-1]
    return radial + azimuthal + vertical - center_weight * center


def chemical(density, grains):
    square_sum = jnp.sum(grains * grains, axis=0)
    cube_sum = jnp.sum(grains * grains * grains, axis=0)
    bulk_drive = 2.0 * bulk_weight * density * (1.0 - density) * (
        1.0 - 2.0 * density
    ) + grain_weight * (2.0 * density - 6.0 * square_sum + 4.0 * cube_sum)
    grain_drive = (
        12.0
        * grain_weight
        * (grains * (1.0 - density) - grains * grains * (2.0 - density) + grains * square_sum)
    )
    return (bulk_drive, grain_drive)


def reach():
    need_lc, need_lg = [0], [0]
    for moment in range(STEPS):
        need_lc.append(need_lc[-1] + 2)
        need_lg.append(max(need_lg[-1] + 1, need_lc[moment]))
    need_d, need_e = [need_lc[STEPS]], [-1]
    for moment in range(STEPS - 1, -1, -1):
        pot_width = need_d[0] + 1
        need_d.insert(0, max(pot_width + 1, need_e[0], need_lc[moment]))
        need_e.insert(0, max(pot_width, need_e[0] + 1, need_lc[moment]))
    return need_d, need_e, need_lc, need_lg


def chemical_pullback(density, grains, copotential, codrive):
    square_sum = jnp.sum(grains * grains, axis=0)
    grain_square = grains * grains
    drive_slope = 12.0 * grain_weight * (grain_square - grains)
    bulk_slope = 2.0 * bulk_weight * (1.0 - 6.0 * density + 6.0 * density * density) + 2.0 * grain_weight
    if codrive is None:
        return copotential * bulk_slope, copotential * drive_slope
    pull_density = copotential * bulk_slope + jnp.sum(codrive * drive_slope, axis=0)
    coupling = jnp.sum(codrive * grains, axis=0)
    pull_grains = (
        copotential * drive_slope
        + 12.0 * grain_weight * codrive * ((1.0 - density) - 2.0 * grains * (2.0 - density) + square_sum)
        + 24.0 * grain_weight * grains * coupling
    )
    return pull_density, pull_grains


def shards(density, labels, observed, measured):
    height_rows, azim_rows, radius_rows = density.shape
    total_hgt = height_rows * lax.axis_size("hgt")
    part = radius_rows // lax.axis_size("hgt")
    geometry = (
        lax.axis_index("rad") * radius_rows + lax.axis_index("hgt") * part,
        total_hgt,
        azim_rows * lax.axis_size("azim"),
        radius_rows * lax.axis_size("rad"),
        part,
    )
    field = lax.broadcasted_iota(jnp.int32, (4,) + density.shape, 0)
    packed = jnp.where(
        field == 0,
        density[None],
        jnp.where(
            field == 1,
            labels[None].astype(jnp.float32),
            jnp.where(field == 2, observed[None], measured[None].astype(jnp.float32)),
        ),
    )
    if lax.axis_size("hgt") == 2:
        received = edge_columns(packed, HALO)
        packed = two_core_window(gather_axis(packed, "hgt", 1), received, HALO)
    else:
        packed = chip_window(gather_axis(packed, "hgt", 1), HALO)
    need_d, need_e, need_lc, need_lg = reach()
    widths = (need_d[0], need_e[0], need_lc[STEPS], need_lc[STEPS])
    trim = lambda f, w: f[..., HALO - w : f.shape[-1] - (HALO - w)]
    density, grain_label = [
        trim(f, w) for f, w in zip(azim_exchange([packed[0], packed[1]], widths[:2]), widths[:2])
    ]
    misfit_terms, density = lax.optimization_barrier((packed[2:], density))
    observed, measured = [
        trim(f, w) for f, w in zip(azim_exchange([misfit_terms[0], misfit_terms[1]], widths[2:]), widths[2:])
    ]
    grains = (
        grain_label[None] == jnp.arange(GRAINS, dtype=jnp.float32)[:, None, None, None]
    ).astype(jnp.float32)
    need_d, need_e, need_lc, need_lg = reach()
    density = in_domain(density, need_d[0], geometry)
    grains = in_domain(grains, need_e[0], geometry)
    history = []
    for moment in range(STEPS):
        d_width, e_width = need_d[moment], need_e[moment]
        history.append((density, d_width, grains, e_width))
        pot_width = need_d[moment + 1] + 1
        next_e = need_e[moment + 1]
        both = max(pot_width, next_e)
        bulk_drive, grain_drive = chemical(crop(density, d_width, both), crop(grains, e_width, both))
        potential = crop(bulk_drive, both, pot_width) - cahn_gradient * laplace(
            crop(density, d_width, pot_width + 1), pot_width + 1, geometry, False
        )
        flux_term = laplace(potential, pot_width, geometry, False)
        new_density = crop(density, d_width, need_d[moment + 1]) + cahn_step * flux_term
        if next_e >= 0:
            grain_spread = laplace(crop(grains, e_width, next_e + 1), next_e + 1, geometry, False)
            new_grains = crop(grains, e_width, next_e) - allen_step * (
                crop(grain_drive, both, next_e) - allen_gradient * grain_spread
            )
            grains = in_domain(new_grains, next_e, geometry)
        density = in_domain(new_density, need_d[moment + 1], geometry)
    d_width = need_d[STEPS]

    observed = crop(observed, widths[2], d_width)
    measured = crop(measured, widths[3], d_width)
    costate = in_domain(measured * (density - observed), d_width, geometry)
    c_width = d_width
    last_density = crop(density, d_width, 0)
    cograins, cg_width = None, None
    for moment in range(STEPS - 1, -1, -1):
        fields_density, fd_width, fields_grains, fg_width = history[moment]
        point = need_lc[moment]
        nu_width = point + 1
        copotential = cahn_step * laplace(crop(costate, c_width, nu_width + 1), nu_width + 1, geometry, True)
        here_density = crop(fields_density, fd_width, point)
        here_grains = crop(fields_grains, fg_width, point)
        here_copotential = crop(copotential, nu_width, point)
        if cograins is None:
            pull_density, pull_grains = chemical_pullback(
                here_density, here_grains, here_copotential, None
            )
        else:
            pull_density, pull_grains = chemical_pullback(
                here_density, here_grains, here_copotential, -allen_step * crop(cograins, cg_width, point)
            )
        reaction = laplace(in_domain(copotential, nu_width, geometry), nu_width, geometry, True)
        new_costate = crop(costate, c_width, point) + pull_density - cahn_gradient * reaction
        new_cg_width = need_lg[moment]
        if cograins is None:
            new_cograins = crop(pull_grains, point, new_cg_width)
        else:
            grain_spread = laplace(
                crop(cograins, cg_width, new_cg_width + 1), new_cg_width + 1, geometry, True
            )
            new_cograins = (
                crop(cograins, cg_width, new_cg_width)
                + crop(pull_grains, point, new_cg_width)
                + allen_step * allen_gradient * grain_spread
            )
        costate, c_width = in_domain(new_costate, point, geometry), point
        cograins, cg_width = in_domain(new_cograins, new_cg_width, geometry), new_cg_width

    costate = crop(costate, c_width, 0)
    cograins = crop(cograins, cg_width, 0)
    last_density, costate, cograins = scatter_heights(
        jnp.concatenate([last_density[None], costate[None], cograins], axis=0),
        height_rows,
        ((0, 1), (1, 2), (2, 2 + GRAINS)),
    )
    return (last_density[0], costate[0], cograins)


def solution(mesh):
    in_specs = (
        P("hgt", "azim", "rad"),
        P("hgt", "azim", "rad"),
        P("hgt", "azim", "rad"),
        P("hgt", "azim", "rad"),
    )
    out_specs = (P("hgt", "azim", "rad"), P("hgt", "azim", "rad"), P(None, "hgt", "azim", "rad"))
    return jax.shard_map(shards, mesh=mesh, in_specs=in_specs, out_specs=out_specs, check_vma=False)
```

```python
import jax
import jax.numpy as jnp
from jax import lax
from jax.sharding import PartitionSpec as P

STEPS = 3
GRAINS = 4


bulk_weight = 16.0
grain_weight = 1.0
cahn_step = 0.005
allen_step = 0.05
cahn_gradient = 1.0
allen_gradient = 1.0
full_turn = 6.283185307179586

HALO = 4 * STEPS


def halo_exchange(block, axis, dim, width, cyclic):
    peers, length = (lax.axis_size(axis), block.shape[dim])
    up = [(i, (i + 1) % peers) for i in range(peers) if cyclic or i + 1 < peers]
    down = [(j, i) for i, j in up]
    last = lax.slice_in_dim(block, length - width, length, axis=dim)
    leading = lax.slice_in_dim(block, 0, width, axis=dim)
    before = lax.ppermute(last, axis, up)
    after = lax.ppermute(leading, axis, down)
    return jnp.concatenate([before, block, after], axis=dim)


def azim_exchange(fields, widths):
    peers = lax.axis_size("azim")
    up = [(i, (i + 1) % peers) for i in range(peers)]
    down = [(j, i) for i, j in up]
    rows = fields[0].shape[-2]
    last = jnp.concatenate([f[..., rows - w :, :] for f, w in zip(fields, widths)], axis=-2)
    leading = jnp.concatenate([f[..., :w, :] for f, w in zip(fields, widths)], axis=-2)
    before = lax.ppermute(last, "azim", up)
    after = lax.ppermute(leading, "azim", down)
    out, at = [], 0
    for f, w in zip(fields, widths):
        out.append(jnp.concatenate([before[..., at : at + w, :], f, after[..., at : at + w, :]], axis=-2))
        at += w
    return out


def gather_axis(block, axis, dim):
    peers = lax.axis_size(axis)
    if peers == 1:
        return block
    own = lax.axis_index(axis)
    parts = [block]
    for shift in range(1, peers):
        parts.append(lax.ppermute(block, axis, [(i, (i + shift) % peers) for i in range(peers)]))
    if peers == 2:
        return jnp.where(
            own == 0,
            jnp.concatenate([parts[0], parts[1]], axis=dim),
            jnp.concatenate([parts[1], parts[0]], axis=dim),
        )
    stacked = jnp.stack(parts)
    order = (own - jnp.arange(peers, dtype=jnp.int32)) % peers
    ordered = jnp.take(stacked, order, axis=0)
    ordered = jnp.moveaxis(ordered, 0, dim)
    shape = list(block.shape)
    shape[dim] = shape[dim] * peers
    return ordered.reshape(shape)


def chip_window(block, width):
    peers, own, rad_peers = (lax.axis_size("hgt"), lax.axis_index("hgt"), lax.axis_size("rad"))
    cols = block.shape[-1]
    part = cols // peers
    piece = jnp.where(own == 0, block[..., :width], block[..., cols - width :])
    pairs = []
    for r in range(rad_peers - 1):
        pairs.append((r * peers + peers - 1, (r + 1) * peers))
        pairs.append(((r + 1) * peers, r * peers + peers - 1))
    received = lax.ppermute(piece, ("rad", "hgt"), pairs)
    padded = jnp.concatenate([received, block, received], axis=-1)
    return lax.dynamic_slice_in_dim(padded, own * part, part + 2 * width, axis=padded.ndim - 1)


def edge_columns(block, width):
    own, rad_peers = (lax.axis_index("hgt"), lax.axis_size("rad"))
    cols = block.shape[-1]
    first, last = (block[..., :width], block[..., cols - width :])
    cross, same = ([], [])
    for r in range(rad_peers - 1):
        cross += [(2 * r + 1, 2 * r + 2), (2 * r + 2, 2 * r + 1)]
        same += [(2 * r, 2 * r + 2), (2 * r + 3, 2 * r + 1)]
    from_cross = lax.ppermute(jnp.where(own == 0, first, last), ("rad", "hgt"), cross)
    from_same = lax.ppermute(jnp.where(own == 0, last, first), ("rad", "hgt"), same)
    return jnp.where(
        own == 0,
        jnp.concatenate([from_same, from_cross], axis=1),
        jnp.concatenate([from_cross, from_same], axis=1),
    )


def two_core_window(block, received, width):
    own = lax.axis_index("hgt")
    part = block.shape[-1] // 2
    padded = jnp.concatenate([received, block, received], axis=-1)
    return lax.dynamic_slice_in_dim(padded, own * part, part + 2 * width, axis=padded.ndim - 1)


def scatter_heights(x, height_rows):
    peers, own = (lax.axis_size("hgt"), lax.axis_index("hgt"))
    parts = []
    for shift in range(peers):
        dest = (own + shift) % peers
        piece = lax.dynamic_slice_in_dim(x, dest * height_rows, height_rows, axis=1)
        if shift:
            piece = lax.ppermute(piece, "hgt", [(i, (i + shift) % peers) for i in range(peers)])
        parts.append(piece)
    if peers == 2:
        return jnp.where(
            own == 0,
            jnp.concatenate([parts[0], parts[1]], axis=-1),
            jnp.concatenate([parts[1], parts[0]], axis=-1),
        )
    stacked = jnp.stack(parts)
    order = (own - jnp.arange(peers, dtype=jnp.int32)) % peers
    ordered = jnp.moveaxis(jnp.take(stacked, order, axis=0), 0, -2)
    shape = ordered.shape
    return ordered.reshape(shape[:-2] + (shape[-2] * shape[-1],))


def crop(x, width, new_width):
    cut = width - new_width
    if cut == 0:
        return x
    return x[..., cut : x.shape[-2] - cut, cut : x.shape[-1] - cut]


def radial_mask(width, geometry):
    rad_start, total_hgt, total_azim, total_rad, cols = geometry
    rad_index = rad_start - width + jnp.arange(cols + 2 * width, dtype=jnp.int32)
    return (rad_index >= 0) & (rad_index < total_rad)


def in_domain(x, width, geometry):
    return jnp.where(radial_mask(width, geometry), x, 0.0)


def laplace(x, width, geometry, transpose):
    rad_start, total_hgt, total_azim, total_rad, cols = geometry
    margin = width - 1
    height_rows = x.shape[-3]
    radius_rows = x.shape[-1] - 2
    rad_index_all = rad_start - margin - 1 + jnp.arange(radius_rows + 2, dtype=jnp.int32)
    radius_all = total_azim / full_turn + rad_index_all.astype(jnp.float32) + 0.5
    rad_index = rad_index_all[1:-1]
    radius = radius_all[1:-1]
    outer_face = (radius + 0.5) * (rad_index < total_rad - 1).astype(jnp.float32)
    inner_face = (radius - 0.5) * (rad_index > 0).astype(jnp.float32)
    if transpose:
        outward_weight = outer_face / radius_all[2:]
        inward_weight = inner_face / radius_all[:-2]
    else:
        outward_weight = outer_face / radius
        inward_weight = inner_face / radius
    arc_length = radius * (full_turn / total_azim)
    arc_weight = 1.0 / (arc_length * arc_length)
    hgt_index = jnp.arange(height_rows, dtype=jnp.int32)
    faces = (hgt_index < total_hgt - 1).astype(jnp.float32) + (hgt_index > 0).astype(jnp.float32)
    center_weight = (outer_face + inner_face) / radius + 2.0 * arc_weight + faces[:, None, None]
    leading = x.ndim - 3
    padded = jnp.pad(x, [(0, 0)] * leading + [(1, 1), (0, 0), (0, 0)])
    center = padded[..., 1:-1, 1:-1, 1:-1]
    radial = outward_weight * padded[..., 1:-1, 1:-1, 2:] + inward_weight * padded[..., 1:-1, 1:-1, :-2]
    azimuthal = arc_weight * (padded[..., 1:-1, 2:, 1:-1] + padded[..., 1:-1, :-2, 1:-1])
    vertical = padded[..., 2:, 1:-1, 1:-1] + padded[..., :-2, 1:-1, 1:-1]
    return radial + azimuthal + vertical - center_weight * center


def chemical(density, grains):
    square_sum = jnp.sum(grains * grains, axis=0)
    cube_sum = jnp.sum(grains * grains * grains, axis=0)
    bulk_drive = 2.0 * bulk_weight * density * (1.0 - density) * (
        1.0 - 2.0 * density
    ) + grain_weight * (2.0 * density - 6.0 * square_sum + 4.0 * cube_sum)
    grain_drive = (
        12.0
        * grain_weight
        * (grains * (1.0 - density) - grains * grains * (2.0 - density) + grains * square_sum)
    )
    return (bulk_drive, grain_drive)


def reach():
    need_lc, need_lg = [0], [0]
    for moment in range(STEPS):
        need_lc.append(need_lc[-1] + 2)
        need_lg.append(max(need_lg[-1] + 1, need_lc[moment]))
    need_d, need_e = [need_lc[STEPS]], [-1]
    for moment in range(STEPS - 1, -1, -1):
        pot_width = need_d[0] + 1
        need_d.insert(0, max(pot_width + 1, need_e[0], need_lc[moment]))
        need_e.insert(0, max(pot_width, need_e[0] + 1, need_lc[moment]))
    return need_d, need_e, need_lc, need_lg


def chemical_pullback(density, grains, copotential, codrive):
    square_sum = jnp.sum(grains * grains, axis=0)
    grain_square = grains * grains
    drive_slope = 12.0 * grain_weight * (grain_square - grains)
    bulk_slope = 2.0 * bulk_weight * (1.0 - 6.0 * density + 6.0 * density * density) + 2.0 * grain_weight
    if codrive is None:
        return copotential * bulk_slope, copotential * drive_slope
    pull_density = copotential * bulk_slope + jnp.sum(codrive * drive_slope, axis=0)
    coupling = jnp.sum(codrive * grains, axis=0)
    pull_grains = (
        copotential * drive_slope
        + 12.0 * grain_weight * codrive * ((1.0 - density) - 2.0 * grains * (2.0 - density) + square_sum)
        + 24.0 * grain_weight * grains * coupling
    )
    return pull_density, pull_grains


def shards(density, labels, observed, measured):
    height_rows, azim_rows, radius_rows = density.shape
    total_hgt = height_rows * lax.axis_size("hgt")
    part = radius_rows // lax.axis_size("hgt")
    geometry = (
        lax.axis_index("rad") * radius_rows + lax.axis_index("hgt") * part,
        total_hgt,
        azim_rows * lax.axis_size("azim"),
        radius_rows * lax.axis_size("rad"),
        part,
    )
    packed = jnp.stack([density, labels.astype(jnp.float32), observed, measured.astype(jnp.float32)])
    if lax.axis_size("hgt") == 2:
        received = edge_columns(packed, HALO)
        packed = two_core_window(gather_axis(packed, "hgt", 1), received, HALO)
    else:
        packed = chip_window(gather_axis(packed, "hgt", 1), HALO)
    need_d, need_e, need_lc, need_lg = reach()
    widths = (need_d[0], need_e[0], need_lc[STEPS], need_lc[STEPS])
    trim = lambda f, w: f[..., HALO - w : f.shape[-1] - (HALO - w)]
    density, grain_label = [
        trim(f, w) for f, w in zip(azim_exchange([packed[0], packed[1]], widths[:2]), widths[:2])
    ]
    misfit_terms, density = lax.optimization_barrier((packed[2:], density))
    observed, measured = [
        trim(f, w) for f, w in zip(azim_exchange([misfit_terms[0], misfit_terms[1]], widths[2:]), widths[2:])
    ]
    grains = (
        grain_label[None] == jnp.arange(GRAINS, dtype=jnp.float32)[:, None, None, None]
    ).astype(jnp.float32)
    need_d, need_e, need_lc, need_lg = reach()
    density = in_domain(density, need_d[0], geometry)
    grains = in_domain(grains, need_e[0], geometry)
    history = []
    for moment in range(STEPS):
        d_width, e_width = need_d[moment], need_e[moment]
        history.append((density, d_width, grains, e_width))
        pot_width = need_d[moment + 1] + 1
        next_e = need_e[moment + 1]
        both = max(pot_width, next_e)
        bulk_drive, grain_drive = chemical(crop(density, d_width, both), crop(grains, e_width, both))
        potential = crop(bulk_drive, both, pot_width) - cahn_gradient * laplace(
            crop(density, d_width, pot_width + 1), pot_width + 1, geometry, False
        )
        flux_term = laplace(potential, pot_width, geometry, False)
        new_density = crop(density, d_width, need_d[moment + 1]) + cahn_step * flux_term
        if next_e >= 0:
            grain_spread = laplace(crop(grains, e_width, next_e + 1), next_e + 1, geometry, False)
            new_grains = crop(grains, e_width, next_e) - allen_step * (
                crop(grain_drive, both, next_e) - allen_gradient * grain_spread
            )
            grains = lax.optimization_barrier(in_domain(new_grains, next_e, geometry))
        density = in_domain(new_density, need_d[moment + 1], geometry)
    d_width = need_d[STEPS]

    observed = crop(observed, widths[2], d_width)
    measured = crop(measured, widths[3], d_width)
    costate = in_domain(measured * (density - observed), d_width, geometry)
    c_width = d_width
    last_density = crop(density, d_width, 0)
    cograins, cg_width = None, None
    for moment in range(STEPS - 1, -1, -1):
        fields_density, fd_width, fields_grains, fg_width = history[moment]
        point = need_lc[moment]
        nu_width = point + 1
        copotential = cahn_step * laplace(crop(costate, c_width, nu_width + 1), nu_width + 1, geometry, True)
        here_density = crop(fields_density, fd_width, point)
        here_grains = crop(fields_grains, fg_width, point)
        here_copotential = crop(copotential, nu_width, point)
        if cograins is None:
            pull_density, pull_grains = chemical_pullback(
                here_density, here_grains, here_copotential, None
            )
        else:
            pull_density, pull_grains = chemical_pullback(
                here_density, here_grains, here_copotential, -allen_step * crop(cograins, cg_width, point)
            )
        reaction = laplace(in_domain(copotential, nu_width, geometry), nu_width, geometry, True)
        new_costate = crop(costate, c_width, point) + pull_density - cahn_gradient * reaction
        new_cg_width = need_lg[moment]
        if cograins is None:
            new_cograins = crop(pull_grains, point, new_cg_width)
        else:
            grain_spread = laplace(
                crop(cograins, cg_width, new_cg_width + 1), new_cg_width + 1, geometry, True
            )
            new_cograins = (
                crop(cograins, cg_width, new_cg_width)
                + crop(pull_grains, point, new_cg_width)
                + allen_step * allen_gradient * grain_spread
            )
        costate, c_width = in_domain(new_costate, point, geometry), point
        cograins, cg_width = in_domain(new_cograins, new_cg_width, geometry), new_cg_width

    costate = crop(costate, c_width, 0)
    cograins = crop(cograins, cg_width, 0)
    result = scatter_heights(
        jnp.concatenate([last_density[None], costate[None], cograins], axis=0), height_rows
    )
    return (result[0], result[1], result[2:])


def solution(mesh):
    in_specs = (
        P("hgt", "azim", "rad"),
        P("hgt", "azim", "rad"),
        P("hgt", "azim", "rad"),
        P("hgt", "azim", "rad"),
    )
    out_specs = (P("hgt", "azim", "rad"), P("hgt", "azim", "rad"), P(None, "hgt", "azim", "rad"))
    return jax.shard_map(shards, mesh=mesh, in_specs=in_specs, out_specs=out_specs, check_vma=False)
```

```python
import jax
import jax.numpy as jnp
from jax import lax
from jax.sharding import PartitionSpec as P

STEPS = 3
GRAINS = 4


bulk_weight = 16.0
grain_weight = 1.0
cahn_step = 0.005
allen_step = 0.05
cahn_gradient = 1.0
allen_gradient = 1.0
full_turn = 6.283185307179586

HALO = 4 * STEPS


def halo_exchange(block, axis, dim, width, cyclic):
    peers, length = (lax.axis_size(axis), block.shape[dim])
    up = [(i, (i + 1) % peers) for i in range(peers) if cyclic or i + 1 < peers]
    down = [(j, i) for i, j in up]
    last = lax.slice_in_dim(block, length - width, length, axis=dim)
    leading = lax.slice_in_dim(block, 0, width, axis=dim)
    before = lax.ppermute(last, axis, up)
    after = lax.ppermute(leading, axis, down)
    return jnp.concatenate([before, block, after], axis=dim)


def azim_exchange(fields, widths):
    peers = lax.axis_size("azim")
    up = [(i, (i + 1) % peers) for i in range(peers)]
    down = [(j, i) for i, j in up]
    rows = fields[0].shape[-2]
    last = jnp.concatenate([f[..., rows - w :, :] for f, w in zip(fields, widths)], axis=-2)
    leading = jnp.concatenate([f[..., :w, :] for f, w in zip(fields, widths)], axis=-2)
    before = lax.ppermute(last, "azim", up)
    after = lax.ppermute(leading, "azim", down)
    out, at = [], 0
    for f, w in zip(fields, widths):
        out.append(jnp.concatenate([before[..., at : at + w, :], f, after[..., at : at + w, :]], axis=-2))
        at += w
    return out


def gather_axis(block, axis, dim):
    peers = lax.axis_size(axis)
    if peers == 1:
        return block
    own = lax.axis_index(axis)
    parts = [block]
    for shift in range(1, peers):
        parts.append(lax.ppermute(block, axis, [(i, (i + shift) % peers) for i in range(peers)]))
    if peers == 2:
        return jnp.where(
            own == 0,
            jnp.concatenate([parts[0], parts[1]], axis=dim),
            jnp.concatenate([parts[1], parts[0]], axis=dim),
        )
    stacked = jnp.stack(parts)
    order = (own - jnp.arange(peers, dtype=jnp.int32)) % peers
    ordered = jnp.take(stacked, order, axis=0)
    ordered = jnp.moveaxis(ordered, 0, dim)
    shape = list(block.shape)
    shape[dim] = shape[dim] * peers
    return ordered.reshape(shape)


def chip_window(block, width):
    peers, own, rad_peers = (lax.axis_size("hgt"), lax.axis_index("hgt"), lax.axis_size("rad"))
    cols = block.shape[-1]
    part = cols // peers
    piece = jnp.where(own == 0, block[..., :width], block[..., cols - width :])
    pairs = []
    for r in range(rad_peers - 1):
        pairs.append((r * peers + peers - 1, (r + 1) * peers))
        pairs.append(((r + 1) * peers, r * peers + peers - 1))
    received = lax.ppermute(piece, ("rad", "hgt"), pairs)
    padded = jnp.concatenate([received, block, received], axis=-1)
    return lax.dynamic_slice_in_dim(padded, own * part, part + 2 * width, axis=padded.ndim - 1)


def edge_columns(block, width):
    own, rad_peers = (lax.axis_index("hgt"), lax.axis_size("rad"))
    cols = block.shape[-1]
    first, last = (block[..., :width], block[..., cols - width :])
    cross, same = ([], [])
    for r in range(rad_peers - 1):
        cross += [(2 * r + 1, 2 * r + 2), (2 * r + 2, 2 * r + 1)]
        same += [(2 * r, 2 * r + 2), (2 * r + 3, 2 * r + 1)]
    from_cross = lax.ppermute(jnp.where(own == 0, first, last), ("rad", "hgt"), cross)
    from_same = lax.ppermute(jnp.where(own == 0, last, first), ("rad", "hgt"), same)
    return jnp.where(
        own == 0,
        jnp.concatenate([from_same, from_cross], axis=1),
        jnp.concatenate([from_cross, from_same], axis=1),
    )


def two_core_window(block, received, width):
    own = lax.axis_index("hgt")
    part = block.shape[-1] // 2
    padded = jnp.concatenate([received, block, received], axis=-1)
    return lax.dynamic_slice_in_dim(padded, own * part, part + 2 * width, axis=padded.ndim - 1)


def scatter_heights(x, height_rows):
    peers, own = (lax.axis_size("hgt"), lax.axis_index("hgt"))
    parts = []
    for shift in range(peers):
        dest = (own + shift) % peers
        piece = lax.dynamic_slice_in_dim(x, dest * height_rows, height_rows, axis=1)
        if shift:
            piece = lax.ppermute(piece, "hgt", [(i, (i + shift) % peers) for i in range(peers)])
        parts.append(piece)
    if peers == 2:
        return jnp.where(
            own == 0,
            jnp.concatenate([parts[0], parts[1]], axis=-1),
            jnp.concatenate([parts[1], parts[0]], axis=-1),
        )
    stacked = jnp.stack(parts)
    order = (own - jnp.arange(peers, dtype=jnp.int32)) % peers
    ordered = jnp.moveaxis(jnp.take(stacked, order, axis=0), 0, -2)
    shape = ordered.shape
    return ordered.reshape(shape[:-2] + (shape[-2] * shape[-1],))


def crop(x, width, new_width):
    cut = width - new_width
    if cut == 0:
        return x
    return x[..., cut : x.shape[-2] - cut, cut : x.shape[-1] - cut]


def radial_mask(width, geometry):
    rad_start, total_hgt, total_azim, total_rad, cols = geometry
    rad_index = rad_start - width + jnp.arange(cols + 2 * width, dtype=jnp.int32)
    return (rad_index >= 0) & (rad_index < total_rad)


def in_domain(x, width, geometry):
    return jnp.where(radial_mask(width, geometry), x, 0.0)


def laplace(x, width, geometry, transpose):
    rad_start, total_hgt, total_azim, total_rad, cols = geometry
    margin = width - 1
    height_rows = x.shape[-3]
    radius_rows = x.shape[-1] - 2
    rad_index_all = rad_start - margin - 1 + jnp.arange(radius_rows + 2, dtype=jnp.int32)
    radius_all = total_azim / full_turn + rad_index_all.astype(jnp.float32) + 0.5
    rad_index = rad_index_all[1:-1]
    radius = radius_all[1:-1]
    outer_face = (radius + 0.5) * (rad_index < total_rad - 1).astype(jnp.float32)
    inner_face = (radius - 0.5) * (rad_index > 0).astype(jnp.float32)
    if transpose:
        outward_weight = outer_face / radius_all[2:]
        inward_weight = inner_face / radius_all[:-2]
    else:
        outward_weight = outer_face / radius
        inward_weight = inner_face / radius
    arc_length = radius * (full_turn / total_azim)
    arc_weight = 1.0 / (arc_length * arc_length)
    hgt_index = jnp.arange(height_rows, dtype=jnp.int32)
    faces = (hgt_index < total_hgt - 1).astype(jnp.float32) + (hgt_index > 0).astype(jnp.float32)
    center_weight = (outer_face + inner_face) / radius + 2.0 * arc_weight + faces[:, None, None]
    leading = x.ndim - 3
    padded = jnp.pad(x, [(0, 0)] * leading + [(1, 1), (0, 0), (0, 0)])
    center = padded[..., 1:-1, 1:-1, 1:-1]
    radial = outward_weight * padded[..., 1:-1, 1:-1, 2:] + inward_weight * padded[..., 1:-1, 1:-1, :-2]
    azimuthal = arc_weight * (padded[..., 1:-1, 2:, 1:-1] + padded[..., 1:-1, :-2, 1:-1])
    vertical = padded[..., 2:, 1:-1, 1:-1] + padded[..., :-2, 1:-1, 1:-1]
    return radial + azimuthal + vertical - center_weight * center


def chemical(density, grains):
    square_sum = jnp.sum(grains * grains, axis=0)
    cube_sum = jnp.sum(grains * grains * grains, axis=0)
    bulk_drive = 2.0 * bulk_weight * density * (1.0 - density) * (
        1.0 - 2.0 * density
    ) + grain_weight * (2.0 * density - 6.0 * square_sum + 4.0 * cube_sum)
    grain_drive = (
        12.0
        * grain_weight
        * (grains * (1.0 - density) - grains * grains * (2.0 - density) + grains * square_sum)
    )
    return (bulk_drive, grain_drive)


def reach():
    need_lc, need_lg = [0], [0]
    for moment in range(STEPS):
        need_lc.append(need_lc[-1] + 2)
        need_lg.append(max(need_lg[-1] + 1, need_lc[moment]))
    need_d, need_e = [need_lc[STEPS]], [-1]
    for moment in range(STEPS - 1, -1, -1):
        pot_width = need_d[0] + 1
        need_d.insert(0, max(pot_width + 1, need_e[0], need_lc[moment]))
        need_e.insert(0, max(pot_width, need_e[0] + 1, need_lc[moment]))
    return need_d, need_e, need_lc, need_lg


def chemical_pullback(density, grains, copotential, codrive):
    square_sum = jnp.sum(grains * grains, axis=0)
    grain_square = grains * grains
    drive_slope = 12.0 * grain_weight * (grain_square - grains)
    bulk_slope = 2.0 * bulk_weight * (1.0 - 6.0 * density + 6.0 * density * density) + 2.0 * grain_weight
    if codrive is None:
        return copotential * bulk_slope, copotential * drive_slope
    pull_density = copotential * bulk_slope + jnp.sum(codrive * drive_slope, axis=0)
    coupling = jnp.sum(codrive * grains, axis=0)
    pull_grains = (
        copotential * drive_slope
        + 12.0 * grain_weight * codrive * ((1.0 - density) - 2.0 * grains * (2.0 - density) + square_sum)
        + 24.0 * grain_weight * grains * coupling
    )
    return pull_density, pull_grains


def shards(density, labels, observed, measured):
    height_rows, azim_rows, radius_rows = density.shape
    total_hgt = height_rows * lax.axis_size("hgt")
    part = radius_rows // lax.axis_size("hgt")
    geometry = (
        lax.axis_index("rad") * radius_rows + lax.axis_index("hgt") * part,
        total_hgt,
        azim_rows * lax.axis_size("azim"),
        radius_rows * lax.axis_size("rad"),
        part,
    )
    packed = jnp.stack([density, labels.astype(jnp.float32), observed, measured.astype(jnp.float32)])
    if lax.axis_size("hgt") == 2:
        received = edge_columns(packed, HALO)
        packed = two_core_window(gather_axis(packed, "hgt", 1), received, HALO)
    else:
        packed = chip_window(gather_axis(packed, "hgt", 1), HALO)
    need_d, need_e, need_lc, need_lg = reach()
    widths = (need_d[0], need_e[0], need_lc[STEPS], need_lc[STEPS])
    trim = lambda f, w: f[..., HALO - w : f.shape[-1] - (HALO - w)]
    density, grain_label = [
        trim(f, w) for f, w in zip(azim_exchange([packed[0], packed[1]], widths[:2]), widths[:2])
    ]
    misfit_terms = packed[2:]
    grains = (
        grain_label[None] == jnp.arange(GRAINS, dtype=jnp.float32)[:, None, None, None]
    ).astype(jnp.float32)
    need_d, need_e, need_lc, need_lg = reach()
    density = in_domain(density, need_d[0], geometry)
    grains = in_domain(grains, need_e[0], geometry)
    history = []
    for moment in range(STEPS):
        d_width, e_width = need_d[moment], need_e[moment]
        history.append((density, d_width, grains, e_width))
        pot_width = need_d[moment + 1] + 1
        next_e = need_e[moment + 1]
        both = max(pot_width, next_e)
        bulk_drive, grain_drive = chemical(crop(density, d_width, both), crop(grains, e_width, both))
        potential = crop(bulk_drive, both, pot_width) - cahn_gradient * laplace(
            crop(density, d_width, pot_width + 1), pot_width + 1, geometry, False
        )
        flux_term = laplace(potential, pot_width, geometry, False)
        new_density = crop(density, d_width, need_d[moment + 1]) + cahn_step * flux_term
        if next_e >= 0:
            grain_spread = laplace(crop(grains, e_width, next_e + 1), next_e + 1, geometry, False)
            new_grains = crop(grains, e_width, next_e) - allen_step * (
                crop(grain_drive, both, next_e) - allen_gradient * grain_spread
            )
            grains = in_domain(new_grains, next_e, geometry)
        density = in_domain(new_density, need_d[moment + 1], geometry)
        if moment == 0:
            misfit_terms, marker = lax.optimization_barrier((misfit_terms, density[0, 0, 0]))
            observed, measured = [
                trim(f, w)
                for f, w in zip(azim_exchange([misfit_terms[0], misfit_terms[1]], widths[2:]), widths[2:])
            ]
    d_width = need_d[STEPS]

    observed = crop(observed, widths[2], d_width)
    measured = crop(measured, widths[3], d_width)
    costate = in_domain(measured * (density - observed), d_width, geometry)
    c_width = d_width
    last_density = crop(density, d_width, 0)
    cograins, cg_width = None, None
    for moment in range(STEPS - 1, -1, -1):
        fields_density, fd_width, fields_grains, fg_width = history[moment]
        point = need_lc[moment]
        nu_width = point + 1
        copotential = cahn_step * laplace(crop(costate, c_width, nu_width + 1), nu_width + 1, geometry, True)
        here_density = crop(fields_density, fd_width, point)
        here_grains = crop(fields_grains, fg_width, point)
        here_copotential = crop(copotential, nu_width, point)
        if cograins is None:
            pull_density, pull_grains = chemical_pullback(
                here_density, here_grains, here_copotential, None
            )
        else:
            pull_density, pull_grains = chemical_pullback(
                here_density, here_grains, here_copotential, -allen_step * crop(cograins, cg_width, point)
            )
        reaction = laplace(in_domain(copotential, nu_width, geometry), nu_width, geometry, True)
        new_costate = crop(costate, c_width, point) + pull_density - cahn_gradient * reaction
        new_cg_width = need_lg[moment]
        if cograins is None:
            new_cograins = crop(pull_grains, point, new_cg_width)
        else:
            grain_spread = laplace(
                crop(cograins, cg_width, new_cg_width + 1), new_cg_width + 1, geometry, True
            )
            new_cograins = (
                crop(cograins, cg_width, new_cg_width)
                + crop(pull_grains, point, new_cg_width)
                + allen_step * allen_gradient * grain_spread
            )
        costate, c_width = in_domain(new_costate, point, geometry), point
        cograins, cg_width = in_domain(new_cograins, new_cg_width, geometry), new_cg_width

    costate = crop(costate, c_width, 0)
    cograins = crop(cograins, cg_width, 0)
    result = scatter_heights(
        jnp.concatenate([last_density[None], costate[None], cograins], axis=0), height_rows
    )
    return (result[0], result[1], result[2:])


def solution(mesh):
    in_specs = (
        P("hgt", "azim", "rad"),
        P("hgt", "azim", "rad"),
        P("hgt", "azim", "rad"),
        P("hgt", "azim", "rad"),
    )
    out_specs = (P("hgt", "azim", "rad"), P("hgt", "azim", "rad"), P(None, "hgt", "azim", "rad"))
    return jax.shard_map(shards, mesh=mesh, in_specs=in_specs, out_specs=out_specs, check_vma=False)
```

```python
import jax
import jax.numpy as jnp
from jax import lax
from jax.sharding import PartitionSpec as P

STEPS = 3
GRAINS = 4


bulk_weight = 16.0
grain_weight = 1.0
cahn_step = 0.005
allen_step = 0.05
cahn_gradient = 1.0
allen_gradient = 1.0
full_turn = 6.283185307179586

HALO = 4 * STEPS


def halo_exchange(block, axis, dim, width, cyclic):
    peers, length = (lax.axis_size(axis), block.shape[dim])
    up = [(i, (i + 1) % peers) for i in range(peers) if cyclic or i + 1 < peers]
    down = [(j, i) for i, j in up]
    last = lax.slice_in_dim(block, length - width, length, axis=dim)
    leading = lax.slice_in_dim(block, 0, width, axis=dim)
    before = lax.ppermute(last, axis, up)
    after = lax.ppermute(leading, axis, down)
    return jnp.concatenate([before, block, after], axis=dim)


def azim_exchange(fields, widths):
    peers = lax.axis_size("azim")
    up = [(i, (i + 1) % peers) for i in range(peers)]
    down = [(j, i) for i, j in up]
    rows = fields[0].shape[-2]
    last = jnp.concatenate([f[..., rows - w :, :] for f, w in zip(fields, widths)], axis=-2)
    leading = jnp.concatenate([f[..., :w, :] for f, w in zip(fields, widths)], axis=-2)
    before = lax.ppermute(last, "azim", up)
    after = lax.ppermute(leading, "azim", down)
    out, at = [], 0
    for f, w in zip(fields, widths):
        out.append(jnp.concatenate([before[..., at : at + w, :], f, after[..., at : at + w, :]], axis=-2))
        at += w
    return out


def gather_axis(block, axis, dim):
    peers = lax.axis_size(axis)
    if peers == 1:
        return block
    own = lax.axis_index(axis)
    parts = [block]
    for shift in range(1, peers):
        parts.append(lax.ppermute(block, axis, [(i, (i + shift) % peers) for i in range(peers)]))
    if peers == 2:
        return jnp.where(
            own == 0,
            jnp.concatenate([parts[0], parts[1]], axis=dim),
            jnp.concatenate([parts[1], parts[0]], axis=dim),
        )
    stacked = jnp.stack(parts)
    order = (own - jnp.arange(peers, dtype=jnp.int32)) % peers
    ordered = jnp.take(stacked, order, axis=0)
    ordered = jnp.moveaxis(ordered, 0, dim)
    shape = list(block.shape)
    shape[dim] = shape[dim] * peers
    return ordered.reshape(shape)


def chip_window(block, width):
    peers, own, rad_peers = (lax.axis_size("hgt"), lax.axis_index("hgt"), lax.axis_size("rad"))
    cols = block.shape[-1]
    part = cols // peers
    piece = jnp.where(own == 0, block[..., :width], block[..., cols - width :])
    pairs = []
    for r in range(rad_peers - 1):
        pairs.append((r * peers + peers - 1, (r + 1) * peers))
        pairs.append(((r + 1) * peers, r * peers + peers - 1))
    received = lax.ppermute(piece, ("rad", "hgt"), pairs)
    padded = jnp.concatenate([received, block, received], axis=-1)
    return lax.dynamic_slice_in_dim(padded, own * part, part + 2 * width, axis=padded.ndim - 1)


def edge_columns(block, width):
    own, rad_peers = (lax.axis_index("hgt"), lax.axis_size("rad"))
    cols = block.shape[-1]
    first, last = (block[..., :width], block[..., cols - width :])
    cross, same = ([], [])
    for r in range(rad_peers - 1):
        cross += [(2 * r + 1, 2 * r + 2), (2 * r + 2, 2 * r + 1)]
        same += [(2 * r, 2 * r + 2), (2 * r + 3, 2 * r + 1)]
    from_cross = lax.ppermute(jnp.where(own == 0, first, last), ("rad", "hgt"), cross)
    from_same = lax.ppermute(jnp.where(own == 0, last, first), ("rad", "hgt"), same)
    return jnp.where(
        own == 0,
        jnp.concatenate([from_same, from_cross], axis=1),
        jnp.concatenate([from_cross, from_same], axis=1),
    )


def two_core_window(block, received, width):
    own = lax.axis_index("hgt")
    part = block.shape[-1] // 2
    padded = jnp.concatenate([received, block, received], axis=-1)
    return lax.dynamic_slice_in_dim(padded, own * part, part + 2 * width, axis=padded.ndim - 1)


def scatter_heights(x, height_rows):
    peers, own = (lax.axis_size("hgt"), lax.axis_index("hgt"))
    parts = []
    for shift in range(peers):
        dest = (own + shift) % peers
        piece = lax.dynamic_slice_in_dim(x, dest * height_rows, height_rows, axis=1)
        if shift:
            piece = lax.ppermute(piece, "hgt", [(i, (i + shift) % peers) for i in range(peers)])
        parts.append(piece)
    if peers == 2:
        return jnp.where(
            own == 0,
            jnp.concatenate([parts[0], parts[1]], axis=-1),
            jnp.concatenate([parts[1], parts[0]], axis=-1),
        )
    stacked = jnp.stack(parts)
    order = (own - jnp.arange(peers, dtype=jnp.int32)) % peers
    ordered = jnp.moveaxis(jnp.take(stacked, order, axis=0), 0, -2)
    shape = ordered.shape
    return ordered.reshape(shape[:-2] + (shape[-2] * shape[-1],))


def crop(x, width, new_width):
    cut = width - new_width
    if cut == 0:
        return x
    return x[..., cut : x.shape[-2] - cut, cut : x.shape[-1] - cut]


def radial_mask(width, geometry):
    rad_start, total_hgt, total_azim, total_rad, cols = geometry
    rad_index = rad_start - width + jnp.arange(cols + 2 * width, dtype=jnp.int32)
    return (rad_index >= 0) & (rad_index < total_rad)


def in_domain(x, width, geometry):
    return jnp.where(radial_mask(width, geometry), x, 0.0)


def laplace(x, width, geometry, transpose):
    rad_start, total_hgt, total_azim, total_rad, cols = geometry
    margin = width - 1
    height_rows = x.shape[-3]
    radius_rows = x.shape[-1] - 2
    rad_index_all = rad_start - margin - 1 + jnp.arange(radius_rows + 2, dtype=jnp.int32)
    radius_all = total_azim / full_turn + rad_index_all.astype(jnp.float32) + 0.5
    rad_index = rad_index_all[1:-1]
    radius = radius_all[1:-1]
    outer_face = (radius + 0.5) * (rad_index < total_rad - 1).astype(jnp.float32)
    inner_face = (radius - 0.5) * (rad_index > 0).astype(jnp.float32)
    if transpose:
        outward_weight = outer_face / radius_all[2:]
        inward_weight = inner_face / radius_all[:-2]
    else:
        outward_weight = outer_face / radius
        inward_weight = inner_face / radius
    arc_length = radius * (full_turn / total_azim)
    arc_weight = 1.0 / (arc_length * arc_length)
    hgt_index = jnp.arange(height_rows, dtype=jnp.int32)
    faces = (hgt_index < total_hgt - 1).astype(jnp.float32) + (hgt_index > 0).astype(jnp.float32)
    center_weight = (outer_face + inner_face) / radius + 2.0 * arc_weight + faces[:, None, None]
    leading = x.ndim - 3
    padded = jnp.pad(x, [(0, 0)] * leading + [(1, 1), (0, 0), (0, 0)])
    center = padded[..., 1:-1, 1:-1, 1:-1]
    radial = outward_weight * padded[..., 1:-1, 1:-1, 2:] + inward_weight * padded[..., 1:-1, 1:-1, :-2]
    azimuthal = arc_weight * (padded[..., 1:-1, 2:, 1:-1] + padded[..., 1:-1, :-2, 1:-1])
    vertical = padded[..., 2:, 1:-1, 1:-1] + padded[..., :-2, 1:-1, 1:-1]
    return radial + azimuthal + vertical - center_weight * center


def chemical(density, grains):
    square_sum = jnp.sum(grains * grains, axis=0)
    cube_sum = jnp.sum(grains * grains * grains, axis=0)
    bulk_drive = 2.0 * bulk_weight * density * (1.0 - density) * (
        1.0 - 2.0 * density
    ) + grain_weight * (2.0 * density - 6.0 * square_sum + 4.0 * cube_sum)
    grain_drive = (
        12.0
        * grain_weight
        * (grains * (1.0 - density) - grains * grains * (2.0 - density) + grains * square_sum)
    )
    return (bulk_drive, grain_drive)


def reach():
    need_lc, need_lg = [0], [0]
    for moment in range(STEPS):
        need_lc.append(need_lc[-1] + 2)
        need_lg.append(max(need_lg[-1] + 1, need_lc[moment]))
    need_d, need_e = [need_lc[STEPS]], [-1]
    for moment in range(STEPS - 1, -1, -1):
        pot_width = need_d[0] + 1
        need_d.insert(0, max(pot_width + 1, need_e[0], need_lc[moment]))
        need_e.insert(0, max(pot_width, need_e[0] + 1, need_lc[moment]))
    return need_d, need_e, need_lc, need_lg


def chemical_pullback(density, grains, copotential, codrive):
    square_sum = jnp.sum(grains * grains, axis=0)
    grain_square = grains * grains
    drive_slope = 12.0 * grain_weight * (grain_square - grains)
    bulk_slope = 2.0 * bulk_weight * (1.0 - 6.0 * density + 6.0 * density * density) + 2.0 * grain_weight
    if codrive is None:
        return copotential * bulk_slope, copotential * drive_slope
    pull_density = copotential * bulk_slope + jnp.sum(codrive * drive_slope, axis=0)
    coupling = jnp.sum(codrive * grains, axis=0)
    pull_grains = (
        copotential * drive_slope
        + 12.0 * grain_weight * codrive * ((1.0 - density) - 2.0 * grains * (2.0 - density) + square_sum)
        + 24.0 * grain_weight * grains * coupling
    )
    return pull_density, pull_grains


def shards(density, labels, observed, measured):
    height_rows, azim_rows, radius_rows = density.shape
    total_hgt = height_rows * lax.axis_size("hgt")
    part = radius_rows // lax.axis_size("hgt")
    geometry = (
        lax.axis_index("rad") * radius_rows + lax.axis_index("hgt") * part,
        total_hgt,
        azim_rows * lax.axis_size("azim"),
        radius_rows * lax.axis_size("rad"),
        part,
    )
    need_d, need_e, need_lc, need_lg = reach()
    widths = (need_d[0], need_e[0], need_lc[STEPS], need_lc[STEPS])
    trim = lambda f, w: f[..., HALO - w : f.shape[-1] - (HALO - w)]
    inputs = [density, labels.astype(jnp.float32), observed, measured.astype(jnp.float32)]
    if lax.axis_size("hgt") == 2:
        extended = azim_exchange(inputs, widths)
        stacked = jnp.concatenate(extended, axis=-2)[None]
        received = edge_columns(stacked, HALO)
        stacked = two_core_window(gather_axis(stacked, "hgt", 1), received, HALO)[0]
        fields, at = [], 0
        for f, w in zip(extended, widths):
            rows = f.shape[-2]
            fields.append(trim(stacked[..., at : at + rows, :], w))
            at += rows
        density, grain_label, observed, measured = fields
    else:
        packed = chip_window(gather_axis(jnp.stack(inputs), "hgt", 1), HALO)
        density, grain_label, observed, measured = [
            trim(f, w) for f, w in zip(azim_exchange(list(packed), widths), widths)
        ]
    grains = (
        grain_label[None] == jnp.arange(GRAINS, dtype=jnp.float32)[:, None, None, None]
    ).astype(jnp.float32)
    need_d, need_e, need_lc, need_lg = reach()
    density = in_domain(density, need_d[0], geometry)
    grains = in_domain(grains, need_e[0], geometry)
    history = []
    for moment in range(STEPS):
        d_width, e_width = need_d[moment], need_e[moment]
        history.append((density, d_width, grains, e_width))
        pot_width = need_d[moment + 1] + 1
        next_e = need_e[moment + 1]
        both = max(pot_width, next_e)
        bulk_drive, grain_drive = chemical(crop(density, d_width, both), crop(grains, e_width, both))
        potential = crop(bulk_drive, both, pot_width) - cahn_gradient * laplace(
            crop(density, d_width, pot_width + 1), pot_width + 1, geometry, False
        )
        flux_term = laplace(potential, pot_width, geometry, False)
        new_density = crop(density, d_width, need_d[moment + 1]) + cahn_step * flux_term
        if next_e >= 0:
            grain_spread = laplace(crop(grains, e_width, next_e + 1), next_e + 1, geometry, False)
            new_grains = crop(grains, e_width, next_e) - allen_step * (
                crop(grain_drive, both, next_e) - allen_gradient * grain_spread
            )
            grains = in_domain(new_grains, next_e, geometry)
        density = in_domain(new_density, need_d[moment + 1], geometry)
    d_width = need_d[STEPS]

    observed = crop(observed, widths[2], d_width)
    measured = crop(measured, widths[3], d_width)
    costate = in_domain(measured * (density - observed), d_width, geometry)
    c_width = d_width
    last_density = crop(density, d_width, 0)
    cograins, cg_width = None, None
    for moment in range(STEPS - 1, -1, -1):
        fields_density, fd_width, fields_grains, fg_width = history[moment]
        point = need_lc[moment]
        nu_width = point + 1
        copotential = cahn_step * laplace(crop(costate, c_width, nu_width + 1), nu_width + 1, geometry, True)
        here_density = crop(fields_density, fd_width, point)
        here_grains = crop(fields_grains, fg_width, point)
        here_copotential = crop(copotential, nu_width, point)
        if cograins is None:
            pull_density, pull_grains = chemical_pullback(
                here_density, here_grains, here_copotential, None
            )
        else:
            pull_density, pull_grains = chemical_pullback(
                here_density, here_grains, here_copotential, -allen_step * crop(cograins, cg_width, point)
            )
        reaction = laplace(in_domain(copotential, nu_width, geometry), nu_width, geometry, True)
        new_costate = crop(costate, c_width, point) + pull_density - cahn_gradient * reaction
        new_cg_width = need_lg[moment]
        if cograins is None:
            new_cograins = crop(pull_grains, point, new_cg_width)
        else:
            grain_spread = laplace(
                crop(cograins, cg_width, new_cg_width + 1), new_cg_width + 1, geometry, True
            )
            new_cograins = (
                crop(cograins, cg_width, new_cg_width)
                + crop(pull_grains, point, new_cg_width)
                + allen_step * allen_gradient * grain_spread
            )
        costate, c_width = in_domain(new_costate, point, geometry), point
        cograins, cg_width = in_domain(new_cograins, new_cg_width, geometry), new_cg_width

    costate = crop(costate, c_width, 0)
    cograins = crop(cograins, cg_width, 0)
    result = scatter_heights(
        jnp.concatenate([last_density[None], costate[None], cograins], axis=0), height_rows
    )
    return (result[0], result[1], result[2:])


def solution(mesh):
    in_specs = (
        P("hgt", "azim", "rad"),
        P("hgt", "azim", "rad"),
        P("hgt", "azim", "rad"),
        P("hgt", "azim", "rad"),
    )
    out_specs = (P("hgt", "azim", "rad"), P("hgt", "azim", "rad"), P(None, "hgt", "azim", "rad"))
    return jax.shard_map(shards, mesh=mesh, in_specs=in_specs, out_specs=out_specs, check_vma=False)
```

```python
import jax
import jax.numpy as jnp
from jax import lax
from jax.sharding import PartitionSpec as P

STEPS = 3
GRAINS = 4


bulk_weight = 16.0
grain_weight = 1.0
cahn_step = 0.005
allen_step = 0.05
cahn_gradient = 1.0
allen_gradient = 1.0
full_turn = 6.283185307179586

HALO = 4 * STEPS


def halo_exchange(block, axis, dim, width, cyclic):
    peers, length = (lax.axis_size(axis), block.shape[dim])
    up = [(i, (i + 1) % peers) for i in range(peers) if cyclic or i + 1 < peers]
    down = [(j, i) for i, j in up]
    last = lax.slice_in_dim(block, length - width, length, axis=dim)
    leading = lax.slice_in_dim(block, 0, width, axis=dim)
    before = lax.ppermute(last, axis, up)
    after = lax.ppermute(leading, axis, down)
    return jnp.concatenate([before, block, after], axis=dim)


def azim_exchange(fields, widths):
    peers = lax.axis_size("azim")
    up = [(i, (i + 1) % peers) for i in range(peers)]
    down = [(j, i) for i, j in up]
    rows = fields[0].shape[-2]
    last = jnp.concatenate([f[..., rows - w :, :] for f, w in zip(fields, widths)], axis=-2)
    leading = jnp.concatenate([f[..., :w, :] for f, w in zip(fields, widths)], axis=-2)
    before = lax.ppermute(last, "azim", up)
    after = lax.ppermute(leading, "azim", down)
    out, at = [], 0
    for f, w in zip(fields, widths):
        out.append(jnp.concatenate([before[..., at : at + w, :], f, after[..., at : at + w, :]], axis=-2))
        at += w
    return out


def gather_axis(block, axis, dim):
    peers = lax.axis_size(axis)
    if peers == 1:
        return block
    own = lax.axis_index(axis)
    parts = [block]
    for shift in range(1, peers):
        parts.append(lax.ppermute(block, axis, [(i, (i + shift) % peers) for i in range(peers)]))
    if peers == 2:
        return jnp.where(
            own == 0,
            jnp.concatenate([parts[0], parts[1]], axis=dim),
            jnp.concatenate([parts[1], parts[0]], axis=dim),
        )
    stacked = jnp.stack(parts)
    order = (own - jnp.arange(peers, dtype=jnp.int32)) % peers
    ordered = jnp.take(stacked, order, axis=0)
    ordered = jnp.moveaxis(ordered, 0, dim)
    shape = list(block.shape)
    shape[dim] = shape[dim] * peers
    return ordered.reshape(shape)


def chip_window(block, width):
    peers, own, rad_peers = (lax.axis_size("hgt"), lax.axis_index("hgt"), lax.axis_size("rad"))
    cols = block.shape[-1]
    part = cols // peers
    piece = jnp.where(own == 0, block[..., :width], block[..., cols - width :])
    pairs = []
    for r in range(rad_peers - 1):
        pairs.append((r * peers + peers - 1, (r + 1) * peers))
        pairs.append(((r + 1) * peers, r * peers + peers - 1))
    received = lax.ppermute(piece, ("rad", "hgt"), pairs)
    padded = jnp.concatenate([received, block, received], axis=-1)
    return lax.dynamic_slice_in_dim(padded, own * part, part + 2 * width, axis=padded.ndim - 1)


def edge_columns(block, width):
    own, rad_peers = (lax.axis_index("hgt"), lax.axis_size("rad"))
    cols = block.shape[-1]
    first, last = (block[..., :width], block[..., cols - width :])
    cross, same = ([], [])
    for r in range(rad_peers - 1):
        cross += [(2 * r + 1, 2 * r + 2), (2 * r + 2, 2 * r + 1)]
        same += [(2 * r, 2 * r + 2), (2 * r + 3, 2 * r + 1)]
    from_cross = lax.ppermute(jnp.where(own == 0, first, last), ("rad", "hgt"), cross)
    from_same = lax.ppermute(jnp.where(own == 0, last, first), ("rad", "hgt"), same)
    return jnp.where(
        own == 0,
        jnp.concatenate([from_same, from_cross], axis=1),
        jnp.concatenate([from_cross, from_same], axis=1),
    )


def two_core_window(block, received, width):
    own = lax.axis_index("hgt")
    part = block.shape[-1] // 2
    padded = jnp.concatenate([received, block, received], axis=-1)
    return lax.dynamic_slice_in_dim(padded, own * part, part + 2 * width, axis=padded.ndim - 1)


def two_core_join(block, received, width):
    own = lax.axis_index("hgt")
    cols = block.shape[-1]
    part = cols // 2
    span = part + width
    piece = jnp.where(own == 0, block[..., cols - span :], block[..., :span])
    partner = lax.ppermute(piece, "hgt", [(0, 1), (1, 0)])
    halves = block.shape[1]
    low, high = received[:, :halves], received[:, halves:]
    first = jnp.concatenate(
        [
            jnp.concatenate([low, block[..., :span]], axis=-1),
            jnp.concatenate([high, partner], axis=-1),
        ],
        axis=1,
    )
    second = jnp.concatenate(
        [
            jnp.concatenate([partner, low], axis=-1),
            jnp.concatenate([block[..., cols - span :], high], axis=-1),
        ],
        axis=1,
    )
    return jnp.where(own == 0, first, second)


def scatter_heights(x, height_rows):
    peers, own = (lax.axis_size("hgt"), lax.axis_index("hgt"))
    parts = []
    for shift in range(peers):
        dest = (own + shift) % peers
        piece = lax.dynamic_slice_in_dim(x, dest * height_rows, height_rows, axis=1)
        if shift:
            piece = lax.ppermute(piece, "hgt", [(i, (i + shift) % peers) for i in range(peers)])
        parts.append(piece)
    if peers == 2:
        return jnp.where(
            own == 0,
            jnp.concatenate([parts[0], parts[1]], axis=-1),
            jnp.concatenate([parts[1], parts[0]], axis=-1),
        )
    stacked = jnp.stack(parts)
    order = (own - jnp.arange(peers, dtype=jnp.int32)) % peers
    ordered = jnp.moveaxis(jnp.take(stacked, order, axis=0), 0, -2)
    shape = ordered.shape
    return ordered.reshape(shape[:-2] + (shape[-2] * shape[-1],))


def crop(x, width, new_width):
    cut = width - new_width
    if cut == 0:
        return x
    return x[..., cut : x.shape[-2] - cut, cut : x.shape[-1] - cut]


def radial_mask(width, geometry):
    rad_start, total_hgt, total_azim, total_rad, cols = geometry
    rad_index = rad_start - width + jnp.arange(cols + 2 * width, dtype=jnp.int32)
    return (rad_index >= 0) & (rad_index < total_rad)


def in_domain(x, width, geometry):
    return jnp.where(radial_mask(width, geometry), x, 0.0)


def laplace(x, width, geometry, transpose):
    rad_start, total_hgt, total_azim, total_rad, cols = geometry
    margin = width - 1
    height_rows = x.shape[-3]
    radius_rows = x.shape[-1] - 2
    rad_index_all = rad_start - margin - 1 + jnp.arange(radius_rows + 2, dtype=jnp.int32)
    radius_all = total_azim / full_turn + rad_index_all.astype(jnp.float32) + 0.5
    rad_index = rad_index_all[1:-1]
    radius = radius_all[1:-1]
    outer_face = (radius + 0.5) * (rad_index < total_rad - 1).astype(jnp.float32)
    inner_face = (radius - 0.5) * (rad_index > 0).astype(jnp.float32)
    if transpose:
        outward_weight = outer_face / radius_all[2:]
        inward_weight = inner_face / radius_all[:-2]
    else:
        outward_weight = outer_face / radius
        inward_weight = inner_face / radius
    arc_length = radius * (full_turn / total_azim)
    arc_weight = 1.0 / (arc_length * arc_length)
    hgt_index = jnp.arange(height_rows, dtype=jnp.int32)
    faces = (hgt_index < total_hgt - 1).astype(jnp.float32) + (hgt_index > 0).astype(jnp.float32)
    center_weight = (outer_face + inner_face) / radius + 2.0 * arc_weight + faces[:, None, None]
    leading = x.ndim - 3
    padded = jnp.pad(x, [(0, 0)] * leading + [(1, 1), (0, 0), (0, 0)])
    center = padded[..., 1:-1, 1:-1, 1:-1]
    radial = outward_weight * padded[..., 1:-1, 1:-1, 2:] + inward_weight * padded[..., 1:-1, 1:-1, :-2]
    azimuthal = arc_weight * (padded[..., 1:-1, 2:, 1:-1] + padded[..., 1:-1, :-2, 1:-1])
    vertical = padded[..., 2:, 1:-1, 1:-1] + padded[..., :-2, 1:-1, 1:-1]
    return radial + azimuthal + vertical - center_weight * center


def chemical(density, grains):
    square_sum = jnp.sum(grains * grains, axis=0)
    cube_sum = jnp.sum(grains * grains * grains, axis=0)
    bulk_drive = 2.0 * bulk_weight * density * (1.0 - density) * (
        1.0 - 2.0 * density
    ) + grain_weight * (2.0 * density - 6.0 * square_sum + 4.0 * cube_sum)
    grain_drive = (
        12.0
        * grain_weight
        * (grains * (1.0 - density) - grains * grains * (2.0 - density) + grains * square_sum)
    )
    return (bulk_drive, grain_drive)


def reach():
    need_lc, need_lg = [0], [0]
    for moment in range(STEPS):
        need_lc.append(need_lc[-1] + 2)
        need_lg.append(max(need_lg[-1] + 1, need_lc[moment]))
    need_d, need_e = [need_lc[STEPS]], [-1]
    for moment in range(STEPS - 1, -1, -1):
        pot_width = need_d[0] + 1
        need_d.insert(0, max(pot_width + 1, need_e[0], need_lc[moment]))
        need_e.insert(0, max(pot_width, need_e[0] + 1, need_lc[moment]))
    return need_d, need_e, need_lc, need_lg


def chemical_pullback(density, grains, copotential, codrive):
    square_sum = jnp.sum(grains * grains, axis=0)
    grain_square = grains * grains
    drive_slope = 12.0 * grain_weight * (grain_square - grains)
    bulk_slope = 2.0 * bulk_weight * (1.0 - 6.0 * density + 6.0 * density * density) + 2.0 * grain_weight
    if codrive is None:
        return copotential * bulk_slope, copotential * drive_slope
    pull_density = copotential * bulk_slope + jnp.sum(codrive * drive_slope, axis=0)
    coupling = jnp.sum(codrive * grains, axis=0)
    pull_grains = (
        copotential * drive_slope
        + 12.0 * grain_weight * codrive * ((1.0 - density) - 2.0 * grains * (2.0 - density) + square_sum)
        + 24.0 * grain_weight * grains * coupling
    )
    return pull_density, pull_grains


def shards(density, labels, observed, measured):
    height_rows, azim_rows, radius_rows = density.shape
    total_hgt = height_rows * lax.axis_size("hgt")
    part = radius_rows // lax.axis_size("hgt")
    geometry = (
        lax.axis_index("rad") * radius_rows + lax.axis_index("hgt") * part,
        total_hgt,
        azim_rows * lax.axis_size("azim"),
        radius_rows * lax.axis_size("rad"),
        part,
    )
    need_d, need_e, need_lc, need_lg = reach()
    widths = (need_d[0], need_e[0], need_lc[STEPS], need_lc[STEPS])
    trim = lambda f, w: f[..., HALO - w : f.shape[-1] - (HALO - w)]
    inputs = [density, labels.astype(jnp.float32), observed, measured.astype(jnp.float32)]
    if lax.axis_size("hgt") == 2:
        extended = azim_exchange(inputs, widths)
        stacked = jnp.concatenate(extended, axis=-2)[None]
        received = edge_columns(stacked, HALO)
        stacked = two_core_join(stacked, received, HALO)[0]
        fields, at = [], 0
        for f, w in zip(extended, widths):
            rows = f.shape[-2]
            fields.append(trim(stacked[..., at : at + rows, :], w))
            at += rows
        density, grain_label, observed, measured = fields
    else:
        packed = chip_window(gather_axis(jnp.stack(inputs), "hgt", 1), HALO)
        density, grain_label, observed, measured = [
            trim(f, w) for f, w in zip(azim_exchange(list(packed), widths), widths)
        ]
    grains = (
        grain_label[None] == jnp.arange(GRAINS, dtype=jnp.float32)[:, None, None, None]
    ).astype(jnp.float32)
    need_d, need_e, need_lc, need_lg = reach()
    density = in_domain(density, need_d[0], geometry)
    grains = in_domain(grains, need_e[0], geometry)
    history = []
    for moment in range(STEPS):
        d_width, e_width = need_d[moment], need_e[moment]
        history.append((density, d_width, grains, e_width))
        pot_width = need_d[moment + 1] + 1
        next_e = need_e[moment + 1]
        both = max(pot_width, next_e)
        bulk_drive, grain_drive = chemical(crop(density, d_width, both), crop(grains, e_width, both))
        potential = crop(bulk_drive, both, pot_width) - cahn_gradient * laplace(
            crop(density, d_width, pot_width + 1), pot_width + 1, geometry, False
        )
        flux_term = laplace(potential, pot_width, geometry, False)
        new_density = crop(density, d_width, need_d[moment + 1]) + cahn_step * flux_term
        if next_e >= 0:
            grain_spread = laplace(crop(grains, e_width, next_e + 1), next_e + 1, geometry, False)
            new_grains = crop(grains, e_width, next_e) - allen_step * (
                crop(grain_drive, both, next_e) - allen_gradient * grain_spread
            )
            grains = in_domain(new_grains, next_e, geometry)
        density = in_domain(new_density, need_d[moment + 1], geometry)
    d_width = need_d[STEPS]

    observed = crop(observed, widths[2], d_width)
    measured = crop(measured, widths[3], d_width)
    costate = in_domain(measured * (density - observed), d_width, geometry)
    c_width = d_width
    last_density = crop(density, d_width, 0)
    cograins, cg_width = None, None
    for moment in range(STEPS - 1, -1, -1):
        fields_density, fd_width, fields_grains, fg_width = history[moment]
        point = need_lc[moment]
        nu_width = point + 1
        copotential = cahn_step * laplace(crop(costate, c_width, nu_width + 1), nu_width + 1, geometry, True)
        here_density = crop(fields_density, fd_width, point)
        here_grains = crop(fields_grains, fg_width, point)
        here_copotential = crop(copotential, nu_width, point)
        if cograins is None:
            pull_density, pull_grains = chemical_pullback(
                here_density, here_grains, here_copotential, None
            )
        else:
            pull_density, pull_grains = chemical_pullback(
                here_density, here_grains, here_copotential, -allen_step * crop(cograins, cg_width, point)
            )
        reaction = laplace(in_domain(copotential, nu_width, geometry), nu_width, geometry, True)
        new_costate = crop(costate, c_width, point) + pull_density - cahn_gradient * reaction
        new_cg_width = need_lg[moment]
        if cograins is None:
            new_cograins = crop(pull_grains, point, new_cg_width)
        else:
            grain_spread = laplace(
                crop(cograins, cg_width, new_cg_width + 1), new_cg_width + 1, geometry, True
            )
            new_cograins = (
                crop(cograins, cg_width, new_cg_width)
                + crop(pull_grains, point, new_cg_width)
                + allen_step * allen_gradient * grain_spread
            )
        costate, c_width = in_domain(new_costate, point, geometry), point
        cograins, cg_width = in_domain(new_cograins, new_cg_width, geometry), new_cg_width

    costate = crop(costate, c_width, 0)
    cograins = crop(cograins, cg_width, 0)
    result = scatter_heights(
        jnp.concatenate([last_density[None], costate[None], cograins], axis=0), height_rows
    )
    return (result[0], result[1], result[2:])


def solution(mesh):
    in_specs = (
        P("hgt", "azim", "rad"),
        P("hgt", "azim", "rad"),
        P("hgt", "azim", "rad"),
        P("hgt", "azim", "rad"),
    )
    out_specs = (P("hgt", "azim", "rad"), P("hgt", "azim", "rad"), P(None, "hgt", "azim", "rad"))
    return jax.shard_map(shards, mesh=mesh, in_specs=in_specs, out_specs=out_specs, check_vma=False)
```

```python
import jax
import jax.numpy as jnp
from jax import lax
from jax.sharding import PartitionSpec as P

STEPS = 3
GRAINS = 4


bulk_weight = 16.0
grain_weight = 1.0
cahn_step = 0.005
allen_step = 0.05
cahn_gradient = 1.0
allen_gradient = 1.0
full_turn = 6.283185307179586

HALO = 4 * STEPS


def halo_exchange(block, axis, dim, width, cyclic):
    peers, length = (lax.axis_size(axis), block.shape[dim])
    up = [(i, (i + 1) % peers) for i in range(peers) if cyclic or i + 1 < peers]
    down = [(j, i) for i, j in up]
    last = lax.slice_in_dim(block, length - width, length, axis=dim)
    leading = lax.slice_in_dim(block, 0, width, axis=dim)
    before = lax.ppermute(last, axis, up)
    after = lax.ppermute(leading, axis, down)
    return jnp.concatenate([before, block, after], axis=dim)


def azim_exchange(fields, widths):
    peers = lax.axis_size("azim")
    up = [(i, (i + 1) % peers) for i in range(peers)]
    down = [(j, i) for i, j in up]
    rows = fields[0].shape[-2]
    last = jnp.concatenate([f[..., rows - w :, :] for f, w in zip(fields, widths)], axis=-2)
    leading = jnp.concatenate([f[..., :w, :] for f, w in zip(fields, widths)], axis=-2)
    before = lax.ppermute(last, "azim", up)
    after = lax.ppermute(leading, "azim", down)
    out, at = [], 0
    for f, w in zip(fields, widths):
        out.append(jnp.concatenate([before[..., at : at + w, :], f, after[..., at : at + w, :]], axis=-2))
        at += w
    return out


def gather_axis(block, axis, dim):
    peers = lax.axis_size(axis)
    if peers == 1:
        return block
    own = lax.axis_index(axis)
    parts = [block]
    for shift in range(1, peers):
        parts.append(lax.ppermute(block, axis, [(i, (i + shift) % peers) for i in range(peers)]))
    if peers == 2:
        return jnp.where(
            own == 0,
            jnp.concatenate([parts[0], parts[1]], axis=dim),
            jnp.concatenate([parts[1], parts[0]], axis=dim),
        )
    stacked = jnp.stack(parts)
    order = (own - jnp.arange(peers, dtype=jnp.int32)) % peers
    ordered = jnp.take(stacked, order, axis=0)
    ordered = jnp.moveaxis(ordered, 0, dim)
    shape = list(block.shape)
    shape[dim] = shape[dim] * peers
    return ordered.reshape(shape)


def chip_window(block, width):
    peers, own, rad_peers = (lax.axis_size("hgt"), lax.axis_index("hgt"), lax.axis_size("rad"))
    cols = block.shape[-1]
    part = cols // peers
    piece = jnp.where(own == 0, block[..., :width], block[..., cols - width :])
    pairs = []
    for r in range(rad_peers - 1):
        pairs.append((r * peers + peers - 1, (r + 1) * peers))
        pairs.append(((r + 1) * peers, r * peers + peers - 1))
    received = lax.ppermute(piece, ("rad", "hgt"), pairs)
    padded = jnp.concatenate([received, block, received], axis=-1)
    return lax.dynamic_slice_in_dim(padded, own * part, part + 2 * width, axis=padded.ndim - 1)


def edge_columns(block, width):
    own, rad_peers = (lax.axis_index("hgt"), lax.axis_size("rad"))
    cols = block.shape[-1]
    first, last = (block[..., :width], block[..., cols - width :])
    cross, same = ([], [])
    for r in range(rad_peers - 1):
        cross += [(2 * r + 1, 2 * r + 2), (2 * r + 2, 2 * r + 1)]
        same += [(2 * r, 2 * r + 2), (2 * r + 3, 2 * r + 1)]
    from_cross = lax.ppermute(jnp.where(own == 0, first, last), ("rad", "hgt"), cross)
    from_same = lax.ppermute(jnp.where(own == 0, last, first), ("rad", "hgt"), same)
    return jnp.where(
        own == 0,
        jnp.concatenate([from_same, from_cross], axis=1),
        jnp.concatenate([from_cross, from_same], axis=1),
    )


def two_core_window(block, received, width):
    own = lax.axis_index("hgt")
    part = block.shape[-1] // 2
    padded = jnp.concatenate([received, block, received], axis=-1)
    return lax.dynamic_slice_in_dim(padded, own * part, part + 2 * width, axis=padded.ndim - 1)


def two_core_join(block, received, width):
    own = lax.axis_index("hgt")
    cols = block.shape[-1]
    part = cols // 2
    span = part + width
    piece = jnp.where(own == 0, block[..., cols - span :], block[..., :span])
    partner = lax.ppermute(piece, "hgt", [(0, 1), (1, 0)])
    halves = block.shape[1]
    low, high = received[:, :halves], received[:, halves:]
    first = jnp.concatenate(
        [
            jnp.concatenate([low, block[..., :span]], axis=-1),
            jnp.concatenate([high, partner], axis=-1),
        ],
        axis=1,
    )
    second = jnp.concatenate(
        [
            jnp.concatenate([partner, low], axis=-1),
            jnp.concatenate([block[..., cols - span :], high], axis=-1),
        ],
        axis=1,
    )
    return jnp.where(own == 0, first, second)


def scatter_heights(x, height_rows):
    peers, own = (lax.axis_size("hgt"), lax.axis_index("hgt"))
    parts = []
    for shift in range(peers):
        dest = (own + shift) % peers
        piece = lax.dynamic_slice_in_dim(x, dest * height_rows, height_rows, axis=1)
        if shift:
            piece = lax.ppermute(piece, "hgt", [(i, (i + shift) % peers) for i in range(peers)])
        parts.append(piece)
    if peers == 2:
        return jnp.where(
            own == 0,
            jnp.concatenate([parts[0], parts[1]], axis=-1),
            jnp.concatenate([parts[1], parts[0]], axis=-1),
        )
    stacked = jnp.stack(parts)
    order = (own - jnp.arange(peers, dtype=jnp.int32)) % peers
    ordered = jnp.moveaxis(jnp.take(stacked, order, axis=0), 0, -2)
    shape = ordered.shape
    return ordered.reshape(shape[:-2] + (shape[-2] * shape[-1],))


def crop(x, width, new_width):
    cut = width - new_width
    if cut == 0:
        return x
    return x[..., cut : x.shape[-2] - cut, cut : x.shape[-1] - cut]


def radial_mask(width, geometry):
    rad_start, total_hgt, total_azim, total_rad, cols = geometry
    rad_index = rad_start - width + jnp.arange(cols + 2 * width, dtype=jnp.int32)
    return (rad_index >= 0) & (rad_index < total_rad)


def in_domain(x, width, geometry):
    if width <= 0:
        return x
    return jnp.where(radial_mask(width, geometry), x, 0.0)


def laplace(x, width, geometry, transpose):
    rad_start, total_hgt, total_azim, total_rad, cols = geometry
    margin = width - 1
    height_rows = x.shape[-3]
    radius_rows = x.shape[-1] - 2
    rad_index_all = rad_start - margin - 1 + jnp.arange(radius_rows + 2, dtype=jnp.int32)
    radius_all = total_azim / full_turn + rad_index_all.astype(jnp.float32) + 0.5
    rad_index = rad_index_all[1:-1]
    radius = radius_all[1:-1]
    outer_face = (radius + 0.5) * (rad_index < total_rad - 1).astype(jnp.float32)
    inner_face = (radius - 0.5) * (rad_index > 0).astype(jnp.float32)
    if transpose:
        outward_weight = outer_face / radius_all[2:]
        inward_weight = inner_face / radius_all[:-2]
    else:
        outward_weight = outer_face / radius
        inward_weight = inner_face / radius
    arc_length = radius * (full_turn / total_azim)
    arc_weight = 1.0 / (arc_length * arc_length)
    hgt_index = jnp.arange(height_rows, dtype=jnp.int32)
    faces = (hgt_index < total_hgt - 1).astype(jnp.float32) + (hgt_index > 0).astype(jnp.float32)
    center_weight = (outer_face + inner_face) / radius + 2.0 * arc_weight + faces[:, None, None]
    leading = x.ndim - 3
    padded = jnp.pad(x, [(0, 0)] * leading + [(1, 1), (0, 0), (0, 0)])
    center = padded[..., 1:-1, 1:-1, 1:-1]
    radial = outward_weight * padded[..., 1:-1, 1:-1, 2:] + inward_weight * padded[..., 1:-1, 1:-1, :-2]
    azimuthal = arc_weight * (padded[..., 1:-1, 2:, 1:-1] + padded[..., 1:-1, :-2, 1:-1])
    vertical = padded[..., 2:, 1:-1, 1:-1] + padded[..., :-2, 1:-1, 1:-1]
    return radial + azimuthal + vertical - center_weight * center


def chemical(density, grains):
    square_sum = jnp.sum(grains * grains, axis=0)
    cube_sum = jnp.sum(grains * grains * grains, axis=0)
    bulk_drive = 2.0 * bulk_weight * density * (1.0 - density) * (
        1.0 - 2.0 * density
    ) + grain_weight * (2.0 * density - 6.0 * square_sum + 4.0 * cube_sum)
    grain_drive = (
        12.0
        * grain_weight
        * (grains * (1.0 - density) - grains * grains * (2.0 - density) + grains * square_sum)
    )
    return (bulk_drive, grain_drive)


def reach():
    need_lc, need_lg = [0], [0]
    for moment in range(STEPS):
        need_lc.append(need_lc[-1] + 2)
        need_lg.append(max(need_lg[-1] + 1, need_lc[moment]))
    need_d, need_e = [need_lc[STEPS]], [-1]
    for moment in range(STEPS - 1, -1, -1):
        pot_width = need_d[0] + 1
        need_d.insert(0, max(pot_width + 1, need_e[0], need_lc[moment]))
        need_e.insert(0, max(pot_width, need_e[0] + 1, need_lc[moment]))
    return need_d, need_e, need_lc, need_lg


def chemical_pullback(density, grains, copotential, codrive):
    square_sum = jnp.sum(grains * grains, axis=0)
    grain_square = grains * grains
    drive_slope = 12.0 * grain_weight * (grain_square - grains)
    bulk_slope = 2.0 * bulk_weight * (1.0 - 6.0 * density + 6.0 * density * density) + 2.0 * grain_weight
    if codrive is None:
        return copotential * bulk_slope, copotential * drive_slope
    pull_density = copotential * bulk_slope + jnp.sum(codrive * drive_slope, axis=0)
    coupling = jnp.sum(codrive * grains, axis=0)
    pull_grains = (
        copotential * drive_slope
        + 12.0 * grain_weight * codrive * ((1.0 - density) - 2.0 * grains * (2.0 - density) + square_sum)
        + 24.0 * grain_weight * grains * coupling
    )
    return pull_density, pull_grains


def shards(density, labels, observed, measured):
    height_rows, azim_rows, radius_rows = density.shape
    total_hgt = height_rows * lax.axis_size("hgt")
    part = radius_rows // lax.axis_size("hgt")
    geometry = (
        lax.axis_index("rad") * radius_rows + lax.axis_index("hgt") * part,
        total_hgt,
        azim_rows * lax.axis_size("azim"),
        radius_rows * lax.axis_size("rad"),
        part,
    )
    need_d, need_e, need_lc, need_lg = reach()
    widths = (need_d[0], need_e[0], need_lc[STEPS], need_lc[STEPS])
    trim = lambda f, w: f[..., HALO - w : f.shape[-1] - (HALO - w)]
    inputs = [density, labels.astype(jnp.float32), observed, measured.astype(jnp.float32)]
    if lax.axis_size("hgt") == 2:
        extended = azim_exchange(inputs, widths)
        stacked = jnp.concatenate(extended, axis=-2)[None]
        received = edge_columns(stacked, HALO)
        stacked = two_core_join(stacked, received, HALO)[0]
        fields, at = [], 0
        for f, w in zip(extended, widths):
            rows = f.shape[-2]
            fields.append(trim(stacked[..., at : at + rows, :], w))
            at += rows
        density, grain_label, observed, measured = fields
    else:
        packed = chip_window(gather_axis(jnp.stack(inputs), "hgt", 1), HALO)
        density, grain_label, observed, measured = [
            trim(f, w) for f, w in zip(azim_exchange(list(packed), widths), widths)
        ]
    grains = (
        grain_label[None] == jnp.arange(GRAINS, dtype=jnp.float32)[:, None, None, None]
    ).astype(jnp.float32)
    need_d, need_e, need_lc, need_lg = reach()
    density = in_domain(density, need_d[0], geometry)
    grains = in_domain(grains, need_e[0], geometry)
    history = []
    for moment in range(STEPS):
        d_width, e_width = need_d[moment], need_e[moment]
        history.append((density, d_width, grains, e_width))
        pot_width = need_d[moment + 1] + 1
        next_e = need_e[moment + 1]
        both = max(pot_width, next_e)
        bulk_drive, grain_drive = chemical(crop(density, d_width, both), crop(grains, e_width, both))
        potential = crop(bulk_drive, both, pot_width) - cahn_gradient * laplace(
            crop(density, d_width, pot_width + 1), pot_width + 1, geometry, False
        )
        flux_term = laplace(potential, pot_width, geometry, False)
        new_density = crop(density, d_width, need_d[moment + 1]) + cahn_step * flux_term
        if next_e >= 0:
            grain_spread = laplace(crop(grains, e_width, next_e + 1), next_e + 1, geometry, False)
            new_grains = crop(grains, e_width, next_e) - allen_step * (
                crop(grain_drive, both, next_e) - allen_gradient * grain_spread
            )
            grains = in_domain(new_grains, next_e, geometry)
        density = in_domain(new_density, need_d[moment + 1], geometry)
    d_width = need_d[STEPS]

    observed = crop(observed, widths[2], d_width)
    measured = crop(measured, widths[3], d_width)
    costate = in_domain(measured * (density - observed), d_width, geometry)
    c_width = d_width
    last_density = crop(density, d_width, 0)
    cograins, cg_width = None, None
    for moment in range(STEPS - 1, -1, -1):
        fields_density, fd_width, fields_grains, fg_width = history[moment]
        point = need_lc[moment]
        nu_width = point + 1
        copotential = cahn_step * laplace(crop(costate, c_width, nu_width + 1), nu_width + 1, geometry, True)
        here_density = crop(fields_density, fd_width, point)
        here_grains = crop(fields_grains, fg_width, point)
        here_copotential = crop(copotential, nu_width, point)
        if cograins is None:
            pull_density, pull_grains = chemical_pullback(
                here_density, here_grains, here_copotential, None
            )
        else:
            pull_density, pull_grains = chemical_pullback(
                here_density, here_grains, here_copotential, -allen_step * crop(cograins, cg_width, point)
            )
        reaction = laplace(in_domain(copotential, nu_width, geometry), nu_width, geometry, True)
        new_costate = crop(costate, c_width, point) + pull_density - cahn_gradient * reaction
        new_cg_width = need_lg[moment]
        if cograins is None:
            new_cograins = crop(pull_grains, point, new_cg_width)
        else:
            grain_spread = laplace(
                crop(cograins, cg_width, new_cg_width + 1), new_cg_width + 1, geometry, True
            )
            new_cograins = (
                crop(cograins, cg_width, new_cg_width)
                + crop(pull_grains, point, new_cg_width)
                + allen_step * allen_gradient * grain_spread
            )
        costate, c_width = in_domain(new_costate, point, geometry), point
        cograins, cg_width = in_domain(new_cograins, new_cg_width, geometry), new_cg_width

    costate = crop(costate, c_width, 0)
    cograins = crop(cograins, cg_width, 0)
    result = scatter_heights(
        jnp.concatenate([last_density[None], costate[None], cograins], axis=0), height_rows
    )
    return (result[0], result[1], result[2:])


def solution(mesh):
    in_specs = (
        P("hgt", "azim", "rad"),
        P("hgt", "azim", "rad"),
        P("hgt", "azim", "rad"),
        P("hgt", "azim", "rad"),
    )
    out_specs = (P("hgt", "azim", "rad"), P("hgt", "azim", "rad"), P(None, "hgt", "azim", "rad"))
    return jax.shard_map(shards, mesh=mesh, in_specs=in_specs, out_specs=out_specs, check_vma=False)
```
